256 devices in a mesh: ctx: 32 (over z, x), head: 8 (over y, core).
Axes of the slice: x: 4, y: 4, z: 8, core: 2. Of those that a mesh axis runs over, the one named last changes fastest.
Arguments:
- query_matrix: bfloat16 [32768, 4096], P(('ctx', 'head')), may hold values from -5 to 5
- key_matrix: bfloat16 [32768, 1024], P(('ctx', 'head')), may hold values from -5 to 5
- value_matrix: bfloat16 [32768, 1024], P(('ctx', 'head')), may hold values from -12 to 12
- output_gradient: bfloat16 [32768, 4096], P('ctx', 'head'), may hold values from -12 to 12
- doc_start: int32 [128], replicated, may hold values from 0 to 1, as said below
Outputs:
- attended: bfloat16 [32768, 4096], P('ctx', 'head')
- grad_q: bfloat16 [32768, 4096], P('ctx', 'head')
- grad_k: bfloat16 [32768, 1024], P('ctx', 'head')
- grad_v: bfloat16 [32768, 1024], P('ctx', 'head')
The draws below stay inside these ranges and needn't reach their ends.
Inputs may be any that keep to these rules, and one draw needn't show every extreme that they name: `doc_start`: entry 0 is 1; a document starts at each unit whose entry is 1 and lasts to the next start or the end; every document has 1 to 4 units, and some document has exactly 1024 tokens.
All inputs are finite; a program needn't handle non-finite values.
Results may differ from the reference program's by a relative error of at most 0.019.
Values may be sent and summed in bfloat16 or wider, within the bound.
No kernel may reach another device: no remote copies, remote signals or barrier semaphores. Data moves between devices by JAX's collectives and lax.ppermute only.
A program may use at most 64 MiB of HBM per device.

```python
import jax
import jax.numpy as jnp
from jax import lax

QUERY_HEADS = 32
KEY_VALUE_HEADS = 8
HEAD_SIZE = 128
PACKED_TOKENS = 32768
DOC_MIN = 256
DOC_MAX = 1024
UNITS = 128


def draw_query_matrix(key, part):
    value_array = jnp.clip(1.2 * jax.random.normal(jax.random.fold_in(key, 11), (PACKED_TOKENS, QUERY_HEADS * HEAD_SIZE)), -4.8, 4.8)
    return value_array.astype(jnp.bfloat16)


def draw_key_matrix(key, part):
    value_array = jnp.clip(1.2 * jax.random.normal(jax.random.fold_in(key, 21), (PACKED_TOKENS, KEY_VALUE_HEADS * HEAD_SIZE)), -4.8, 4.8)
    return value_array.astype(jnp.bfloat16)


def draw_doc_start(key, part):
    longest = DOC_MAX // DOC_MIN
    first_key = jax.random.fold_in(key, 31)
    lengths = jax.random.randint(first_key, (UNITS,), 1, longest + 1)
    starts = jnp.cumsum(lengths) - lengths
    unit_index = jnp.arange(UNITS)
    marked = jnp.any(starts[None, :] == unit_index[:, None], axis=1)
    anchor = UNITS // 2 - longest // 2
    inside = (unit_index >= anchor) & (unit_index < anchor + 2 * longest)
    forced = (unit_index == anchor) | (unit_index == anchor + longest) | (unit_index == anchor + 2 * longest)
    marked = jnp.where(inside, forced, marked | forced)
    return marked.astype(jnp.int32)


def block_scale(own_key, dims, split, least, high):
    def one(axis_at, blocks):
        heights = jax.random.uniform(jax.random.fold_in(jax.random.fold_in(own_key, 6), axis_at), (blocks,), jnp.float32, least / len(split), high / len(split))
        return jnp.repeat(jnp.exp(heights), dims[axis_at] // blocks).reshape((-1,) + (1,) * (len(dims) - axis_at - 1))

    level = one(*split[0])
    for cut in split[1:]:
        level = level * one(*cut)
    return level


def noise(rng, shape, width, bound, pieces=(), held_as=jnp.bfloat16):
    loudness = block_scale(rng, shape, pieces, -0.22, 0.18) if pieces else 1.0
    array = jax.random.normal(rng, shape, jnp.float32) * width * loudness
    return jnp.minimum(jnp.maximum(array, -bound), bound).astype(held_as)


def setup_inputs(seed: int = 0) -> dict:
    splits = jax.random.split(jax.random.key(seed), 6)
    return {
        "query_matrix": draw_query_matrix(jax.random.fold_in(splits[5], 71), 0),
        "key_matrix": draw_key_matrix(jax.random.fold_in(splits[5], 71), 0),
        "value_matrix": noise(splits[2], (PACKED_TOKENS, KEY_VALUE_HEADS * HEAD_SIZE), 2.0, 12.0, ((0, 256),)),
        "output_gradient": noise(splits[3], (PACKED_TOKENS, QUERY_HEADS * HEAD_SIZE), 2.0, 12.0, ((0, 32), (1, 8))),
        "doc_start": draw_doc_start(jax.random.fold_in(splits[5], 71), 0),
    }


def tile_grads(query_tile, grad_tile, key_rows, value_rows, query_doc, key_doc, query_pos, key_pos):
    score_scale = query_tile.shape[-1] ** -0.5
    scores = jnp.einsum("tgrd,ngd->grtn", query_tile.astype(jnp.float32), key_rows.astype(jnp.float32)) * score_scale
    visible = (key_doc[None, :] == query_doc[:, None]) & (key_pos[None, :] <= query_pos[:, None])
    scores = jnp.where(visible, scores, -jnp.inf)
    row_top = jnp.max(scores, axis=-1, keepdims=True)
    log_total = row_top + jnp.log(jnp.sum(jnp.exp(scores - row_top), axis=-1, keepdims=True))
    weights = jnp.exp(scores - log_total)
    weights_low = weights.astype(jnp.bfloat16)
    attended = jnp.einsum("grtn,ngd->tgrd", weights_low.astype(jnp.float32), value_rows.astype(jnp.float32)).astype(jnp.bfloat16)
    row_delta = jnp.sum(grad_tile.astype(jnp.float32) * attended.astype(jnp.float32), axis=-1)
    row_delta = jnp.transpose(row_delta, (1, 2, 0))[..., None]
    grad_weights = jnp.einsum("tgrd,ngd->grtn", grad_tile.astype(jnp.float32), value_rows.astype(jnp.float32))
    grad_scores = (weights * (grad_weights - row_delta)).astype(jnp.bfloat16)
    grad_query = (jnp.einsum("grtn,ngd->tgrd", grad_scores.astype(jnp.float32), key_rows.astype(jnp.float32)) * score_scale).astype(jnp.bfloat16)
    grad_key = jnp.einsum("grtn,tgrd->ngd", grad_scores.astype(jnp.float32), query_tile.astype(jnp.float32)) * score_scale
    grad_value = jnp.einsum("grtn,tgrd->ngd", weights_low.astype(jnp.float32), grad_tile.astype(jnp.float32))
    return attended, grad_query, grad_key, grad_value


def reference(query_matrix, key_matrix, value_matrix, output_gradient, doc_start):
    sequence_rows = query_matrix.shape[0]
    rows_per_block = DOC_MAX
    count_of_blocks = sequence_rows // rows_per_block
    heads_per_group = QUERY_HEADS // KEY_VALUE_HEADS
    unit_doc = jnp.cumsum(doc_start).astype(jnp.int32)
    token_doc = jnp.repeat(unit_doc, DOC_MIN, total_repeat_length=sequence_rows).reshape(count_of_blocks, rows_per_block)
    query_array = query_matrix.reshape(count_of_blocks, rows_per_block, KEY_VALUE_HEADS, heads_per_group, HEAD_SIZE)
    gradient_per_head = output_gradient.reshape(count_of_blocks, rows_per_block, KEY_VALUE_HEADS, heads_per_group, HEAD_SIZE)
    heads_of_keys = key_matrix.reshape(count_of_blocks, rows_per_block, KEY_VALUE_HEADS, HEAD_SIZE)
    heads_of_values = value_matrix.reshape(count_of_blocks, rows_per_block, KEY_VALUE_HEADS, HEAD_SIZE)
    blank_row_count = jnp.zeros((1, rows_per_block, KEY_VALUE_HEADS, HEAD_SIZE), jnp.bfloat16)
    lead_keys = jnp.concatenate([blank_row_count, heads_of_keys[:-1]], axis=0)
    lead_values = jnp.concatenate([blank_row_count, heads_of_values[:-1]], axis=0)
    lead_doc = jnp.concatenate([jnp.full((1, rows_per_block), -1, jnp.int32), token_doc[:-1]], axis=0)
    key_pos = jnp.arange(2 * rows_per_block, dtype=jnp.int32) - rows_per_block
    query_pos = jnp.arange(rows_per_block, dtype=jnp.int32)

    def one_block(items):
        query_block, grad_block, prev_keys, prev_values, cur_keys, cur_values, prev_doc, cur_doc = items
        return tile_grads(query_block, grad_block,
                          jnp.concatenate([prev_keys, cur_keys], axis=0),
                          jnp.concatenate([prev_values, cur_values], axis=0),
                          cur_doc, jnp.concatenate([prev_doc, cur_doc], axis=0),
                          query_pos, key_pos)

    attended, grad_query, grad_key, grad_value = lax.map(
        one_block, (query_array, gradient_per_head, lead_keys, lead_values, heads_of_keys, heads_of_values, lead_doc, token_doc))
    trailing_rows = jnp.zeros((1, rows_per_block, KEY_VALUE_HEADS, HEAD_SIZE), jnp.float32)
    summed_keys = grad_key[:, rows_per_block:] + jnp.concatenate([grad_key[1:, :rows_per_block], trailing_rows], axis=0)
    summed_values = grad_value[:, rows_per_block:] + jnp.concatenate([grad_value[1:, :rows_per_block], trailing_rows], axis=0)
    return (attended.reshape(sequence_rows, QUERY_HEADS * HEAD_SIZE),
            grad_query.reshape(sequence_rows, QUERY_HEADS * HEAD_SIZE),
            summed_keys.astype(jnp.bfloat16).reshape(sequence_rows, KEY_VALUE_HEADS * HEAD_SIZE),
            summed_values.astype(jnp.bfloat16).reshape(sequence_rows, KEY_VALUE_HEADS * HEAD_SIZE))
```

```python
import jax
import jax.numpy as jnp
from jax import lax
from jax.sharding import PartitionSpec as P

QUERY_HEADS = 32
KEY_VALUE_HEADS = 8
HEAD_SIZE = 128


def from_behind(block, axis, distance):
    devices = range(lax.axis_size(axis))
    route = [(i - distance, i) for i in devices if i - distance in devices]
    return lax.ppermute(block, axis, route)


def tile_grads(query_tile, grad_tile, key_rows, value_rows, query_doc, key_doc, query_pos, key_pos):
    score_scale = query_tile.shape[-1] ** (-0.5)
    scores = (
        jnp.einsum("tgrd,ngd->grtn", query_tile, key_rows, preferred_element_type=jnp.float32)
        * score_scale
    )
    visible = (key_doc[None, :] == query_doc[:, None]) & (key_pos[None, :] <= query_pos[:, None])
    scores = jnp.where(visible, scores, -jnp.inf)
    row_top = jnp.max(scores, axis=-1, keepdims=True)
    log_total = row_top + jnp.log(jnp.sum(jnp.exp(scores - row_top), axis=-1, keepdims=True))
    weights = jnp.exp(scores - log_total)
    weights_low = weights.astype(jnp.bfloat16)
    attended = jnp.einsum(
        "grtn,ngd->tgrd", weights_low, value_rows, preferred_element_type=jnp.float32
    ).astype(jnp.bfloat16)
    row_delta = jnp.sum(grad_tile.astype(jnp.float32) * attended.astype(jnp.float32), axis=-1)
    row_delta = jnp.transpose(row_delta, (1, 2, 0))[..., None]
    grad_weights = jnp.einsum(
        "tgrd,ngd->grtn", grad_tile, value_rows, preferred_element_type=jnp.float32
    )
    grad_scores = (weights * (grad_weights - row_delta)).astype(jnp.bfloat16)
    grad_query = (
        jnp.einsum("grtn,ngd->tgrd", grad_scores, key_rows, preferred_element_type=jnp.float32)
        * score_scale
    ).astype(jnp.bfloat16)
    grad_key = (
        jnp.einsum("grtn,tgrd->ngd", grad_scores, query_tile, preferred_element_type=jnp.float32)
        * score_scale
    )
    grad_value = jnp.einsum(
        "grtn,tgrd->ngd", weights_low, grad_tile, preferred_element_type=jnp.float32
    )
    return (attended, grad_query, grad_key, grad_value)


def local(query_matrix, key_matrix, value_matrix, output_gradient, doc_start):
    token_per_shard = query_matrix.shape[0]
    head_groups = lax.axis_size("head")
    q_cols = query_matrix.shape[1] // head_groups
    k_cols = key_matrix.shape[1] // head_groups
    packed = jnp.concatenate(
        [
            query_matrix.reshape(token_per_shard, head_groups, q_cols),
            key_matrix.reshape(token_per_shard, head_groups, k_cols),
            value_matrix.reshape(token_per_shard, head_groups, k_cols),
        ],
        axis=2,
    )
    packed = lax.all_to_all(packed, "head", split_axis=1, concat_axis=0, tiled=True)
    ctx_rows = packed.shape[0]
    packed = packed.reshape(ctx_rows, q_cols + 2 * k_cols)
    kv_local = k_cols // HEAD_SIZE
    heads_per_group = q_cols // k_cols
    query_array = packed[:, :q_cols].reshape(ctx_rows, kv_local, heads_per_group, HEAD_SIZE)
    own_kv = packed[:, q_cols:]
    own_keys = own_kv[:, :k_cols].reshape(ctx_rows, kv_local, HEAD_SIZE)
    own_values = own_kv[:, k_cols:].reshape(ctx_rows, kv_local, HEAD_SIZE)
    unit_rows = 2 * token_per_shard
    earlier_kv = from_behind(own_kv, "ctx", 1)
    earlier_keys = earlier_kv[:, :k_cols].reshape(ctx_rows, kv_local, HEAD_SIZE)
    earlier_values = earlier_kv[:, k_cols:].reshape(ctx_rows, kv_local, HEAD_SIZE)
    gradient_per_head = output_gradient.reshape(ctx_rows, kv_local, heads_per_group, HEAD_SIZE)
    per_shard = ctx_rows // unit_rows
    ctx_index = lax.axis_index("ctx")
    unit_doc = jnp.cumsum(doc_start)
    own_units = lax.dynamic_slice_in_dim(unit_doc, ctx_index * per_shard, per_shard)
    prior_units = lax.dynamic_slice_in_dim(
        unit_doc, jnp.maximum(ctx_index - 1, 0) * per_shard, per_shard
    )
    prior_units = jnp.where(ctx_index > 0, prior_units, -1)
    own_doc = jnp.repeat(own_units, unit_rows, total_repeat_length=ctx_rows)
    prior_doc = jnp.repeat(prior_units, unit_rows, total_repeat_length=ctx_rows)
    joined_keys = jnp.concatenate([earlier_keys, own_keys], axis=0)
    joined_values = jnp.concatenate([earlier_values, own_values], axis=0)
    joined_doc = jnp.concatenate([prior_doc, own_doc], axis=0)
    joined_pos = jnp.arange(ctx_rows + ctx_rows, dtype=jnp.int32) - ctx_rows
    before = ctx_rows - unit_rows
    key_grad = jnp.zeros((ctx_rows + ctx_rows, kv_local, HEAD_SIZE), jnp.float32)
    value_grad = jnp.zeros((ctx_rows + ctx_rows, kv_local, HEAD_SIZE), jnp.float32)
    pieces = []
    query_grads = []
    for unit_number in range(per_shard):
        first_row = unit_number * unit_rows
        end_row = first_row + unit_rows
        window_start = ctx_rows - before + first_row
        window_end = window_start + ctx_rows
        query_tile = query_array[first_row:end_row]
        grad_tile = gradient_per_head[first_row:end_row]
        query_doc = own_doc[first_row:end_row]
        query_pos = jnp.arange(first_row, end_row, dtype=jnp.int32)
        results = tile_grads(
            query_tile,
            grad_tile,
            joined_keys[window_start:window_end],
            joined_values[window_start:window_end],
            query_doc,
            joined_doc[window_start:window_end],
            query_pos,
            joined_pos[window_start:window_end],
        )
        attended, grad_query, grad_key, grad_value = results
        pieces.append(attended)
        query_grads.append(grad_query)
        key_grad = key_grad.at[window_start:window_end].add(grad_key)
        value_grad = value_grad.at[window_start:window_end].add(grad_value)
    prior_grads = jnp.concatenate(
        [
            key_grad[:ctx_rows].astype(jnp.bfloat16).reshape(ctx_rows, k_cols),
            value_grad[:ctx_rows].astype(jnp.bfloat16).reshape(ctx_rows, k_cols),
        ],
        axis=1,
    )
    later = from_behind(prior_grads, "ctx", -1).astype(jnp.float32)
    key_own = key_grad[ctx_rows:].reshape(ctx_rows, k_cols) + later[:, :k_cols]
    value_own = value_grad[ctx_rows:].reshape(ctx_rows, k_cols) + later[:, k_cols:]
    summed_keys = key_own.astype(jnp.bfloat16)
    summed_values = value_own.astype(jnp.bfloat16)
    attended_all = jnp.concatenate(pieces, axis=0).reshape(
        ctx_rows, kv_local * heads_per_group * HEAD_SIZE
    )
    query_total = jnp.concatenate(query_grads, axis=0).reshape(
        ctx_rows, kv_local * heads_per_group * HEAD_SIZE
    )
    return (attended_all, query_total, summed_keys, summed_values)


def solution(mesh):
    placed = (
        P(("ctx", "head"), None),
        P(("ctx", "head"), None),
        P(("ctx", "head"), None),
        P("ctx", "head"),
        P(),
    )
    return jax.shard_map(
        local,
        mesh=mesh,
        in_specs=placed,
        out_specs=(P("ctx", "head"), P("ctx", "head"), P("ctx", "head"), P("ctx", "head")),
        check_vma=False,
    )
```

```python
import jax
import jax.numpy as jnp
from jax import lax
from jax.sharding import PartitionSpec as P
import functools
from jax.experimental import pallas as pl
from jax.experimental.pallas import tpu as pltpu

QUERY_HEADS = 32
KEY_VALUE_HEADS = 8
HEAD_SIZE = 128
BLOCK = 256
INTERPRET = False


def from_behind(block, axis, distance):
    devices = range(lax.axis_size(axis))
    route = [(i - distance, i) for i in devices if i - distance in devices]
    return lax.ppermute(block, axis, route)


def _nt(a, b):
    return lax.dot_general(a, b, (((1,), (1,)), ((), ())), preferred_element_type=jnp.float32)


def _tn(a, b):
    return lax.dot_general(a, b, (((0,), (0,)), ((), ())), preferred_element_type=jnp.float32)


def _nn(a, b):
    return lax.dot_general(a, b, (((1,), (0,)), ((), ())), preferred_element_type=jnp.float32)


def attention_kernel(lo_ref, packed_ref, earlier_ref, grad_ref,
                     att_ref, dq_ref, prior_ref, own_ref,
                     s_scr, att_scr, dq_scr, *, units, heads, q_cols):
    scale = HEAD_SIZE ** (-0.5)
    prior_ref[...] = jnp.zeros(prior_ref.shape, prior_ref.dtype)
    own_ref[...] = jnp.zeros(own_ref.shape, own_ref.dtype)
    rows = heads * BLOCK
    causal = (lax.broadcasted_iota(jnp.int32, (rows, BLOCK), 0) % BLOCK
              >= lax.broadcasted_iota(jnp.int32, (rows, BLOCK), 1))

    def load_kv(ref, col0, blk):
        start = pl.multiple_of(blk * BLOCK, BLOCK)
        return (ref[pl.ds(start, BLOCK), col0:col0 + HEAD_SIZE],
                ref[pl.ds(start, BLOCK), col0 + HEAD_SIZE:col0 + 2 * HEAD_SIZE])

    for u in range(units):
        r0 = u * BLOCK
        qs = jnp.concatenate(
            [packed_ref[r0:r0 + BLOCK, h * HEAD_SIZE:(h + 1) * HEAD_SIZE] for h in range(heads)], axis=0)
        dos = jnp.concatenate(
            [grad_ref[r0:r0 + BLOCK, h * HEAD_SIZE:(h + 1) * HEAD_SIZE] for h in range(heads)], axis=0)
        lo = lo_ref[u]
        diag = units + u
        first_own = jnp.maximum(lo, units)
        segments = ((earlier_ref, 0, prior_ref, lo, units, 0),
                    (packed_ref, q_cols, own_ref, first_own, diag, units))

        def pass1(b, carry, ref, col0, off):
            m, l = carry
            k, _ = load_kv(ref, col0, b - off)
            s = _nt(qs, k) * scale
            s_scr[b - (u + 1)] = s
            m_new = jnp.maximum(m, jnp.max(s, axis=1, keepdims=True))
            l = l * jnp.exp(m - m_new) + jnp.sum(jnp.exp(s - m_new), axis=1, keepdims=True)
            return m_new, l

        carry = (jnp.full((rows, 1), -jnp.inf, jnp.float32), jnp.zeros((rows, 1), jnp.float32))
        for ref, col0, _, start, stop, off in segments:
            carry = lax.fori_loop(start, stop, functools.partial(pass1, ref=ref, col0=col0, off=off), carry)
        m, l = carry
        k_d, v_d = load_kv(packed_ref, q_cols, u)
        s = jnp.where(causal, _nt(qs, k_d) * scale, -jnp.inf)
        s_scr[units - 1] = s
        m_new = jnp.maximum(m, jnp.max(s, axis=1, keepdims=True))
        l = l * jnp.exp(m - m_new) + jnp.sum(jnp.exp(s - m_new), axis=1, keepdims=True)
        lse = m_new + jnp.log(l)

        def pass2(b, _, ref, col0, off):
            _, v = load_kv(ref, col0, b - off)
            p = jnp.exp(s_scr[b - (u + 1)] - lse)
            s_scr[b - (u + 1)] = p
            att_scr[...] += _nn(p.astype(jnp.bfloat16), v)
            return 0

        p = jnp.exp(s - lse)
        s_scr[units - 1] = p
        att_scr[...] = _nn(p.astype(jnp.bfloat16), v_d)
        for ref, col0, _, start, stop, off in segments:
            lax.fori_loop(start, stop, functools.partial(pass2, ref=ref, col0=col0, off=off), 0)
        att = att_scr[...].astype(jnp.bfloat16)
        delta = jnp.sum(dos.astype(jnp.float32) * att.astype(jnp.float32), axis=1, keepdims=True)

        def pass3(b, _, ref, col0, gref, off):
            k, v = load_kv(ref, col0, b - off)
            p = s_scr[b - (u + 1)]
            ds = (p * (_nt(dos, v) - delta)).astype(jnp.bfloat16)
            dq_scr[...] += _nn(ds, k)
            start = pl.multiple_of((b - off) * BLOCK, BLOCK)
            gref[pl.ds(start, BLOCK), 0:HEAD_SIZE] += _tn(ds, qs)
            gref[pl.ds(start, BLOCK), HEAD_SIZE:2 * HEAD_SIZE] += _tn(p.astype(jnp.bfloat16), dos)
            return 0

        ds = (p * (_nt(dos, v_d) - delta)).astype(jnp.bfloat16)
        dq_scr[...] = _nn(ds, k_d)
        own_ref[r0:r0 + BLOCK, 0:HEAD_SIZE] += _tn(ds, qs)
        own_ref[r0:r0 + BLOCK, HEAD_SIZE:2 * HEAD_SIZE] += _tn(p.astype(jnp.bfloat16), dos)
        for ref, col0, gref, start, stop, off in segments:
            lax.fori_loop(start, stop, functools.partial(pass3, ref=ref, col0=col0, gref=gref, off=off), 0)
        dq = (dq_scr[...] * scale).astype(jnp.bfloat16)
        for h in range(heads):
            att_ref[r0:r0 + BLOCK, h * HEAD_SIZE:(h + 1) * HEAD_SIZE] = att[h * BLOCK:(h + 1) * BLOCK]
            dq_ref[r0:r0 + BLOCK, h * HEAD_SIZE:(h + 1) * HEAD_SIZE] = dq[h * BLOCK:(h + 1) * BLOCK]


def attention_call(lo, packed, earlier, grad, *, heads, interpret=False):
    ctx_rows = packed.shape[0]
    units = ctx_rows // BLOCK
    q_cols = heads * HEAD_SIZE
    kv_cols = 2 * HEAD_SIZE
    vmem = pltpu.MemorySpace.VMEM
    kernel = functools.partial(attention_kernel, units=units, heads=heads, q_cols=q_cols)
    rows = heads * BLOCK
    visible_blocks = units * (units + 1) // 2 + units
    flops = 12 * rows * BLOCK * HEAD_SIZE * visible_blocks
    return pl.pallas_call(
        kernel,
        out_shape=(
            jax.ShapeDtypeStruct((ctx_rows, q_cols), jnp.bfloat16),
            jax.ShapeDtypeStruct((ctx_rows, q_cols), jnp.bfloat16),
            jax.ShapeDtypeStruct((ctx_rows, kv_cols), jnp.float32),
            jax.ShapeDtypeStruct((ctx_rows, kv_cols), jnp.float32),
        ),
        in_specs=[pl.BlockSpec(memory_space=pltpu.SMEM)] + [pl.BlockSpec(memory_space=vmem)] * 3,
        out_specs=tuple(pl.BlockSpec(memory_space=vmem) for _ in range(4)),
        scratch_shapes=[
            pltpu.VMEM((units, rows, BLOCK), jnp.float32),
            pltpu.VMEM((rows, HEAD_SIZE), jnp.float32),
            pltpu.VMEM((rows, HEAD_SIZE), jnp.float32),
        ],
        compiler_params=pltpu.CompilerParams(vmem_limit_bytes=48 * 1024 * 1024),
        cost_estimate=pl.CostEstimate(flops=flops, transcendentals=2 * rows * BLOCK * visible_blocks,
                                      bytes_accessed=8 * 1024 * 1024),
        interpret=interpret,
    )(lo, packed, earlier, grad)


def local(query_matrix, key_matrix, value_matrix, output_gradient, doc_start):
    token_per_shard = query_matrix.shape[0]
    head_groups = lax.axis_size("head")
    q_cols = query_matrix.shape[1] // head_groups
    k_cols = key_matrix.shape[1] // head_groups
    assert k_cols == HEAD_SIZE and 2 * token_per_shard == BLOCK
    packed = jnp.concatenate(
        [
            query_matrix.reshape(token_per_shard, head_groups, q_cols),
            key_matrix.reshape(token_per_shard, head_groups, k_cols),
            value_matrix.reshape(token_per_shard, head_groups, k_cols),
        ],
        axis=2,
    )
    packed = lax.all_to_all(packed, "head", split_axis=1, concat_axis=0, tiled=True)
    ctx_rows = packed.shape[0]
    packed = packed.reshape(ctx_rows, q_cols + 2 * k_cols)
    earlier_kv = from_behind(packed[:, q_cols:], "ctx", 1)
    units = ctx_rows // BLOCK
    ctx_index = lax.axis_index("ctx")
    unit_doc = jnp.cumsum(doc_start)
    own_units = lax.dynamic_slice_in_dim(unit_doc, ctx_index * units, units)
    prior_units = lax.dynamic_slice_in_dim(unit_doc, jnp.maximum(ctx_index - 1, 0) * units, units)
    prior_units = jnp.where(ctx_index > 0, prior_units, -1)
    joined_units = jnp.concatenate([prior_units, own_units])
    unit_ids = jnp.arange(units, dtype=jnp.int32)
    window = unit_ids[:, None] + 1 + unit_ids[None, :]
    same = (joined_units[window] == own_units[:, None]).astype(jnp.int32)
    lo = (unit_ids + units + 1 - jnp.sum(same, axis=1)).astype(jnp.int32)
    attended_all, query_total, prior_grads, own_grads = attention_call(
        lo, packed, earlier_kv, output_gradient, heads=q_cols // HEAD_SIZE, interpret=INTERPRET
    )
    score_scale = HEAD_SIZE ** (-0.5)
    prior_grads = jnp.concatenate(
        [(prior_grads[:, :k_cols] * score_scale).astype(jnp.bfloat16),
         prior_grads[:, k_cols:].astype(jnp.bfloat16)],
        axis=1,
    )
    later = from_behind(prior_grads, "ctx", -1).astype(jnp.float32)
    summed_keys = (own_grads[:, :k_cols] * score_scale + later[:, :k_cols]).astype(jnp.bfloat16)
    summed_values = (own_grads[:, k_cols:] + later[:, k_cols:]).astype(jnp.bfloat16)
    return (attended_all, query_total, summed_keys, summed_values)


def solution(mesh):
    placed = (
        P(("ctx", "head"), None),
        P(("ctx", "head"), None),
        P(("ctx", "head"), None),
        P("ctx", "head"),
        P(),
    )
    return jax.shard_map(
        local,
        mesh=mesh,
        in_specs=placed,
        out_specs=(P("ctx", "head"), P("ctx", "head"), P("ctx", "head"), P("ctx", "head")),
        check_vma=False,
    )
```

```python
import jax
import jax.numpy as jnp
from jax import lax
from jax.sharding import PartitionSpec as P
import functools
from jax.experimental import pallas as pl
from jax.experimental.pallas import tpu as pltpu

QUERY_HEADS = 32
KEY_VALUE_HEADS = 8
HEAD_SIZE = 128
BLOCK = 256
INTERPRET = False


def from_behind(block, axis, distance):
    devices = range(lax.axis_size(axis))
    route = [(i - distance, i) for i in devices if i - distance in devices]
    return lax.ppermute(block, axis, route)


def _nt(a, b):
    return lax.dot_general(a, b, (((1,), (1,)), ((), ())), preferred_element_type=jnp.float32)


def _tn(a, b):
    return lax.dot_general(a, b, (((0,), (0,)), ((), ())), preferred_element_type=jnp.float32)


def _nn(a, b):
    return lax.dot_general(a, b, (((1,), (0,)), ((), ())), preferred_element_type=jnp.float32)


def attention_kernel(lo_ref, packed_ref, kv_ref, earlier_ref, grad_ref,
                     att_ref, dq_ref, prior_ref, own_ref,
                     s_scr, att_scr, dq_scr, *, units, heads, q_cols):
    scale = HEAD_SIZE ** (-0.5)
    prior_ref[...] = jnp.zeros(prior_ref.shape, prior_ref.dtype)
    own_ref[...] = jnp.zeros(own_ref.shape, own_ref.dtype)
    rows = heads * BLOCK
    causal = (lax.broadcasted_iota(jnp.int32, (rows, BLOCK), 0) % BLOCK
              >= lax.broadcasted_iota(jnp.int32, (rows, BLOCK), 1))

    def load_kv(ref, col0, blk):
        start = pl.multiple_of(blk * BLOCK, BLOCK)
        return (ref[pl.ds(start, BLOCK), col0:col0 + HEAD_SIZE],
                ref[pl.ds(start, BLOCK), col0 + HEAD_SIZE:col0 + 2 * HEAD_SIZE])

    for u in range(units):
        r0 = u * BLOCK
        qs = jnp.concatenate(
            [packed_ref[r0:r0 + BLOCK, h * HEAD_SIZE:(h + 1) * HEAD_SIZE] for h in range(heads)], axis=0)
        dos = jnp.concatenate(
            [grad_ref[r0:r0 + BLOCK, h * HEAD_SIZE:(h + 1) * HEAD_SIZE] for h in range(heads)], axis=0)
        lo = lo_ref[u]
        diag = units + u
        first_own = jnp.maximum(lo, units)
        segments = ((earlier_ref, 0, prior_ref, lo, units, 1),
                    (kv_ref, 0, own_ref, first_own, diag, units))

        def pass1(b, carry, ref, col0, off):
            m, l = carry
            k, _ = load_kv(ref, col0, b - off)
            s = _nt(qs, k) * scale
            s_scr[b - (u + 1)] = s
            m_new = jnp.maximum(m, jnp.max(s, axis=1, keepdims=True))
            l = l * jnp.exp(m - m_new) + jnp.sum(jnp.exp(s - m_new), axis=1, keepdims=True)
            return m_new, l

        carry = (jnp.full((rows, 1), -jnp.inf, jnp.float32), jnp.zeros((rows, 1), jnp.float32))
        for ref, col0, _, start, stop, off in segments:
            carry = lax.fori_loop(start, stop, functools.partial(pass1, ref=ref, col0=col0, off=off), carry)
        m, l = carry
        k_d, v_d = load_kv(kv_ref, 0, u)
        s = jnp.where(causal, _nt(qs, k_d) * scale, -jnp.inf)
        s_scr[units - 1] = s
        m_new = jnp.maximum(m, jnp.max(s, axis=1, keepdims=True))
        l = l * jnp.exp(m - m_new) + jnp.sum(jnp.exp(s - m_new), axis=1, keepdims=True)
        lse = m_new + jnp.log(l)

        def pass2(b, _, ref, col0, off):
            _, v = load_kv(ref, col0, b - off)
            p = jnp.exp(s_scr[b - (u + 1)] - lse)
            s_scr[b - (u + 1)] = p
            att_scr[...] += _nn(p.astype(jnp.bfloat16), v)
            return 0

        p = jnp.exp(s - lse)
        s_scr[units - 1] = p
        att_scr[...] = _nn(p.astype(jnp.bfloat16), v_d)
        for ref, col0, _, start, stop, off in segments:
            lax.fori_loop(start, stop, functools.partial(pass2, ref=ref, col0=col0, off=off), 0)
        att = att_scr[...].astype(jnp.bfloat16)
        delta = jnp.sum(dos.astype(jnp.float32) * att.astype(jnp.float32), axis=1, keepdims=True)

        def pass3(b, _, ref, col0, gref, off):
            k, v = load_kv(ref, col0, b - off)
            p = s_scr[b - (u + 1)]
            ds = (p * (_nt(dos, v) - delta)).astype(jnp.bfloat16)
            dq_scr[...] += _nn(ds, k)
            start = pl.multiple_of((b - off) * BLOCK, BLOCK)
            gref[pl.ds(start, BLOCK), 0:HEAD_SIZE] += _tn(ds, qs)
            gref[pl.ds(start, BLOCK), HEAD_SIZE:2 * HEAD_SIZE] += _tn(p.astype(jnp.bfloat16), dos)
            return 0

        ds = (p * (_nt(dos, v_d) - delta)).astype(jnp.bfloat16)
        dq_scr[...] = _nn(ds, k_d)
        own_ref[r0:r0 + BLOCK, 0:HEAD_SIZE] += _tn(ds, qs)
        own_ref[r0:r0 + BLOCK, HEAD_SIZE:2 * HEAD_SIZE] += _tn(p.astype(jnp.bfloat16), dos)
        for ref, col0, gref, start, stop, off in segments:
            lax.fori_loop(start, stop, functools.partial(pass3, ref=ref, col0=col0, gref=gref, off=off), 0)
        dq = (dq_scr[...] * scale).astype(jnp.bfloat16)
        for h in range(heads):
            att_ref[r0:r0 + BLOCK, h * HEAD_SIZE:(h + 1) * HEAD_SIZE] = att[h * BLOCK:(h + 1) * BLOCK]
            dq_ref[r0:r0 + BLOCK, h * HEAD_SIZE:(h + 1) * HEAD_SIZE] = dq[h * BLOCK:(h + 1) * BLOCK]


def attention_call(lo, packed, kv, earlier, grad, *, heads, interpret=False):
    ctx_rows = packed.shape[0]
    units = ctx_rows // BLOCK
    q_cols = heads * HEAD_SIZE
    kv_cols = 2 * HEAD_SIZE
    vmem = pltpu.MemorySpace.VMEM
    kernel = functools.partial(attention_kernel, units=units, heads=heads, q_cols=q_cols)
    rows = heads * BLOCK
    visible_blocks = units * (units + 1) // 2 + units
    flops = 12 * rows * BLOCK * HEAD_SIZE * visible_blocks
    return pl.pallas_call(
        kernel,
        out_shape=(
            jax.ShapeDtypeStruct((ctx_rows, q_cols), jnp.bfloat16),
            jax.ShapeDtypeStruct((ctx_rows, q_cols), jnp.bfloat16),
            jax.ShapeDtypeStruct(earlier.shape, jnp.float32),
            jax.ShapeDtypeStruct((ctx_rows, kv_cols), jnp.float32),
        ),
        in_specs=[pl.BlockSpec(memory_space=pltpu.SMEM)] + [pl.BlockSpec(memory_space=vmem)] * 4,
        out_specs=tuple(pl.BlockSpec(memory_space=vmem) for _ in range(4)),
        scratch_shapes=[
            pltpu.VMEM((units, rows, BLOCK), jnp.float32),
            pltpu.VMEM((rows, HEAD_SIZE), jnp.float32),
            pltpu.VMEM((rows, HEAD_SIZE), jnp.float32),
        ],
        compiler_params=pltpu.CompilerParams(vmem_limit_bytes=48 * 1024 * 1024),
        cost_estimate=pl.CostEstimate(flops=flops, transcendentals=2 * rows * BLOCK * visible_blocks,
                                      bytes_accessed=8 * 1024 * 1024),
        interpret=interpret,
    )(lo, packed, kv, earlier, grad)


def local(query_matrix, key_matrix, value_matrix, output_gradient, doc_start):
    token_per_shard = query_matrix.shape[0]
    head_groups = lax.axis_size("head")
    q_cols = query_matrix.shape[1] // head_groups
    k_cols = key_matrix.shape[1] // head_groups
    assert k_cols == HEAD_SIZE and 2 * token_per_shard == BLOCK
    kv_packed = jnp.concatenate(
        [
            key_matrix.reshape(token_per_shard, head_groups, k_cols),
            value_matrix.reshape(token_per_shard, head_groups, k_cols),
        ],
        axis=2,
    )
    kv = lax.all_to_all(kv_packed, "head", split_axis=1, concat_axis=0, tiled=True)
    ctx_rows = kv.shape[0]
    kv = kv.reshape(ctx_rows, 2 * k_cols)
    earlier_kv = from_behind(kv[BLOCK:], "ctx", 1)
    packed = lax.all_to_all(
        query_matrix.reshape(token_per_shard, head_groups, q_cols),
        "head", split_axis=1, concat_axis=0, tiled=True,
    ).reshape(ctx_rows, q_cols)
    units = ctx_rows // BLOCK
    ctx_index = lax.axis_index("ctx")
    unit_doc = jnp.cumsum(doc_start)
    own_units = lax.dynamic_slice_in_dim(unit_doc, ctx_index * units, units)
    prior_units = lax.dynamic_slice_in_dim(unit_doc, jnp.maximum(ctx_index - 1, 0) * units, units)
    prior_units = jnp.where(ctx_index > 0, prior_units, -1)
    joined_units = jnp.concatenate([prior_units, own_units])
    unit_ids = jnp.arange(units, dtype=jnp.int32)
    window = unit_ids[:, None] + 1 + unit_ids[None, :]
    same = (joined_units[window] == own_units[:, None]).astype(jnp.int32)
    lo = (unit_ids + units + 1 - jnp.sum(same, axis=1)).astype(jnp.int32)
    attended_all, query_total, prior_grads, own_grads = attention_call(
        lo, packed, kv, earlier_kv, output_gradient, heads=q_cols // HEAD_SIZE, interpret=INTERPRET
    )
    score_scale = HEAD_SIZE ** (-0.5)
    prior_grads = jnp.concatenate(
        [(prior_grads[:, :k_cols] * score_scale).astype(jnp.bfloat16),
         prior_grads[:, k_cols:].astype(jnp.bfloat16)],
        axis=1,
    )
    later = from_behind(prior_grads, "ctx", -1).astype(jnp.float32)
    later = jnp.concatenate([jnp.zeros((BLOCK, 2 * k_cols), jnp.float32), later], axis=0)
    summed_keys = (own_grads[:, :k_cols] * score_scale + later[:, :k_cols]).astype(jnp.bfloat16)
    summed_values = (own_grads[:, k_cols:] + later[:, k_cols:]).astype(jnp.bfloat16)
    return (attended_all, query_total, summed_keys, summed_values)


def solution(mesh):
    placed = (
        P(("ctx", "head"), None),
        P(("ctx", "head"), None),
        P(("ctx", "head"), None),
        P("ctx", "head"),
        P(),
    )
    return jax.shard_map(
        local,
        mesh=mesh,
        in_specs=placed,
        out_specs=(P("ctx", "head"), P("ctx", "head"), P("ctx", "head"), P("ctx", "head")),
        check_vma=False,
    )
```

```python
import jax
import jax.numpy as jnp
from jax import lax
from jax.sharding import PartitionSpec as P
import functools
from jax.experimental import pallas as pl
from jax.experimental.pallas import tpu as pltpu

QUERY_HEADS = 32
KEY_VALUE_HEADS = 8
HEAD_SIZE = 128
BLOCK = 256
INTERPRET = False


def from_behind(block, axis, distance):
    devices = range(lax.axis_size(axis))
    route = [(i - distance, i) for i in devices if i - distance in devices]
    return lax.ppermute(block, axis, route)


def _nt(a, b):
    return lax.dot_general(a, b, (((1,), (1,)), ((), ())), preferred_element_type=jnp.float32)


def _tn(a, b):
    return lax.dot_general(a, b, (((0,), (0,)), ((), ())), preferred_element_type=jnp.float32)


def _nn(a, b):
    return lax.dot_general(a, b, (((1,), (0,)), ((), ())), preferred_element_type=jnp.float32)


def attention_kernel(*refs, unit_list, units, heads, with_prior, aliased):
    refs = list(refs)
    lo_ref, q_ref, kv_ref = refs[:3]
    refs = refs[3:]
    earlier_ref = refs.pop(0) if with_prior else None
    grad_ref = refs.pop(0)
    refs = refs[aliased:]
    att_ref, dq_ref = refs[:2]
    refs = refs[2:]
    prior_ref = refs.pop(0) if with_prior else None
    own_ref, s_scr, att_scr, dq_scr = refs
    scale = HEAD_SIZE ** (-0.5)
    if with_prior:
        prior_ref[...] = jnp.zeros(prior_ref.shape, prior_ref.dtype)
    own_ref[...] = jnp.zeros(own_ref.shape, own_ref.dtype)
    rows = heads * BLOCK
    causal = (lax.broadcasted_iota(jnp.int32, (rows, BLOCK), 0) % BLOCK
              >= lax.broadcasted_iota(jnp.int32, (rows, BLOCK), 1))

    def load_kv(ref, col0, blk):
        start = pl.multiple_of(blk * BLOCK, BLOCK)
        return (ref[pl.ds(start, BLOCK), col0:col0 + HEAD_SIZE],
                ref[pl.ds(start, BLOCK), col0 + HEAD_SIZE:col0 + 2 * HEAD_SIZE])

    for u in unit_list:
        r0 = u * BLOCK
        w0 = (u - unit_list[0]) * BLOCK
        qs = jnp.concatenate(
            [q_ref[r0:r0 + BLOCK, h * HEAD_SIZE:(h + 1) * HEAD_SIZE] for h in range(heads)], axis=0)
        dos = jnp.concatenate(
            [grad_ref[r0:r0 + BLOCK, h * HEAD_SIZE:(h + 1) * HEAD_SIZE] for h in range(heads)], axis=0)
        lo = lo_ref[u]
        diag = units + u
        first_own = jnp.maximum(lo, units)
        segments = ((kv_ref, 0, own_ref, first_own, diag, units),)
        if with_prior:
            segments = ((earlier_ref, 0, prior_ref, lo, units, 1),) + segments

        def pass1(b, carry, ref, col0, off):
            m, l = carry
            k, _ = load_kv(ref, col0, b - off)
            s = _nt(qs, k) * scale
            s_scr[b - (u + 1)] = s
            m_new = jnp.maximum(m, jnp.max(s, axis=1, keepdims=True))
            l = l * jnp.exp(m - m_new) + jnp.sum(jnp.exp(s - m_new), axis=1, keepdims=True)
            return m_new, l

        carry = (jnp.full((rows, 1), -jnp.inf, jnp.float32), jnp.zeros((rows, 1), jnp.float32))
        for ref, col0, _, start, stop, off in segments:
            carry = lax.fori_loop(start, stop, functools.partial(pass1, ref=ref, col0=col0, off=off), carry)
        m, l = carry
        k_d, v_d = load_kv(kv_ref, 0, u)
        s = jnp.where(causal, _nt(qs, k_d) * scale, -jnp.inf)
        m_new = jnp.maximum(m, jnp.max(s, axis=1, keepdims=True))
        l = l * jnp.exp(m - m_new) + jnp.sum(jnp.exp(s - m_new), axis=1, keepdims=True)
        lse = m_new + jnp.log(l)

        def pass2(b, _, ref, col0, off):
            _, v = load_kv(ref, col0, b - off)
            p = jnp.exp(s_scr[b - (u + 1)] - lse)
            s_scr[b - (u + 1)] = p
            att_scr[...] += _nn(p.astype(jnp.bfloat16), v)
            return 0

        p = jnp.exp(s - lse)
        att_scr[...] = _nn(p.astype(jnp.bfloat16), v_d)
        for ref, col0, _, start, stop, off in segments:
            lax.fori_loop(start, stop, functools.partial(pass2, ref=ref, col0=col0, off=off), 0)
        att = att_scr[...].astype(jnp.bfloat16)
        delta = jnp.sum(dos.astype(jnp.float32) * att.astype(jnp.float32), axis=1, keepdims=True)

        def pass3(b, _, ref, col0, gref, off):
            k, v = load_kv(ref, col0, b - off)
            p = s_scr[b - (u + 1)]
            ds = (p * (_nt(dos, v) - delta)).astype(jnp.bfloat16)
            dq_scr[...] += _nn(ds, k)
            start = pl.multiple_of((b - off) * BLOCK, BLOCK)
            gref[pl.ds(start, BLOCK), 0:HEAD_SIZE] += _tn(ds, qs)
            gref[pl.ds(start, BLOCK), HEAD_SIZE:2 * HEAD_SIZE] += _tn(p.astype(jnp.bfloat16), dos)
            return 0

        ds = (p * (_nt(dos, v_d) - delta)).astype(jnp.bfloat16)
        dq_scr[...] = _nn(ds, k_d)
        own_ref[r0:r0 + BLOCK, 0:HEAD_SIZE] += _tn(ds, qs)
        own_ref[r0:r0 + BLOCK, HEAD_SIZE:2 * HEAD_SIZE] += _tn(p.astype(jnp.bfloat16), dos)
        for ref, col0, gref, start, stop, off in segments:
            lax.fori_loop(start, stop, functools.partial(pass3, ref=ref, col0=col0, gref=gref, off=off), 0)
        dq = (dq_scr[...] * scale).astype(jnp.bfloat16)
        for h in range(heads):
            att_ref[w0:w0 + BLOCK, h * HEAD_SIZE:(h + 1) * HEAD_SIZE] = att[h * BLOCK:(h + 1) * BLOCK]
            dq_ref[w0:w0 + BLOCK, h * HEAD_SIZE:(h + 1) * HEAD_SIZE] = dq[h * BLOCK:(h + 1) * BLOCK]


def attention_call(lo, packed, kv, earlier, grad, unit_list, out_alias=None, *, heads, interpret=False):
    ctx_rows = packed.shape[0]
    units = ctx_rows // BLOCK
    q_cols = heads * HEAD_SIZE
    kv_cols = 2 * HEAD_SIZE
    with_prior = earlier is not None
    aliased = 0 if out_alias is None else 2
    kernel = functools.partial(attention_kernel, unit_list=tuple(unit_list), units=units, heads=heads,
                               with_prior=with_prior, aliased=aliased)
    rows = heads * BLOCK
    n_rows = len(unit_list) * BLOCK
    block_index = unit_list[0] // len(unit_list)
    assert block_index * len(unit_list) == unit_list[0]

    def whole(x):
        return pl.BlockSpec(x.shape, lambda i: (0,) * len(x.shape))

    operands = [lo, packed, kv] + ([earlier] if with_prior else []) + [grad]
    in_specs = [pl.BlockSpec(memory_space=pltpu.SMEM)] + [whole(x) for x in operands[1:]]
    if out_alias is not None:
        operands += list(out_alias)
        in_specs += [pl.BlockSpec(memory_space=pl.ANY)] * 2
    out_shape = [jax.ShapeDtypeStruct((ctx_rows, q_cols), jnp.bfloat16)] * 2
    out_specs = [pl.BlockSpec((n_rows, q_cols), lambda i: (block_index, 0))] * 2
    if with_prior:
        out_shape.append(jax.ShapeDtypeStruct(earlier.shape, jnp.float32))
        out_specs.append(pl.BlockSpec(earlier.shape, lambda i: (0, 0)))
    out_shape.append(jax.ShapeDtypeStruct((ctx_rows, kv_cols), jnp.float32))
    out_specs.append(pl.BlockSpec((ctx_rows, kv_cols), lambda i: (0, 0)))
    visible_blocks = 4 * len(unit_list)
    flops = 12 * rows * BLOCK * HEAD_SIZE * visible_blocks
    aliases = {} if out_alias is None else {len(operands) - 2: 0, len(operands) - 1: 1}
    return pl.pallas_call(
        kernel,
        grid=(1,),
        out_shape=tuple(out_shape),
        in_specs=in_specs,
        out_specs=tuple(out_specs),
        scratch_shapes=[
            pltpu.VMEM((units, rows, BLOCK), jnp.float32),
            pltpu.VMEM((rows, HEAD_SIZE), jnp.float32),
            pltpu.VMEM((rows, HEAD_SIZE), jnp.float32),
        ],
        input_output_aliases=aliases,
        compiler_params=pltpu.CompilerParams(vmem_limit_bytes=48 * 1024 * 1024),
        cost_estimate=pl.CostEstimate(flops=flops, transcendentals=2 * rows * BLOCK * visible_blocks,
                                      bytes_accessed=6 * 1024 * 1024),
        interpret=interpret,
    )(*operands)


def local(query_matrix, key_matrix, value_matrix, output_gradient, doc_start):
    token_per_shard = query_matrix.shape[0]
    head_groups = lax.axis_size("head")
    q_cols = query_matrix.shape[1] // head_groups
    k_cols = key_matrix.shape[1] // head_groups
    assert k_cols == HEAD_SIZE and 2 * token_per_shard == BLOCK
    kv_packed = jnp.concatenate(
        [
            key_matrix.reshape(token_per_shard, head_groups, k_cols),
            value_matrix.reshape(token_per_shard, head_groups, k_cols),
        ],
        axis=2,
    )
    kv = lax.all_to_all(kv_packed, "head", split_axis=1, concat_axis=0, tiled=True)
    ctx_rows = kv.shape[0]
    kv = kv.reshape(ctx_rows, 2 * k_cols)
    earlier_kv = from_behind(kv[BLOCK:], "ctx", 1)
    packed = lax.all_to_all(
        query_matrix.reshape(token_per_shard, head_groups, q_cols),
        "head", split_axis=1, concat_axis=0, tiled=True,
    ).reshape(ctx_rows, q_cols)
    units = ctx_rows // BLOCK
    ctx_index = lax.axis_index("ctx")
    unit_doc = jnp.cumsum(doc_start)
    own_units = lax.dynamic_slice_in_dim(unit_doc, ctx_index * units, units)
    prior_units = lax.dynamic_slice_in_dim(unit_doc, jnp.maximum(ctx_index - 1, 0) * units, units)
    prior_units = jnp.where(ctx_index > 0, prior_units, -1)
    joined_units = jnp.concatenate([prior_units, own_units])
    unit_ids = jnp.arange(units, dtype=jnp.int32)
    window = unit_ids[:, None] + 1 + unit_ids[None, :]
    same = (joined_units[window] == own_units[:, None]).astype(jnp.int32)
    lo = (unit_ids + units + 1 - jnp.sum(same, axis=1)).astype(jnp.int32)
    heads = q_cols // HEAD_SIZE
    first = attention_call(lo, packed, kv, earlier_kv, output_gradient, range(units - 1),
                           heads=heads, interpret=INTERPRET)
    attended_all, query_total, prior_grads, own_first = first
    last = attention_call(lo, packed, kv, None, output_gradient, [units - 1],
                          (attended_all, query_total), heads=heads, interpret=INTERPRET)
    attended_all, query_total, own_last = last
    own_grads = own_first + own_last
    score_scale = HEAD_SIZE ** (-0.5)
    prior_grads = jnp.concatenate(
        [(prior_grads[:, :k_cols] * score_scale).astype(jnp.bfloat16),
         prior_grads[:, k_cols:].astype(jnp.bfloat16)],
        axis=1,
    )
    later = from_behind(prior_grads, "ctx", -1).astype(jnp.float32)
    later = jnp.concatenate([jnp.zeros((BLOCK, 2 * k_cols), jnp.float32), later], axis=0)
    summed_keys = (own_grads[:, :k_cols] * score_scale + later[:, :k_cols]).astype(jnp.bfloat16)
    summed_values = (own_grads[:, k_cols:] + later[:, k_cols:]).astype(jnp.bfloat16)
    return (attended_all, query_total, summed_keys, summed_values)


def solution(mesh):
    placed = (
        P(("ctx", "head"), None),
        P(("ctx", "head"), None),
        P(("ctx", "head"), None),
        P("ctx", "head"),
        P(),
    )
    return jax.shard_map(
        local,
        mesh=mesh,
        in_specs=placed,
        out_specs=(P("ctx", "head"), P("ctx", "head"), P("ctx", "head"), P("ctx", "head")),
        check_vma=False,
    )
```

```python
import jax
import jax.numpy as jnp
from jax import lax
from jax.sharding import PartitionSpec as P
import functools
from jax.experimental import pallas as pl
from jax.experimental.pallas import tpu as pltpu

QUERY_HEADS = 32
KEY_VALUE_HEADS = 8
HEAD_SIZE = 128
BLOCK = 256
INTERPRET = False


def from_behind(block, axis, distance):
    devices = range(lax.axis_size(axis))
    route = [(i - distance, i) for i in devices if i - distance in devices]
    return lax.ppermute(block, axis, route)


def _nt(a, b):
    return lax.dot_general(a, b, (((1,), (1,)), ((), ())), preferred_element_type=jnp.float32)


def _tn(a, b):
    return lax.dot_general(a, b, (((0,), (0,)), ((), ())), preferred_element_type=jnp.float32)


def _nn(a, b):
    return lax.dot_general(a, b, (((1,), (0,)), ((), ())), preferred_element_type=jnp.float32)


def attention_kernel(*refs, first_unit, units, heads, with_prior, aliased):
    refs = list(refs)
    lo_ref, q_ref, kv_ref = refs[:3]
    refs = refs[3:]
    earlier_ref = refs.pop(0) if with_prior else None
    grad_ref = refs.pop(0)
    refs = refs[aliased:]
    att_ref, dq_ref = refs[:2]
    refs = refs[2:]
    prior_ref = refs.pop(0) if with_prior else None
    own_ref, s_scr, att_scr, dq_scr = refs
    scale = HEAD_SIZE ** (-0.5)
    step = pl.program_id(0)

    @pl.when(step == 0)
    def _():
        if with_prior:
            prior_ref[...] = jnp.zeros(prior_ref.shape, prior_ref.dtype)
        own_ref[...] = jnp.zeros(own_ref.shape, own_ref.dtype)

    rows = heads * BLOCK
    causal = (lax.broadcasted_iota(jnp.int32, (rows, BLOCK), 0) % BLOCK
              >= lax.broadcasted_iota(jnp.int32, (rows, BLOCK), 1))

    def load_kv(ref, col0, blk):
        start = pl.multiple_of(blk * BLOCK, BLOCK)
        return (ref[pl.ds(start, BLOCK), col0:col0 + HEAD_SIZE],
                ref[pl.ds(start, BLOCK), col0 + HEAD_SIZE:col0 + 2 * HEAD_SIZE])

    if True:
        u = first_unit + step
        qs = jnp.concatenate(
            [q_ref[:, h * HEAD_SIZE:(h + 1) * HEAD_SIZE] for h in range(heads)], axis=0)
        dos = jnp.concatenate(
            [grad_ref[:, h * HEAD_SIZE:(h + 1) * HEAD_SIZE] for h in range(heads)], axis=0)
        lo = lo_ref[u]
        diag = units + u
        first_own = jnp.maximum(lo, units)
        segments = ((kv_ref, 0, own_ref, first_own, diag, units),)
        if with_prior:
            segments = ((earlier_ref, 0, prior_ref, lo, units, 1),) + segments

        def pass1(b, carry, ref, col0, off):
            m, l = carry
            k, _ = load_kv(ref, col0, b - off)
            s = _nt(qs, k) * scale
            s_scr[b - (u + 1)] = s
            m_new = jnp.maximum(m, jnp.max(s, axis=1, keepdims=True))
            l = l * jnp.exp(m - m_new) + jnp.sum(jnp.exp(s - m_new), axis=1, keepdims=True)
            return m_new, l

        carry = (jnp.full((rows, 1), -jnp.inf, jnp.float32), jnp.zeros((rows, 1), jnp.float32))
        for ref, col0, _, start, stop, off in segments:
            carry = lax.fori_loop(start, stop, functools.partial(pass1, ref=ref, col0=col0, off=off), carry)
        m, l = carry
        k_d, v_d = load_kv(kv_ref, 0, u)
        s = jnp.where(causal, _nt(qs, k_d) * scale, -jnp.inf)
        m_new = jnp.maximum(m, jnp.max(s, axis=1, keepdims=True))
        l = l * jnp.exp(m - m_new) + jnp.sum(jnp.exp(s - m_new), axis=1, keepdims=True)
        lse = m_new + jnp.log(l)

        def pass2(b, _, ref, col0, off):
            _, v = load_kv(ref, col0, b - off)
            p = jnp.exp(s_scr[b - (u + 1)] - lse)
            s_scr[b - (u + 1)] = p
            att_scr[...] += _nn(p.astype(jnp.bfloat16), v)
            return 0

        p = jnp.exp(s - lse)
        att_scr[...] = _nn(p.astype(jnp.bfloat16), v_d)
        for ref, col0, _, start, stop, off in segments:
            lax.fori_loop(start, stop, functools.partial(pass2, ref=ref, col0=col0, off=off), 0)
        att = att_scr[...].astype(jnp.bfloat16)
        delta = jnp.sum(dos.astype(jnp.float32) * att.astype(jnp.float32), axis=1, keepdims=True)

        def pass3(b, _, ref, col0, gref, off):
            k, v = load_kv(ref, col0, b - off)
            p = s_scr[b - (u + 1)]
            ds = (p * (_nt(dos, v) - delta)).astype(jnp.bfloat16)
            dq_scr[...] += _nn(ds, k)
            start = pl.multiple_of((b - off) * BLOCK, BLOCK)
            gref[pl.ds(start, BLOCK), 0:HEAD_SIZE] += _tn(ds, qs)
            gref[pl.ds(start, BLOCK), HEAD_SIZE:2 * HEAD_SIZE] += _tn(p.astype(jnp.bfloat16), dos)
            return 0

        ds = (p * (_nt(dos, v_d) - delta)).astype(jnp.bfloat16)
        dq_scr[...] = _nn(ds, k_d)
        r0 = pl.multiple_of(u * BLOCK, BLOCK)
        own_ref[pl.ds(r0, BLOCK), 0:HEAD_SIZE] += _tn(ds, qs)
        own_ref[pl.ds(r0, BLOCK), HEAD_SIZE:2 * HEAD_SIZE] += _tn(p.astype(jnp.bfloat16), dos)
        for ref, col0, gref, start, stop, off in segments:
            lax.fori_loop(start, stop, functools.partial(pass3, ref=ref, col0=col0, gref=gref, off=off), 0)
        dq = (dq_scr[...] * scale).astype(jnp.bfloat16)
        for h in range(heads):
            att_ref[:, h * HEAD_SIZE:(h + 1) * HEAD_SIZE] = att[h * BLOCK:(h + 1) * BLOCK]
            dq_ref[:, h * HEAD_SIZE:(h + 1) * HEAD_SIZE] = dq[h * BLOCK:(h + 1) * BLOCK]


def attention_call(lo, packed, kv, earlier, grad, unit_list, out_alias=None, *, heads, interpret=False):
    ctx_rows = packed.shape[0]
    units = ctx_rows // BLOCK
    q_cols = heads * HEAD_SIZE
    kv_cols = 2 * HEAD_SIZE
    with_prior = earlier is not None
    aliased = 0 if out_alias is None else 2
    first_unit = unit_list[0]
    steps = len(unit_list)
    kernel = functools.partial(attention_kernel, first_unit=first_unit, units=units, heads=heads,
                               with_prior=with_prior, aliased=aliased)
    rows = heads * BLOCK

    def whole(x):
        return pl.BlockSpec(x.shape, lambda i: (0,) * len(x.shape))

    operands = [lo, packed, kv] + ([earlier] if with_prior else []) + [grad]
    unit_block = pl.BlockSpec((BLOCK, q_cols), lambda i: (first_unit + i, 0))
    in_specs = [pl.BlockSpec(memory_space=pltpu.SMEM), unit_block]
    in_specs += [whole(x) for x in operands[2:-1]] + [unit_block]
    if out_alias is not None:
        operands += list(out_alias)
        in_specs += [pl.BlockSpec(memory_space=pl.ANY)] * 2
    out_shape = [jax.ShapeDtypeStruct((ctx_rows, q_cols), jnp.bfloat16)] * 2
    out_specs = [unit_block] * 2
    if with_prior:
        out_shape.append(jax.ShapeDtypeStruct(earlier.shape, jnp.float32))
        out_specs.append(pl.BlockSpec(earlier.shape, lambda i: (0, 0)))
    out_shape.append(jax.ShapeDtypeStruct((ctx_rows, kv_cols), jnp.float32))
    out_specs.append(pl.BlockSpec((ctx_rows, kv_cols), lambda i: (0, 0)))
    visible_blocks = 4 * len(unit_list)
    flops = 12 * rows * BLOCK * HEAD_SIZE * visible_blocks
    aliases = {} if out_alias is None else {len(operands) - 2: 0, len(operands) - 1: 1}
    return pl.pallas_call(
        kernel,
        grid=(steps,),
        out_shape=tuple(out_shape),
        in_specs=in_specs,
        out_specs=tuple(out_specs),
        scratch_shapes=[
            pltpu.VMEM((units, rows, BLOCK), jnp.float32),
            pltpu.VMEM((rows, HEAD_SIZE), jnp.float32),
            pltpu.VMEM((rows, HEAD_SIZE), jnp.float32),
        ],
        input_output_aliases=aliases,
        compiler_params=pltpu.CompilerParams(
            dimension_semantics=("arbitrary",), vmem_limit_bytes=48 * 1024 * 1024),
        cost_estimate=pl.CostEstimate(flops=flops, transcendentals=2 * rows * BLOCK * visible_blocks,
                                      bytes_accessed=6 * 1024 * 1024),
        interpret=interpret,
    )(*operands)


def local(query_matrix, key_matrix, value_matrix, output_gradient, doc_start):
    token_per_shard = query_matrix.shape[0]
    head_groups = lax.axis_size("head")
    q_cols = query_matrix.shape[1] // head_groups
    k_cols = key_matrix.shape[1] // head_groups
    assert k_cols == HEAD_SIZE and 2 * token_per_shard == BLOCK
    kv_packed = jnp.concatenate(
        [
            key_matrix.reshape(token_per_shard, head_groups, k_cols),
            value_matrix.reshape(token_per_shard, head_groups, k_cols),
        ],
        axis=2,
    )
    kv = lax.all_to_all(kv_packed, "head", split_axis=1, concat_axis=0, tiled=True)
    ctx_rows = kv.shape[0]
    kv = kv.reshape(ctx_rows, 2 * k_cols)
    earlier_kv = from_behind(kv[BLOCK:], "ctx", 1)
    packed = lax.all_to_all(
        query_matrix.reshape(token_per_shard, head_groups, q_cols),
        "head", split_axis=1, concat_axis=0, tiled=True,
    ).reshape(ctx_rows, q_cols)
    units = ctx_rows // BLOCK
    ctx_index = lax.axis_index("ctx")
    unit_doc = jnp.cumsum(doc_start)
    own_units = lax.dynamic_slice_in_dim(unit_doc, ctx_index * units, units)
    prior_units = lax.dynamic_slice_in_dim(unit_doc, jnp.maximum(ctx_index - 1, 0) * units, units)
    prior_units = jnp.where(ctx_index > 0, prior_units, -1)
    joined_units = jnp.concatenate([prior_units, own_units])
    unit_ids = jnp.arange(units, dtype=jnp.int32)
    window = unit_ids[:, None] + 1 + unit_ids[None, :]
    same = (joined_units[window] == own_units[:, None]).astype(jnp.int32)
    lo = (unit_ids + units + 1 - jnp.sum(same, axis=1)).astype(jnp.int32)
    heads = q_cols // HEAD_SIZE
    first = attention_call(lo, packed, kv, earlier_kv, output_gradient, range(units - 1),
                           heads=heads, interpret=INTERPRET)
    attended_all, query_total, prior_grads, own_first = first
    last = attention_call(lo, packed, kv, None, output_gradient, [units - 1],
                          (attended_all, query_total), heads=heads, interpret=INTERPRET)
    attended_all, query_total, own_last = last
    own_grads = own_first + own_last
    score_scale = HEAD_SIZE ** (-0.5)
    prior_grads = jnp.concatenate(
        [(prior_grads[:, :k_cols] * score_scale).astype(jnp.bfloat16),
         prior_grads[:, k_cols:].astype(jnp.bfloat16)],
        axis=1,
    )
    later = from_behind(prior_grads, "ctx", -1).astype(jnp.float32)
    later = jnp.concatenate([jnp.zeros((BLOCK, 2 * k_cols), jnp.float32), later], axis=0)
    summed_keys = (own_grads[:, :k_cols] * score_scale + later[:, :k_cols]).astype(jnp.bfloat16)
    summed_values = (own_grads[:, k_cols:] + later[:, k_cols:]).astype(jnp.bfloat16)
    return (attended_all, query_total, summed_keys, summed_values)


def solution(mesh):
    placed = (
        P(("ctx", "head"), None),
        P(("ctx", "head"), None),
        P(("ctx", "head"), None),
        P("ctx", "head"),
        P(),
    )
    return jax.shard_map(
        local,
        mesh=mesh,
        in_specs=placed,
        out_specs=(P("ctx", "head"), P("ctx", "head"), P("ctx", "head"), P("ctx", "head")),
        check_vma=False,
    )
```

```python
import jax
import jax.numpy as jnp
from jax import lax
from jax.sharding import PartitionSpec as P
import functools
from jax.experimental import pallas as pl
from jax.experimental.pallas import tpu as pltpu

QUERY_HEADS = 32
KEY_VALUE_HEADS = 8
HEAD_SIZE = 128
BLOCK = 256
INTERPRET = False


def from_behind(block, axis, distance):
    devices = range(lax.axis_size(axis))
    route = [(i - distance, i) for i in devices if i - distance in devices]
    return lax.ppermute(block, axis, route)


def _nt(a, b):
    return lax.dot_general(a, b, (((1,), (1,)), ((), ())), preferred_element_type=jnp.float32)


def _tn(a, b):
    return lax.dot_general(a, b, (((0,), (0,)), ((), ())), preferred_element_type=jnp.float32)


def _nn(a, b):
    return lax.dot_general(a, b, (((1,), (0,)), ((), ())), preferred_element_type=jnp.float32)


def attention_kernel(*refs, first_unit, units, heads, with_prior, has_att, init_prior, init_own):
    refs = list(refs)
    lo_ref, q_ref, kv_ref = refs[:3]
    refs = refs[3:]
    earlier_ref = refs.pop(0) if with_prior else None
    grad_ref = refs.pop(0)
    if has_att:
        refs = refs[2:]
    prior_in = refs.pop(0) if with_prior and not init_prior else None
    own_in = None if init_own else refs.pop(0)
    att_ref, dq_ref = refs[:2]
    refs = refs[2:]
    prior_ref = refs.pop(0) if with_prior else None
    own_ref, s_scr, att_scr, dq_scr = refs
    scale = HEAD_SIZE ** (-0.5)
    step = pl.program_id(0)

    @pl.when(step == 0)
    def _():
        if with_prior:
            prior_ref[...] = (jnp.zeros(prior_ref.shape, prior_ref.dtype) if init_prior
                              else prior_in[...])
        own_ref[...] = jnp.zeros(own_ref.shape, own_ref.dtype) if init_own else own_in[...]

    rows = heads * BLOCK
    causal = (lax.broadcasted_iota(jnp.int32, (rows, BLOCK), 0) % BLOCK
              >= lax.broadcasted_iota(jnp.int32, (rows, BLOCK), 1))

    def load_kv(ref, col0, blk):
        start = pl.multiple_of(blk * BLOCK, BLOCK)
        return (ref[pl.ds(start, BLOCK), col0:col0 + HEAD_SIZE],
                ref[pl.ds(start, BLOCK), col0 + HEAD_SIZE:col0 + 2 * HEAD_SIZE])

    u = first_unit + step
    qs = jnp.concatenate(
        [q_ref[:, h * HEAD_SIZE:(h + 1) * HEAD_SIZE] for h in range(heads)], axis=0)
    dos = jnp.concatenate(
        [grad_ref[:, h * HEAD_SIZE:(h + 1) * HEAD_SIZE] for h in range(heads)], axis=0)
    lo = lo_ref[u]
    diag = units + u
    first_own = jnp.maximum(lo, units)
    segments = ((kv_ref, 0, own_ref, first_own, diag, units),)
    if with_prior:
        segments = ((earlier_ref, 0, prior_ref, lo, units, 1),) + segments

    def pass1(b, carry, ref, col0, off):
        m, l = carry
        k, _ = load_kv(ref, col0, b - off)
        s = _nt(qs, k) * scale
        s_scr[b - (u + 1)] = s
        m_new = jnp.maximum(m, jnp.max(s, axis=1, keepdims=True))
        l = l * jnp.exp(m - m_new) + jnp.sum(jnp.exp(s - m_new), axis=1, keepdims=True)
        return m_new, l

    carry = (jnp.full((rows, 1), -jnp.inf, jnp.float32), jnp.zeros((rows, 1), jnp.float32))
    for ref, col0, _, start, stop, off in segments:
        carry = lax.fori_loop(start, stop, functools.partial(pass1, ref=ref, col0=col0, off=off), carry)
    m, l = carry
    k_d, v_d = load_kv(kv_ref, 0, u)
    s = jnp.where(causal, _nt(qs, k_d) * scale, -jnp.inf)
    m_new = jnp.maximum(m, jnp.max(s, axis=1, keepdims=True))
    l = l * jnp.exp(m - m_new) + jnp.sum(jnp.exp(s - m_new), axis=1, keepdims=True)
    lse = m_new + jnp.log(l)

    def pass2(b, _, ref, col0, off):
        _, v = load_kv(ref, col0, b - off)
        p = jnp.exp(s_scr[b - (u + 1)] - lse)
        s_scr[b - (u + 1)] = p
        att_scr[...] += _nn(p.astype(jnp.bfloat16), v)
        return 0

    p = jnp.exp(s - lse)
    att_scr[...] = _nn(p.astype(jnp.bfloat16), v_d)
    for ref, col0, _, start, stop, off in segments:
        lax.fori_loop(start, stop, functools.partial(pass2, ref=ref, col0=col0, off=off), 0)
    att = att_scr[...].astype(jnp.bfloat16)
    delta = jnp.sum(dos.astype(jnp.float32) * att.astype(jnp.float32), axis=1, keepdims=True)

    def pass3(b, _, ref, col0, gref, off):
        k, v = load_kv(ref, col0, b - off)
        p = s_scr[b - (u + 1)]
        ds = (p * (_nt(dos, v) - delta)).astype(jnp.bfloat16)
        dq_scr[...] += _nn(ds, k)
        start = pl.multiple_of((b - off) * BLOCK, BLOCK)
        gref[pl.ds(start, BLOCK), 0:HEAD_SIZE] += _tn(ds, qs)
        gref[pl.ds(start, BLOCK), HEAD_SIZE:2 * HEAD_SIZE] += _tn(p.astype(jnp.bfloat16), dos)
        return 0

    ds = (p * (_nt(dos, v_d) - delta)).astype(jnp.bfloat16)
    dq_scr[...] = _nn(ds, k_d)
    r0 = pl.multiple_of(u * BLOCK, BLOCK)
    own_ref[pl.ds(r0, BLOCK), 0:HEAD_SIZE] += _tn(ds, qs)
    own_ref[pl.ds(r0, BLOCK), HEAD_SIZE:2 * HEAD_SIZE] += _tn(p.astype(jnp.bfloat16), dos)
    for ref, col0, gref, start, stop, off in segments:
        lax.fori_loop(start, stop, functools.partial(pass3, ref=ref, col0=col0, gref=gref, off=off), 0)
    dq = (dq_scr[...] * scale).astype(jnp.bfloat16)
    for h in range(heads):
        att_ref[:, h * HEAD_SIZE:(h + 1) * HEAD_SIZE] = att[h * BLOCK:(h + 1) * BLOCK]
        dq_ref[:, h * HEAD_SIZE:(h + 1) * HEAD_SIZE] = dq[h * BLOCK:(h + 1) * BLOCK]


def attention_call(lo, q, q_block, kv, earlier, grad, grad_block, unit_list, att=None, prior=None,
                   own=None, *, heads, interpret=False):
    ctx_rows = q.shape[0]
    units = ctx_rows // BLOCK
    width = heads * HEAD_SIZE
    kv_cols = 2 * HEAD_SIZE
    with_prior = earlier is not None
    first_unit = unit_list[0]
    steps = len(unit_list)
    kernel = functools.partial(attention_kernel, first_unit=first_unit, units=units, heads=heads,
                               with_prior=with_prior, has_att=att is not None,
                               init_prior=prior is None, init_own=own is None)
    rows = heads * BLOCK

    def whole(x):
        return pl.BlockSpec(x.shape, lambda i: (0,) * len(x.shape))

    operands = [lo, q, kv]
    in_specs = [pl.BlockSpec(memory_space=pltpu.SMEM),
                pl.BlockSpec((BLOCK, width), lambda i: (first_unit + i, q_block)),
                pl.BlockSpec((ctx_rows, kv_cols), lambda i: (0, 0))]
    if with_prior:
        operands.append(earlier)
        in_specs.append(whole(earlier))
    out_block = pl.BlockSpec((BLOCK, width), lambda i: (first_unit + i, grad_block))
    operands.append(grad)
    in_specs.append(out_block)
    aliases = {}
    if att is not None:
        aliases[len(operands)] = 0
        aliases[len(operands) + 1] = 1
        operands += list(att)
        in_specs += [pl.BlockSpec(memory_space=pl.ANY)] * 2
    n_out = 2
    if with_prior:
        if prior is not None:
            aliases[len(operands)] = n_out
            operands.append(prior)
            in_specs.append(whole(prior))
        n_out += 1
    if own is not None:
        aliases[len(operands)] = n_out
        operands.append(own)
        in_specs.append(whole(own))
    out_shape = [jax.ShapeDtypeStruct(grad.shape, jnp.bfloat16)] * 2
    out_specs = [out_block] * 2
    if with_prior:
        out_shape.append(jax.ShapeDtypeStruct(earlier.shape, jnp.float32))
        out_specs.append(whole(earlier))
    out_shape.append(jax.ShapeDtypeStruct((ctx_rows, kv_cols), jnp.float32))
    out_specs.append(pl.BlockSpec((ctx_rows, kv_cols), lambda i: (0, 0)))
    visible_blocks = 4 * steps
    flops = 12 * rows * BLOCK * HEAD_SIZE * visible_blocks
    return pl.pallas_call(
        kernel,
        grid=(steps,),
        out_shape=tuple(out_shape),
        in_specs=in_specs,
        out_specs=tuple(out_specs),
        scratch_shapes=[
            pltpu.VMEM((units, rows, BLOCK), jnp.float32),
            pltpu.VMEM((rows, HEAD_SIZE), jnp.float32),
            pltpu.VMEM((rows, HEAD_SIZE), jnp.float32),
        ],
        input_output_aliases=aliases,
        compiler_params=pltpu.CompilerParams(
            dimension_semantics=("arbitrary",), vmem_limit_bytes=48 * 1024 * 1024),
        cost_estimate=pl.CostEstimate(flops=flops, transcendentals=2 * rows * BLOCK * visible_blocks,
                                      bytes_accessed=3 * 1024 * 1024),
        interpret=interpret,
    )(*operands)


def local(query_matrix, key_matrix, value_matrix, output_gradient, doc_start):
    token_per_shard = query_matrix.shape[0]
    head_groups = lax.axis_size("head")
    q_cols = query_matrix.shape[1] // head_groups
    k_cols = key_matrix.shape[1] // head_groups
    assert k_cols == HEAD_SIZE and 2 * token_per_shard == BLOCK
    heads = q_cols // HEAD_SIZE
    half = heads // 2
    assert half * 2 == heads and half * HEAD_SIZE == 2 * k_cols
    query_groups = query_matrix.reshape(token_per_shard, head_groups, q_cols)
    first_packed = jnp.concatenate(
        [
            key_matrix.reshape(token_per_shard, head_groups, k_cols),
            value_matrix.reshape(token_per_shard, head_groups, k_cols),
            query_groups[:, :, : half * HEAD_SIZE],
        ],
        axis=2,
    )
    first = lax.all_to_all(first_packed, "head", split_axis=1, concat_axis=0, tiled=True)
    ctx_rows = first.shape[0]
    first = first.reshape(ctx_rows, 4 * k_cols)
    earlier_kv = from_behind(first[BLOCK:, : 2 * k_cols], "ctx", 1)
    second = lax.all_to_all(
        query_groups[:, :, half * HEAD_SIZE:], "head", split_axis=1, concat_axis=0, tiled=True
    ).reshape(ctx_rows, half * HEAD_SIZE)
    units = ctx_rows // BLOCK
    ctx_index = lax.axis_index("ctx")
    unit_doc = jnp.cumsum(doc_start)
    own_units = lax.dynamic_slice_in_dim(unit_doc, ctx_index * units, units)
    prior_units = lax.dynamic_slice_in_dim(unit_doc, jnp.maximum(ctx_index - 1, 0) * units, units)
    prior_units = jnp.where(ctx_index > 0, prior_units, -1)
    joined_units = jnp.concatenate([prior_units, own_units])
    unit_ids = jnp.arange(units, dtype=jnp.int32)
    window = unit_ids[:, None] + 1 + unit_ids[None, :]
    same = (joined_units[window] == own_units[:, None]).astype(jnp.int32)
    lo = (unit_ids + units + 1 - jnp.sum(same, axis=1)).astype(jnp.int32)
    call = functools.partial(attention_call, heads=half, interpret=INTERPRET)
    last_unit = [units - 1]
    early_units = range(units - 1)
    att, dq, own = call(lo, first, 1, first, None, output_gradient, 0, last_unit)
    att, dq, prior, own = call(lo, first, 1, first, earlier_kv, output_gradient, 0, early_units,
                               (att, dq), None, own)
    att, dq, prior, own = call(lo, second, 0, first, earlier_kv, output_gradient, 1, early_units,
                               (att, dq), prior, own)
    score_scale = HEAD_SIZE ** (-0.5)
    prior_grads = jnp.concatenate(
        [(prior[:, :k_cols] * score_scale).astype(jnp.bfloat16),
         prior[:, k_cols:].astype(jnp.bfloat16)],
        axis=1,
    )
    later = from_behind(prior_grads, "ctx", -1).astype(jnp.float32)
    att, dq, own = call(lo, second, 0, first, None, output_gradient, 1, last_unit, (att, dq), None, own)
    later = jnp.concatenate([jnp.zeros((BLOCK, 2 * k_cols), jnp.float32), later], axis=0)
    summed_keys = (own[:, :k_cols] * score_scale + later[:, :k_cols]).astype(jnp.bfloat16)
    summed_values = (own[:, k_cols:] + later[:, k_cols:]).astype(jnp.bfloat16)
    return (att, dq, summed_keys, summed_values)


def solution(mesh):
    placed = (
        P(("ctx", "head"), None),
        P(("ctx", "head"), None),
        P(("ctx", "head"), None),
        P("ctx", "head"),
        P(),
    )
    return jax.shard_map(
        local,
        mesh=mesh,
        in_specs=placed,
        out_specs=(P("ctx", "head"), P("ctx", "head"), P("ctx", "head"), P("ctx", "head")),
        check_vma=False,
    )
```

```python
import jax
import jax.numpy as jnp
from jax import lax
from jax.sharding import PartitionSpec as P
import functools
from jax.experimental import pallas as pl
from jax.experimental.pallas import tpu as pltpu

QUERY_HEADS = 32
KEY_VALUE_HEADS = 8
HEAD_SIZE = 128
BLOCK = 256
INTERPRET = False


def from_behind(block, axis, distance):
    devices = range(lax.axis_size(axis))
    route = [(i - distance, i) for i in devices if i - distance in devices]
    return lax.ppermute(block, axis, route)


def _nt(a, b):
    return lax.dot_general(a, b, (((1,), (1,)), ((), ())), preferred_element_type=jnp.float32)


def _tn(a, b):
    return lax.dot_general(a, b, (((0,), (0,)), ((), ())), preferred_element_type=jnp.float32)


def _nn(a, b):
    return lax.dot_general(a, b, (((1,), (0,)), ((), ())), preferred_element_type=jnp.float32)


def attention_kernel(*refs, first_unit, units, heads, with_prior, aliased):
    refs = list(refs)
    lo_ref, q_ref, kv_ref = refs[:3]
    refs = refs[3:]
    earlier_ref = refs.pop(0) if with_prior else None
    grad_ref = refs.pop(0)
    refs = refs[aliased:]
    att_ref, dq_ref = refs[:2]
    refs = refs[2:]
    prior_ref = refs.pop(0) if with_prior else None
    own_ref, s_scr, att_scr, dq_scr = refs
    scale = HEAD_SIZE ** (-0.5)
    step = pl.program_id(0)

    @pl.when(step == 0)
    def _():
        if with_prior:
            prior_ref[...] = jnp.zeros(prior_ref.shape, prior_ref.dtype)
        own_ref[...] = jnp.zeros(own_ref.shape, own_ref.dtype)

    rows = heads * BLOCK
    causal = (lax.broadcasted_iota(jnp.int32, (rows, BLOCK), 0) % BLOCK
              >= lax.broadcasted_iota(jnp.int32, (rows, BLOCK), 1))

    def load_kv(ref, col0, blk):
        start = pl.multiple_of(blk * BLOCK, BLOCK)
        return (ref[pl.ds(start, BLOCK), col0:col0 + HEAD_SIZE],
                ref[pl.ds(start, BLOCK), col0 + HEAD_SIZE:col0 + 2 * HEAD_SIZE])

    if True:
        u = first_unit + step
        qs = jnp.concatenate(
            [q_ref[:, h * HEAD_SIZE:(h + 1) * HEAD_SIZE] for h in range(heads)], axis=0)
        dos = jnp.concatenate(
            [grad_ref[:, h * HEAD_SIZE:(h + 1) * HEAD_SIZE] for h in range(heads)], axis=0)
        lo = lo_ref[u]
        diag = units + u
        first_own = jnp.maximum(lo, units)
        segments = ((kv_ref, 0, own_ref, first_own, diag, units),)
        if with_prior:
            segments = ((earlier_ref, 0, prior_ref, lo, units, 1),) + segments

        half = BLOCK // 2

        def pass1(b, m, ref, col0, off):
            k, _ = load_kv(ref, col0, b - off)
            s = _nt(qs, k) * scale
            s_scr[b - (u + 1)] = s
            return jnp.maximum(m, jnp.maximum(s[:, :half], s[:, half:]))

        k_d, v_d = load_kv(kv_ref, 0, u)
        s = jnp.where(causal, _nt(qs, k_d) * scale, -jnp.inf)
        m = jnp.maximum(s[:, :half], s[:, half:])
        for ref, col0, _, start, stop, off in segments:
            m = lax.fori_loop(start, stop, functools.partial(pass1, ref=ref, col0=col0, off=off), m)
        m = jnp.max(m, axis=1, keepdims=True)

        def pass1b(b, l):
            e = jnp.exp(s_scr[b - (u + 1)] - m)
            s_scr[b - (u + 1)] = e
            return l + e[:, :half] + e[:, half:]

        e = jnp.exp(s - m)
        l = lax.fori_loop(lo, diag, pass1b, e[:, :half] + e[:, half:])
        inv_total = 1.0 / jnp.sum(l, axis=1, keepdims=True)

        def pass2(b, _, ref, col0, off):
            _, v = load_kv(ref, col0, b - off)
            p = s_scr[b - (u + 1)] * inv_total
            s_scr[b - (u + 1)] = p
            att_scr[...] += _nn(p.astype(jnp.bfloat16), v)
            return 0

        p = e * inv_total
        att_scr[...] = _nn(p.astype(jnp.bfloat16), v_d)
        for ref, col0, _, start, stop, off in segments:
            lax.fori_loop(start, stop, functools.partial(pass2, ref=ref, col0=col0, off=off), 0)
        att = att_scr[...].astype(jnp.bfloat16)
        delta = jnp.sum(dos.astype(jnp.float32) * att.astype(jnp.float32), axis=1, keepdims=True)

        def pass3(b, _, ref, col0, gref, off):
            k, v = load_kv(ref, col0, b - off)
            p = s_scr[b - (u + 1)]
            ds = (p * (_nt(dos, v) - delta)).astype(jnp.bfloat16)
            dq_scr[...] += _nn(ds, k)
            start = pl.multiple_of((b - off) * BLOCK, BLOCK)
            gref[pl.ds(start, BLOCK), 0:HEAD_SIZE] += _tn(ds, qs)
            gref[pl.ds(start, BLOCK), HEAD_SIZE:2 * HEAD_SIZE] += _tn(p.astype(jnp.bfloat16), dos)
            return 0

        ds = (p * (_nt(dos, v_d) - delta)).astype(jnp.bfloat16)
        dq_scr[...] = _nn(ds, k_d)
        r0 = pl.multiple_of(u * BLOCK, BLOCK)
        own_ref[pl.ds(r0, BLOCK), 0:HEAD_SIZE] += _tn(ds, qs)
        own_ref[pl.ds(r0, BLOCK), HEAD_SIZE:2 * HEAD_SIZE] += _tn(p.astype(jnp.bfloat16), dos)
        for ref, col0, gref, start, stop, off in segments:
            lax.fori_loop(start, stop, functools.partial(pass3, ref=ref, col0=col0, gref=gref, off=off), 0)
        dq = (dq_scr[...] * scale).astype(jnp.bfloat16)
        for h in range(heads):
            att_ref[:, h * HEAD_SIZE:(h + 1) * HEAD_SIZE] = att[h * BLOCK:(h + 1) * BLOCK]
            dq_ref[:, h * HEAD_SIZE:(h + 1) * HEAD_SIZE] = dq[h * BLOCK:(h + 1) * BLOCK]


def attention_call(lo, packed, kv, earlier, grad, unit_list, out_alias=None, *, heads, interpret=False):
    ctx_rows = packed.shape[0]
    units = ctx_rows // BLOCK
    q_cols = heads * HEAD_SIZE
    kv_cols = 2 * HEAD_SIZE
    with_prior = earlier is not None
    aliased = 0 if out_alias is None else 2
    first_unit = unit_list[0]
    steps = len(unit_list)
    kernel = functools.partial(attention_kernel, first_unit=first_unit, units=units, heads=heads,
                               with_prior=with_prior, aliased=aliased)
    rows = heads * BLOCK

    def whole(x):
        return pl.BlockSpec(x.shape, lambda i: (0,) * len(x.shape))

    operands = [lo, packed, kv] + ([earlier] if with_prior else []) + [grad]
    unit_block = pl.BlockSpec((BLOCK, q_cols), lambda i: (first_unit + i, 0))
    in_specs = [pl.BlockSpec(memory_space=pltpu.SMEM), unit_block]
    in_specs += [whole(x) for x in operands[2:-1]] + [unit_block]
    if out_alias is not None:
        operands += list(out_alias)
        in_specs += [pl.BlockSpec(memory_space=pl.ANY)] * 2
    out_shape = [jax.ShapeDtypeStruct((ctx_rows, q_cols), jnp.bfloat16)] * 2
    out_specs = [unit_block] * 2
    if with_prior:
        out_shape.append(jax.ShapeDtypeStruct(earlier.shape, jnp.float32))
        out_specs.append(pl.BlockSpec(earlier.shape, lambda i: (0, 0)))
    out_shape.append(jax.ShapeDtypeStruct((ctx_rows, kv_cols), jnp.float32))
    out_specs.append(pl.BlockSpec((ctx_rows, kv_cols), lambda i: (0, 0)))
    visible_blocks = 4 * len(unit_list)
    flops = 12 * rows * BLOCK * HEAD_SIZE * visible_blocks
    aliases = {} if out_alias is None else {len(operands) - 2: 0, len(operands) - 1: 1}
    return pl.pallas_call(
        kernel,
        grid=(steps,),
        out_shape=tuple(out_shape),
        in_specs=in_specs,
        out_specs=tuple(out_specs),
        scratch_shapes=[
            pltpu.VMEM((units, rows, BLOCK), jnp.float32),
            pltpu.VMEM((rows, HEAD_SIZE), jnp.float32),
            pltpu.VMEM((rows, HEAD_SIZE), jnp.float32),
        ],
        input_output_aliases=aliases,
        compiler_params=pltpu.CompilerParams(
            dimension_semantics=("arbitrary",), vmem_limit_bytes=48 * 1024 * 1024),
        cost_estimate=pl.CostEstimate(flops=flops, transcendentals=2 * rows * BLOCK * visible_blocks,
                                      bytes_accessed=6 * 1024 * 1024),
        interpret=interpret,
    )(*operands)


def local(query_matrix, key_matrix, value_matrix, output_gradient, doc_start):
    token_per_shard = query_matrix.shape[0]
    head_groups = lax.axis_size("head")
    q_cols = query_matrix.shape[1] // head_groups
    k_cols = key_matrix.shape[1] // head_groups
    assert k_cols == HEAD_SIZE and 2 * token_per_shard == BLOCK
    kv_packed = jnp.concatenate(
        [
            key_matrix.reshape(token_per_shard, head_groups, k_cols),
            value_matrix.reshape(token_per_shard, head_groups, k_cols),
        ],
        axis=2,
    )
    kv = lax.all_to_all(kv_packed, "head", split_axis=1, concat_axis=0, tiled=True)
    ctx_rows = kv.shape[0]
    kv = kv.reshape(ctx_rows, 2 * k_cols)
    earlier_kv = from_behind(kv[BLOCK:], "ctx", 1)
    packed = lax.all_to_all(
        query_matrix.reshape(token_per_shard, head_groups, q_cols),
        "head", split_axis=1, concat_axis=0, tiled=True,
    ).reshape(ctx_rows, q_cols)
    units = ctx_rows // BLOCK
    ctx_index = lax.axis_index("ctx")
    unit_doc = jnp.cumsum(doc_start)
    own_units = lax.dynamic_slice_in_dim(unit_doc, ctx_index * units, units)
    prior_units = lax.dynamic_slice_in_dim(unit_doc, jnp.maximum(ctx_index - 1, 0) * units, units)
    prior_units = jnp.where(ctx_index > 0, prior_units, -1)
    joined_units = jnp.concatenate([prior_units, own_units])
    unit_ids = jnp.arange(units, dtype=jnp.int32)
    window = unit_ids[:, None] + 1 + unit_ids[None, :]
    same = (joined_units[window] == own_units[:, None]).astype(jnp.int32)
    lo = (unit_ids + units + 1 - jnp.sum(same, axis=1)).astype(jnp.int32)
    heads = q_cols // HEAD_SIZE
    first = attention_call(lo, packed, kv, earlier_kv, output_gradient, range(units - 1),
                           heads=heads, interpret=INTERPRET)
    attended_all, query_total, prior_grads, own_first = first
    last = attention_call(lo, packed, kv, None, output_gradient, [units - 1],
                          (attended_all, query_total), heads=heads, interpret=INTERPRET)
    attended_all, query_total, own_last = last
    own_grads = own_first + own_last
    score_scale = HEAD_SIZE ** (-0.5)
    prior_grads = jnp.concatenate(
        [(prior_grads[:, :k_cols] * score_scale).astype(jnp.bfloat16),
         prior_grads[:, k_cols:].astype(jnp.bfloat16)],
        axis=1,
    )
    later = from_behind(prior_grads, "ctx", -1).astype(jnp.float32)
    later = jnp.concatenate([jnp.zeros((BLOCK, 2 * k_cols), jnp.float32), later], axis=0)
    summed_keys = (own_grads[:, :k_cols] * score_scale + later[:, :k_cols]).astype(jnp.bfloat16)
    summed_values = (own_grads[:, k_cols:] + later[:, k_cols:]).astype(jnp.bfloat16)
    return (attended_all, query_total, summed_keys, summed_values)


def solution(mesh):
    placed = (
        P(("ctx", "head"), None),
        P(("ctx", "head"), None),
        P(("ctx", "head"), None),
        P("ctx", "head"),
        P(),
    )
    return jax.shard_map(
        local,
        mesh=mesh,
        in_specs=placed,
        out_specs=(P("ctx", "head"), P("ctx", "head"), P("ctx", "head"), P("ctx", "head")),
        check_vma=False,
    )
```

```python
import jax
import jax.numpy as jnp
from jax import lax
from jax.sharding import PartitionSpec as P
import functools
from jax.experimental import pallas as pl
from jax.experimental.pallas import tpu as pltpu

HEAD_SIZE = 128
BLOCK = 256
INTERPRET = False


def from_behind(block, axis, distance):
    devices = range(lax.axis_size(axis))
    route = [(i - distance, i) for i in devices if i - distance in devices]
    return lax.ppermute(block, axis, route)


def _nt(a, b):
    return lax.dot_general(a, b, (((1,), (1,)), ((), ())), preferred_element_type=jnp.float32)


def _tn(a, b):
    return lax.dot_general(a, b, (((0,), (0,)), ((), ())), preferred_element_type=jnp.float32)


def _nn(a, b):
    return lax.dot_general(a, b, (((1,), (0,)), ((), ())), preferred_element_type=jnp.float32)


def attention_kernel(*refs, first_unit, units, heads, with_prior, aliased):
    refs = list(refs)
    lo_ref, q_ref, kv_ref = refs[:3]
    refs = refs[3:]
    earlier_ref = refs.pop(0) if with_prior else None
    grad_ref = refs.pop(0)
    refs = refs[aliased:]
    att_ref, dq_ref = refs[:2]
    refs = refs[2:]
    prior_ref = refs.pop(0) if with_prior else None
    own_ref, s_scr, att_scr, dq_scr = refs
    scale = HEAD_SIZE ** (-0.5)
    step = pl.program_id(0)

    @pl.when(step == 0)
    def _():
        if with_prior:
            prior_ref[...] = jnp.zeros(prior_ref.shape, prior_ref.dtype)
        own_ref[...] = jnp.zeros(own_ref.shape, own_ref.dtype)

    rows = heads * BLOCK
    causal = (lax.broadcasted_iota(jnp.int32, (rows, BLOCK), 0) % BLOCK
              >= lax.broadcasted_iota(jnp.int32, (rows, BLOCK), 1))

    def load_kv(ref, col0, blk):
        start = pl.multiple_of(blk * BLOCK, BLOCK)
        return (ref[pl.ds(start, BLOCK), col0:col0 + HEAD_SIZE],
                ref[pl.ds(start, BLOCK), col0 + HEAD_SIZE:col0 + 2 * HEAD_SIZE])

    u = first_unit + step
    qs = jnp.concatenate(
        [q_ref[:, h * HEAD_SIZE:(h + 1) * HEAD_SIZE] for h in range(heads)], axis=0)
    dos = jnp.concatenate(
        [grad_ref[:, h * HEAD_SIZE:(h + 1) * HEAD_SIZE] for h in range(heads)], axis=0)
    lo = lo_ref[u]
    diag = units + u
    first_own = jnp.maximum(lo, units)
    segments = ((kv_ref, 0, own_ref, first_own, diag, units),)
    if with_prior:
        segments = ((earlier_ref, 0, prior_ref, lo, units, 1),) + segments

    half = BLOCK // 2

    def pass1(b, m, ref, col0, off):
        k, _ = load_kv(ref, col0, b - off)
        s = _nt(qs, k) * scale
        s_scr[b - (u + 1)] = s
        return jnp.maximum(m, jnp.maximum(s[:, :half], s[:, half:]))

    k_d, v_d = load_kv(kv_ref, 0, u)
    s = jnp.where(causal, _nt(qs, k_d) * scale, -jnp.inf)
    m = jnp.maximum(s[:, :half], s[:, half:])
    for ref, col0, _, start, stop, off in segments:
        m = lax.fori_loop(start, stop, functools.partial(pass1, ref=ref, col0=col0, off=off), m)
    m = jnp.max(m, axis=1, keepdims=True)

    def pass1b(b, l):
        e = jnp.exp(s_scr[b - (u + 1)] - m)
        s_scr[b - (u + 1)] = e
        return l + e[:, :half] + e[:, half:]

    e = jnp.exp(s - m)
    l = lax.fori_loop(lo, diag, pass1b, e[:, :half] + e[:, half:])
    inv_total = 1.0 / jnp.sum(l, axis=1, keepdims=True)

    def pass2(b, _, ref, col0, off):
        _, v = load_kv(ref, col0, b - off)
        p = s_scr[b - (u + 1)] * inv_total
        s_scr[b - (u + 1)] = p
        att_scr[...] += _nn(p.astype(jnp.bfloat16), v)
        return 0

    p = e * inv_total
    att_scr[...] = _nn(p.astype(jnp.bfloat16), v_d)
    for ref, col0, _, start, stop, off in segments:
        lax.fori_loop(start, stop, functools.partial(pass2, ref=ref, col0=col0, off=off), 0)
    att = att_scr[...].astype(jnp.bfloat16)
    delta = jnp.sum(dos.astype(jnp.float32) * att.astype(jnp.float32), axis=1, keepdims=True)

    def pass3(b, _, ref, col0, gref, off):
        k, v = load_kv(ref, col0, b - off)
        p = s_scr[b - (u + 1)]
        ds = (p * (_nt(dos, v) - delta)).astype(jnp.bfloat16)
        dq_scr[...] += _nn(ds, k)
        start = pl.multiple_of((b - off) * BLOCK, BLOCK)
        gref[pl.ds(start, BLOCK), 0:HEAD_SIZE] += _tn(ds, qs)
        gref[pl.ds(start, BLOCK), HEAD_SIZE:2 * HEAD_SIZE] += _tn(p.astype(jnp.bfloat16), dos)
        return 0

    ds = (p * (_nt(dos, v_d) - delta)).astype(jnp.bfloat16)
    dq_scr[...] = _nn(ds, k_d)
    r0 = pl.multiple_of(u * BLOCK, BLOCK)
    own_ref[pl.ds(r0, BLOCK), 0:HEAD_SIZE] += _tn(ds, qs)
    own_ref[pl.ds(r0, BLOCK), HEAD_SIZE:2 * HEAD_SIZE] += _tn(p.astype(jnp.bfloat16), dos)
    for ref, col0, gref, start, stop, off in segments:
        lax.fori_loop(start, stop, functools.partial(pass3, ref=ref, col0=col0, gref=gref, off=off), 0)
    dq = (dq_scr[...] * scale).astype(jnp.bfloat16)
    for h in range(heads):
        att_ref[:, h * HEAD_SIZE:(h + 1) * HEAD_SIZE] = att[h * BLOCK:(h + 1) * BLOCK]
        dq_ref[:, h * HEAD_SIZE:(h + 1) * HEAD_SIZE] = dq[h * BLOCK:(h + 1) * BLOCK]


def attention_call(lo, packed, kv, earlier, grad, unit_list, out_alias=None, *, heads, interpret=False):
    ctx_rows = packed.shape[0]
    units = ctx_rows // BLOCK
    q_cols = heads * HEAD_SIZE
    kv_cols = 2 * HEAD_SIZE
    with_prior = earlier is not None
    aliased = 0 if out_alias is None else 2
    first_unit = unit_list[0]
    steps = len(unit_list)
    kernel = functools.partial(attention_kernel, first_unit=first_unit, units=units, heads=heads,
                               with_prior=with_prior, aliased=aliased)
    rows = heads * BLOCK

    def whole(x):
        return pl.BlockSpec(x.shape, lambda i: (0,) * len(x.shape))

    operands = [lo, packed, kv] + ([earlier] if with_prior else []) + [grad]
    unit_block = pl.BlockSpec((BLOCK, q_cols), lambda i: (first_unit + i, 0))
    in_specs = [pl.BlockSpec(memory_space=pltpu.SMEM), unit_block]
    in_specs += [whole(x) for x in operands[2:-1]] + [unit_block]
    if out_alias is not None:
        operands += list(out_alias)
        in_specs += [pl.BlockSpec(memory_space=pl.ANY)] * 2
    out_shape = [jax.ShapeDtypeStruct((ctx_rows, q_cols), jnp.bfloat16)] * 2
    out_specs = [unit_block] * 2
    if with_prior:
        out_shape.append(jax.ShapeDtypeStruct(earlier.shape, jnp.float32))
        out_specs.append(pl.BlockSpec(earlier.shape, lambda i: (0, 0)))
    out_shape.append(jax.ShapeDtypeStruct((ctx_rows, kv_cols), jnp.float32))
    out_specs.append(pl.BlockSpec((ctx_rows, kv_cols), lambda i: (0, 0)))
    visible_blocks = 4 * len(unit_list)
    flops = 12 * rows * BLOCK * HEAD_SIZE * visible_blocks
    aliases = {} if out_alias is None else {len(operands) - 2: 0, len(operands) - 1: 1}
    return pl.pallas_call(
        kernel,
        grid=(steps,),
        out_shape=tuple(out_shape),
        in_specs=in_specs,
        out_specs=tuple(out_specs),
        scratch_shapes=[
            pltpu.VMEM((units, rows, BLOCK), jnp.float32),
            pltpu.VMEM((rows, HEAD_SIZE), jnp.float32),
            pltpu.VMEM((rows, HEAD_SIZE), jnp.float32),
        ],
        input_output_aliases=aliases,
        compiler_params=pltpu.CompilerParams(
            dimension_semantics=("arbitrary",), vmem_limit_bytes=48 * 1024 * 1024),
        cost_estimate=pl.CostEstimate(flops=flops, transcendentals=2 * rows * BLOCK * visible_blocks,
                                      bytes_accessed=6 * 1024 * 1024),
        interpret=interpret,
    )(*operands)


def local_body(query_matrix, key_matrix, value_matrix, output_gradient, doc_start):
    token_per_shard = query_matrix.shape[0]
    head_groups = lax.axis_size("head")
    q_cols = query_matrix.shape[1] // head_groups
    k_cols = key_matrix.shape[1] // head_groups
    assert k_cols == HEAD_SIZE and 2 * token_per_shard == BLOCK
    kv_packed = jnp.concatenate(
        [
            key_matrix.reshape(token_per_shard, head_groups, k_cols),
            value_matrix.reshape(token_per_shard, head_groups, k_cols),
        ],
        axis=2,
    )
    kv = lax.all_to_all(kv_packed, "head", split_axis=1, concat_axis=0, tiled=True)
    ctx_rows = kv.shape[0]
    kv = kv.reshape(ctx_rows, 2 * k_cols)
    earlier_kv = from_behind(kv[BLOCK:], "ctx", 1)
    packed = lax.all_to_all(
        query_matrix.reshape(token_per_shard, head_groups, q_cols),
        "head", split_axis=1, concat_axis=0, tiled=True,
    ).reshape(ctx_rows, q_cols)
    units = ctx_rows // BLOCK
    ctx_index = lax.axis_index("ctx")
    unit_doc = jnp.cumsum(doc_start)
    own_units = lax.dynamic_slice_in_dim(unit_doc, ctx_index * units, units)
    prior_units = lax.dynamic_slice_in_dim(unit_doc, jnp.maximum(ctx_index - 1, 0) * units, units)
    prior_units = jnp.where(ctx_index > 0, prior_units, -1)
    joined_units = jnp.concatenate([prior_units, own_units])
    unit_ids = jnp.arange(units, dtype=jnp.int32)
    window = unit_ids[:, None] + 1 + unit_ids[None, :]
    same = (joined_units[window] == own_units[:, None]).astype(jnp.int32)
    lo = (unit_ids + units + 1 - jnp.sum(same, axis=1)).astype(jnp.int32)
    heads = q_cols // HEAD_SIZE
    call = functools.partial(attention_call, heads=heads, interpret=INTERPRET)
    score_scale = HEAD_SIZE ** (-0.5)

    def to_link(grads):
        return jnp.concatenate(
            [(grads[:, :k_cols] * score_scale).astype(jnp.bfloat16),
             grads[:, k_cols:].astype(jnp.bfloat16)],
            axis=1,
        )

    split = (units - 2) * BLOCK
    attended_all, query_total, prior_a, own_a = call(
        lo, packed, kv, earlier_kv, output_gradient, range(units - 2))
    later_a = from_behind(to_link(prior_a[:split]), "ctx", -1)
    attended_all, query_total, prior_b, own_b = call(
        lo, packed, kv, earlier_kv, output_gradient, [units - 2], (attended_all, query_total))
    later_b = from_behind(to_link(prior_a[split:] + prior_b[split:]), "ctx", -1)
    attended_all, query_total, own_c = call(
        lo, packed, kv, None, output_gradient, [units - 1], (attended_all, query_total))
    own_grads = own_a + own_b + own_c
    later = jnp.concatenate(
        [jnp.zeros((BLOCK, 2 * k_cols), jnp.float32), later_a.astype(jnp.float32),
         later_b.astype(jnp.float32)], axis=0)
    summed_keys = (own_grads[:, :k_cols] * score_scale + later[:, :k_cols]).astype(jnp.bfloat16)
    summed_values = (own_grads[:, k_cols:] + later[:, k_cols:]).astype(jnp.bfloat16)
    return (attended_all, query_total, summed_keys, summed_values)


def solution(mesh):
    placed = (
        P(("ctx", "head"), None),
        P(("ctx", "head"), None),
        P(("ctx", "head"), None),
        P("ctx", "head"),
        P(),
    )
    return jax.shard_map(
        local_body,
        mesh=mesh,
        in_specs=placed,
        out_specs=(P("ctx", "head"), P("ctx", "head"), P("ctx", "head"), P("ctx", "head")),
        check_vma=False,
    )
```

```python
import jax
import jax.numpy as jnp
from jax import lax
from jax.sharding import PartitionSpec as P
import functools
from jax.experimental import pallas as pl
from jax.experimental.pallas import tpu as pltpu

QUERY_HEADS = 32
KEY_VALUE_HEADS = 8
HEAD_SIZE = 128
BLOCK = 256
INTERPRET = False


def from_behind(block, axis, distance):
    devices = range(lax.axis_size(axis))
    route = [(i - distance, i) for i in devices if i - distance in devices]
    return lax.ppermute(block, axis, route)


def _nt(a, b):
    return lax.dot_general(a, b, (((1,), (1,)), ((), ())), preferred_element_type=jnp.float32)


def _tn(a, b):
    return lax.dot_general(a, b, (((0,), (0,)), ((), ())), preferred_element_type=jnp.float32)


def _nn(a, b):
    return lax.dot_general(a, b, (((1,), (0,)), ((), ())), preferred_element_type=jnp.float32)


def attention_kernel(*refs, first_unit, units, heads, with_prior, aliased, steps):
    refs = list(refs)
    lo_ref, q_ref, kv_ref = refs[:3]
    refs = refs[3:]
    earlier_ref = refs.pop(0) if with_prior else None
    grad_ref = refs.pop(0)
    refs = refs[aliased:]
    att_ref, dq_ref = refs[:2]
    refs = refs[2:]
    prior_out = refs.pop(0) if with_prior else None
    own_ref, s_scr, att_scr, dq_scr = refs[:4]
    prior_ref = refs[4] if with_prior else None
    scale = HEAD_SIZE ** (-0.5)
    step = pl.program_id(0)

    @pl.when(step == 0)
    def _():
        if with_prior:
            prior_ref[...] = jnp.zeros(prior_ref.shape, prior_ref.dtype)
        own_ref[...] = jnp.zeros(own_ref.shape, own_ref.dtype)

    rows = heads * BLOCK
    causal = (lax.broadcasted_iota(jnp.int32, (rows, BLOCK), 0) % BLOCK
              >= lax.broadcasted_iota(jnp.int32, (rows, BLOCK), 1))

    def load_kv(ref, col0, blk):
        start = pl.multiple_of(blk * BLOCK, BLOCK)
        return (ref[pl.ds(start, BLOCK), col0:col0 + HEAD_SIZE],
                ref[pl.ds(start, BLOCK), col0 + HEAD_SIZE:col0 + 2 * HEAD_SIZE])

    if True:
        u = first_unit + step
        qs = jnp.concatenate(
            [q_ref[:, h * HEAD_SIZE:(h + 1) * HEAD_SIZE] for h in range(heads)], axis=0)
        dos = jnp.concatenate(
            [grad_ref[:, h * HEAD_SIZE:(h + 1) * HEAD_SIZE] for h in range(heads)], axis=0)
        lo = lo_ref[u]
        diag = units + u
        first_own = jnp.maximum(lo, units)
        segments = ((kv_ref, 0, own_ref, first_own, diag, units),)
        if with_prior:
            segments = ((earlier_ref, 0, prior_ref, lo, units, 1),) + segments

        half = BLOCK // 2

        def pass1(b, m, ref, col0, off):
            k, _ = load_kv(ref, col0, b - off)
            s = _nt(qs, k) * scale
            s_scr[b - (u + 1)] = s
            return jnp.maximum(m, jnp.maximum(s[:, :half], s[:, half:]))

        k_d, v_d = load_kv(kv_ref, 0, u)
        s = jnp.where(causal, _nt(qs, k_d) * scale, -jnp.inf)
        m = jnp.maximum(s[:, :half], s[:, half:])
        for ref, col0, _, start, stop, off in segments:
            m = lax.fori_loop(start, stop, functools.partial(pass1, ref=ref, col0=col0, off=off), m)
        m = jnp.max(m, axis=1, keepdims=True)

        def pass1b(b, l):
            e = jnp.exp(s_scr[b - (u + 1)] - m)
            s_scr[b - (u + 1)] = e
            return l + e[:, :half] + e[:, half:]

        e = jnp.exp(s - m)
        l = lax.fori_loop(lo, diag, pass1b, e[:, :half] + e[:, half:])
        inv_total = 1.0 / jnp.sum(l, axis=1, keepdims=True)

        def pass2(b, _, ref, col0, off):
            _, v = load_kv(ref, col0, b - off)
            p = s_scr[b - (u + 1)] * inv_total
            s_scr[b - (u + 1)] = p
            att_scr[...] += _nn(p.astype(jnp.bfloat16), v)
            return 0

        p = e * inv_total
        att_scr[...] = _nn(p.astype(jnp.bfloat16), v_d)
        for ref, col0, _, start, stop, off in segments:
            lax.fori_loop(start, stop, functools.partial(pass2, ref=ref, col0=col0, off=off), 0)
        att = att_scr[...].astype(jnp.bfloat16)
        delta = jnp.sum(dos.astype(jnp.float32) * att.astype(jnp.float32), axis=1, keepdims=True)

        def pass3(b, _, ref, col0, gref, off):
            k, v = load_kv(ref, col0, b - off)
            p = s_scr[b - (u + 1)]
            ds = (p * (_nt(dos, v) - delta)).astype(jnp.bfloat16)
            dq_scr[...] += _nn(ds, k)
            start = pl.multiple_of((b - off) * BLOCK, BLOCK)
            gref[pl.ds(start, BLOCK), 0:HEAD_SIZE] += _tn(ds, qs)
            gref[pl.ds(start, BLOCK), HEAD_SIZE:2 * HEAD_SIZE] += _tn(p.astype(jnp.bfloat16), dos)
            return 0

        ds = (p * (_nt(dos, v_d) - delta)).astype(jnp.bfloat16)
        dq_scr[...] = _nn(ds, k_d)
        r0 = pl.multiple_of(u * BLOCK, BLOCK)
        own_ref[pl.ds(r0, BLOCK), 0:HEAD_SIZE] += _tn(ds, qs)
        own_ref[pl.ds(r0, BLOCK), HEAD_SIZE:2 * HEAD_SIZE] += _tn(p.astype(jnp.bfloat16), dos)
        for ref, col0, gref, start, stop, off in segments:
            lax.fori_loop(start, stop, functools.partial(pass3, ref=ref, col0=col0, gref=gref, off=off), 0)
        dq = (dq_scr[...] * scale).astype(jnp.bfloat16)
        for h in range(heads):
            att_ref[:, h * HEAD_SIZE:(h + 1) * HEAD_SIZE] = att[h * BLOCK:(h + 1) * BLOCK]
            dq_ref[:, h * HEAD_SIZE:(h + 1) * HEAD_SIZE] = dq[h * BLOCK:(h + 1) * BLOCK]

    if with_prior:
        @pl.when(step == steps - 1)
        def _():
            prior_out[:, 0:HEAD_SIZE] = (prior_ref[:, 0:HEAD_SIZE] * scale).astype(prior_out.dtype)
            prior_out[:, HEAD_SIZE:] = prior_ref[:, HEAD_SIZE:].astype(prior_out.dtype)


def attention_call(lo, packed, kv, earlier, grad, unit_list, out_alias=None, *, heads, interpret=False):
    ctx_rows = packed.shape[0]
    units = ctx_rows // BLOCK
    q_cols = heads * HEAD_SIZE
    kv_cols = 2 * HEAD_SIZE
    with_prior = earlier is not None
    aliased = 0 if out_alias is None else 2
    first_unit = unit_list[0]
    steps = len(unit_list)
    kernel = functools.partial(attention_kernel, first_unit=first_unit, units=units, heads=heads,
                               with_prior=with_prior, aliased=aliased, steps=steps)
    rows = heads * BLOCK

    def whole(x):
        return pl.BlockSpec(x.shape, lambda i: (0,) * len(x.shape))

    operands = [lo, packed, kv] + ([earlier] if with_prior else []) + [grad]
    unit_block = pl.BlockSpec((BLOCK, q_cols), lambda i: (first_unit + i, 0))
    in_specs = [pl.BlockSpec(memory_space=pltpu.SMEM), unit_block]
    in_specs += [whole(x) for x in operands[2:-1]] + [unit_block]
    if out_alias is not None:
        operands += list(out_alias)
        in_specs += [pl.BlockSpec(memory_space=pl.ANY)] * 2
    out_shape = [jax.ShapeDtypeStruct((ctx_rows, q_cols), jnp.bfloat16)] * 2
    out_specs = [unit_block] * 2
    if with_prior:
        out_shape.append(jax.ShapeDtypeStruct(earlier.shape, jnp.bfloat16))
        out_specs.append(pl.BlockSpec(earlier.shape, lambda i: (0, 0)))
    out_shape.append(jax.ShapeDtypeStruct((ctx_rows, kv_cols), jnp.float32))
    out_specs.append(pl.BlockSpec((ctx_rows, kv_cols), lambda i: (0, 0)))
    visible_blocks = 4 * len(unit_list)
    flops = 12 * rows * BLOCK * HEAD_SIZE * visible_blocks
    aliases = {} if out_alias is None else {len(operands) - 2: 0, len(operands) - 1: 1}
    return pl.pallas_call(
        kernel,
        grid=(steps,),
        out_shape=tuple(out_shape),
        in_specs=in_specs,
        out_specs=tuple(out_specs),
        scratch_shapes=[
            pltpu.VMEM((units, rows, BLOCK), jnp.float32),
            pltpu.VMEM((rows, HEAD_SIZE), jnp.float32),
            pltpu.VMEM((rows, HEAD_SIZE), jnp.float32),
        ] + ([pltpu.VMEM(earlier.shape, jnp.float32)] if with_prior else []),
        input_output_aliases=aliases,
        compiler_params=pltpu.CompilerParams(
            dimension_semantics=("arbitrary",), vmem_limit_bytes=48 * 1024 * 1024),
        cost_estimate=pl.CostEstimate(flops=flops, transcendentals=2 * rows * BLOCK * visible_blocks,
                                      bytes_accessed=6 * 1024 * 1024),
        interpret=interpret,
    )(*operands)


def local(query_matrix, key_matrix, value_matrix, output_gradient, doc_start):
    token_per_shard = query_matrix.shape[0]
    head_groups = lax.axis_size("head")
    q_cols = query_matrix.shape[1] // head_groups
    k_cols = key_matrix.shape[1] // head_groups
    assert k_cols == HEAD_SIZE and 2 * token_per_shard == BLOCK
    kv_packed = jnp.concatenate(
        [
            key_matrix.reshape(token_per_shard, head_groups, k_cols),
            value_matrix.reshape(token_per_shard, head_groups, k_cols),
        ],
        axis=2,
    )
    kv = lax.all_to_all(kv_packed, "head", split_axis=1, concat_axis=0, tiled=True)
    ctx_rows = kv.shape[0]
    kv = kv.reshape(ctx_rows, 2 * k_cols)
    earlier_kv = from_behind(kv[BLOCK:], "ctx", 1)
    packed = lax.all_to_all(
        query_matrix.reshape(token_per_shard, head_groups, q_cols),
        "head", split_axis=1, concat_axis=0, tiled=True,
    ).reshape(ctx_rows, q_cols)
    units = ctx_rows // BLOCK
    ctx_index = lax.axis_index("ctx")
    wanted = (ctx_index - 1) * units + jnp.arange(2 * units, dtype=jnp.int32)
    unit_at = jnp.arange(doc_start.shape[0], dtype=jnp.int32)
    joined_units = jnp.sum(jnp.where(unit_at[None, :] <= wanted[:, None], doc_start[None, :], 0), axis=1)
    joined_units = jnp.where(wanted >= 0, joined_units, -1)
    own_units = joined_units[units:]
    unit_ids = jnp.arange(units, dtype=jnp.int32)
    window = unit_ids[:, None] + 1 + unit_ids[None, :]
    same = (joined_units[window] == own_units[:, None]).astype(jnp.int32)
    lo = (unit_ids + units + 1 - jnp.sum(same, axis=1)).astype(jnp.int32)
    heads = q_cols // HEAD_SIZE
    first = attention_call(lo, packed, kv, earlier_kv, output_gradient, range(units - 1),
                           heads=heads, interpret=INTERPRET)
    attended_all, query_total, prior_grads, own_first = first
    last = attention_call(lo, packed, kv, None, output_gradient, [units - 1],
                          (attended_all, query_total), heads=heads, interpret=INTERPRET)
    attended_all, query_total, own_last = last
    own_grads = own_first + own_last
    score_scale = HEAD_SIZE ** (-0.5)
    later = from_behind(prior_grads, "ctx", -1).astype(jnp.float32)
    later = jnp.concatenate([jnp.zeros((BLOCK, 2 * k_cols), jnp.float32), later], axis=0)
    summed_keys = (own_grads[:, :k_cols] * score_scale + later[:, :k_cols]).astype(jnp.bfloat16)
    summed_values = (own_grads[:, k_cols:] + later[:, k_cols:]).astype(jnp.bfloat16)
    return (attended_all, query_total, summed_keys, summed_values)


def solution(mesh):
    placed = (
        P(("ctx", "head"), None),
        P(("ctx", "head"), None),
        P(("ctx", "head"), None),
        P("ctx", "head"),
        P(),
    )
    return jax.shard_map(
        local,
        mesh=mesh,
        in_specs=placed,
        out_specs=(P("ctx", "head"), P("ctx", "head"), P("ctx", "head"), P("ctx", "head")),
        check_vma=False,
    )
```

```python
import jax
import jax.numpy as jnp
from jax import lax
from jax.sharding import PartitionSpec as P
import functools
from jax.experimental import pallas as pl
from jax.experimental.pallas import tpu as pltpu

QUERY_HEADS = 32
KEY_VALUE_HEADS = 8
HEAD_SIZE = 128
BLOCK = 256
INTERPRET = False


def from_behind(block, axis, distance):
    devices = range(lax.axis_size(axis))
    route = [(i - distance, i) for i in devices if i - distance in devices]
    return lax.ppermute(block, axis, route)


def _nt(a, b):
    return lax.dot_general(a, b, (((1,), (1,)), ((), ())), preferred_element_type=jnp.float32)


def _tn(a, b):
    return lax.dot_general(a, b, (((0,), (0,)), ((), ())), preferred_element_type=jnp.float32)


def _nn(a, b):
    return lax.dot_general(a, b, (((1,), (0,)), ((), ())), preferred_element_type=jnp.float32)


def attention_kernel(*refs, first_unit, units, heads, with_prior, aliased, steps):
    refs = list(refs)
    lo_ref, q_ref, kv_ref = refs[:3]
    refs = refs[3:]
    earlier_ref = refs.pop(0) if with_prior else None
    grad_ref = refs.pop(0)
    refs = refs[aliased:]
    att_ref, dq_ref = refs[:2]
    refs = refs[2:]
    prior_out = refs.pop(0) if with_prior else None
    own_ref, s_scr, att_scr, dq_scr = refs[:4]
    prior_ref = refs[4] if with_prior else None
    scale = HEAD_SIZE ** (-0.5)
    step = pl.program_id(0)

    @pl.when(step == 0)
    def _():
        if with_prior:
            prior_ref[...] = jnp.zeros(prior_ref.shape, prior_ref.dtype)
        own_ref[...] = jnp.zeros(own_ref.shape, own_ref.dtype)

    rows = heads * BLOCK
    causal = (lax.broadcasted_iota(jnp.int32, (rows, BLOCK), 0) % BLOCK
              >= lax.broadcasted_iota(jnp.int32, (rows, BLOCK), 1))

    def load_kv(ref, col0, blk):
        start = pl.multiple_of(blk * BLOCK, BLOCK)
        return (ref[pl.ds(start, BLOCK), col0:col0 + HEAD_SIZE],
                ref[pl.ds(start, BLOCK), col0 + HEAD_SIZE:col0 + 2 * HEAD_SIZE])

    if True:
        u = first_unit + step
        qs = jnp.concatenate(
            [q_ref[:, h * HEAD_SIZE:(h + 1) * HEAD_SIZE] for h in range(heads)], axis=0)
        dos = jnp.concatenate(
            [grad_ref[:, h * HEAD_SIZE:(h + 1) * HEAD_SIZE] for h in range(heads)], axis=0)
        lo = lo_ref[u]
        diag = units + u
        first_own = jnp.maximum(lo, units)
        segments = ((kv_ref, 0, own_ref, first_own, diag, units),)
        if with_prior:
            segments = ((earlier_ref, 0, prior_ref, lo, units, 1),) + segments

        half = BLOCK // 2

        def pass1(b, m, ref, col0, off):
            k, _ = load_kv(ref, col0, b - off)
            s = _nt(qs, k) * scale
            s_scr[b - (u + 1)] = s
            return jnp.maximum(m, jnp.maximum(s[:, :half], s[:, half:]))

        k_d, v_d = load_kv(kv_ref, 0, u)
        s = jnp.where(causal, _nt(qs, k_d) * scale, -jnp.inf)
        m = jnp.maximum(s[:, :half], s[:, half:])
        for ref, col0, _, start, stop, off in segments:
            m = lax.fori_loop(start, stop, functools.partial(pass1, ref=ref, col0=col0, off=off), m)
        m = jnp.max(m, axis=1, keepdims=True)

        def pass1b(b, l):
            e = jnp.exp(s_scr[b - (u + 1)] - m)
            s_scr[b - (u + 1)] = e
            return l + e[:, :half] + e[:, half:]

        e = jnp.exp(s - m)
        l = lax.fori_loop(lo, diag, pass1b, e[:, :half] + e[:, half:])
        inv_total = 1.0 / jnp.sum(l, axis=1, keepdims=True)

        def pass2(b, _, ref, col0, off):
            _, v = load_kv(ref, col0, b - off)
            p = s_scr[b - (u + 1)] * inv_total
            s_scr[b - (u + 1)] = p
            att_scr[...] += _nn(p.astype(jnp.bfloat16), v)
            return 0

        p = e * inv_total
        att_scr[...] = _nn(p.astype(jnp.bfloat16), v_d)
        for ref, col0, _, start, stop, off in segments:
            lax.fori_loop(start, stop, functools.partial(pass2, ref=ref, col0=col0, off=off), 0)
        att = att_scr[...].astype(jnp.bfloat16)
        delta = jnp.sum(dos.astype(jnp.float32) * att.astype(jnp.float32), axis=1, keepdims=True)

        def pass3(b, _, ref, col0, gref, off):
            k, v = load_kv(ref, col0, b - off)
            p = s_scr[b - (u + 1)]
            ds = (p * (_nt(dos, v) - delta)).astype(jnp.bfloat16)
            dq_scr[...] += _nn(ds, k)
            start = pl.multiple_of((b - off) * BLOCK, BLOCK)
            gref[pl.ds(start, BLOCK), 0:HEAD_SIZE] += _tn(ds, qs)
            gref[pl.ds(start, BLOCK), HEAD_SIZE:2 * HEAD_SIZE] += _tn(p.astype(jnp.bfloat16), dos)
            return 0

        ds = (p * (_nt(dos, v_d) - delta)).astype(jnp.bfloat16)
        dq_scr[...] = _nn(ds, k_d)
        r0 = pl.multiple_of(u * BLOCK, BLOCK)
        own_ref[pl.ds(r0, BLOCK), 0:HEAD_SIZE] += _tn(ds, qs)
        own_ref[pl.ds(r0, BLOCK), HEAD_SIZE:2 * HEAD_SIZE] += _tn(p.astype(jnp.bfloat16), dos)
        for ref, col0, gref, start, stop, off in segments:
            lax.fori_loop(start, stop, functools.partial(pass3, ref=ref, col0=col0, gref=gref, off=off), 0)
        dq = (dq_scr[...] * scale).astype(jnp.bfloat16)
        for h in range(heads):
            att_ref[:, h * HEAD_SIZE:(h + 1) * HEAD_SIZE] = att[h * BLOCK:(h + 1) * BLOCK]
            dq_ref[:, h * HEAD_SIZE:(h + 1) * HEAD_SIZE] = dq[h * BLOCK:(h + 1) * BLOCK]

    if with_prior:
        @pl.when(step == steps - 1)
        def _():
            prior_out[:, 0:HEAD_SIZE] = (prior_ref[:, 0:HEAD_SIZE] * scale).astype(prior_out.dtype)
            prior_out[:, HEAD_SIZE:] = prior_ref[:, HEAD_SIZE:].astype(prior_out.dtype)


def attention_call(lo, packed, kv, earlier, grad, unit_list, out_alias=None, *, heads, kv_block=0,
                   interpret=False):
    ctx_rows = packed.shape[0]
    units = ctx_rows // BLOCK
    q_cols = heads * HEAD_SIZE
    kv_cols = 2 * HEAD_SIZE
    with_prior = earlier is not None
    aliased = 0 if out_alias is None else 2
    first_unit = unit_list[0]
    steps = len(unit_list)
    kernel = functools.partial(attention_kernel, first_unit=first_unit, units=units, heads=heads,
                               with_prior=with_prior, aliased=aliased, steps=steps)
    rows = heads * BLOCK

    def whole(x):
        return pl.BlockSpec(x.shape, lambda i: (0,) * len(x.shape))

    operands = [lo, packed, kv] + ([earlier] if with_prior else []) + [grad]
    unit_block = pl.BlockSpec((BLOCK, q_cols), lambda i: (first_unit + i, 0))
    in_specs = [pl.BlockSpec(memory_space=pltpu.SMEM), unit_block]
    kv_spec = pl.BlockSpec((ctx_rows, kv_cols), lambda i: (0, kv_block))
    in_specs += [kv_spec] + [whole(x) for x in operands[3:-1]] + [unit_block]
    if out_alias is not None:
        operands += list(out_alias)
        in_specs += [pl.BlockSpec(memory_space=pl.ANY)] * 2
    out_shape = [jax.ShapeDtypeStruct((ctx_rows, q_cols), jnp.bfloat16)] * 2
    out_specs = [unit_block] * 2
    if with_prior:
        out_shape.append(jax.ShapeDtypeStruct(earlier.shape, jnp.bfloat16))
        out_specs.append(pl.BlockSpec(earlier.shape, lambda i: (0, 0)))
    out_shape.append(jax.ShapeDtypeStruct((ctx_rows, kv_cols), jnp.float32))
    out_specs.append(pl.BlockSpec((ctx_rows, kv_cols), lambda i: (0, 0)))
    visible_blocks = 4 * len(unit_list)
    flops = 12 * rows * BLOCK * HEAD_SIZE * visible_blocks
    aliases = {} if out_alias is None else {len(operands) - 2: 0, len(operands) - 1: 1}
    return pl.pallas_call(
        kernel,
        grid=(steps,),
        out_shape=tuple(out_shape),
        in_specs=in_specs,
        out_specs=tuple(out_specs),
        scratch_shapes=[
            pltpu.VMEM((units, rows, BLOCK), jnp.float32),
            pltpu.VMEM((rows, HEAD_SIZE), jnp.float32),
            pltpu.VMEM((rows, HEAD_SIZE), jnp.float32),
        ] + ([pltpu.VMEM(earlier.shape, jnp.float32)] if with_prior else []),
        input_output_aliases=aliases,
        compiler_params=pltpu.CompilerParams(
            dimension_semantics=("arbitrary",), vmem_limit_bytes=48 * 1024 * 1024),
        cost_estimate=pl.CostEstimate(flops=flops, transcendentals=2 * rows * BLOCK * visible_blocks,
                                      bytes_accessed=6 * 1024 * 1024),
        interpret=interpret,
    )(*operands)


def local(query_matrix, key_matrix, value_matrix, output_gradient, doc_start):
    token_per_shard = query_matrix.shape[0]
    head_groups = lax.axis_size("head")
    q_cols = query_matrix.shape[1] // head_groups
    k_cols = key_matrix.shape[1] // head_groups
    assert k_cols == HEAD_SIZE and 2 * token_per_shard == BLOCK
    packed = jnp.concatenate(
        [
            query_matrix.reshape(token_per_shard, head_groups, q_cols),
            key_matrix.reshape(token_per_shard, head_groups, k_cols),
            value_matrix.reshape(token_per_shard, head_groups, k_cols),
        ],
        axis=2,
    )
    packed = lax.all_to_all(packed, "head", split_axis=1, concat_axis=0, tiled=True)
    ctx_rows = packed.shape[0]
    packed = packed.reshape(ctx_rows, q_cols + 2 * k_cols)
    earlier_kv = from_behind(packed[BLOCK:, q_cols:], "ctx", 1)
    units = ctx_rows // BLOCK
    ctx_index = lax.axis_index("ctx")
    wanted = (ctx_index - 1) * units + jnp.arange(2 * units, dtype=jnp.int32)
    unit_at = jnp.arange(doc_start.shape[0], dtype=jnp.int32)
    joined_units = jnp.sum(jnp.where(unit_at[None, :] <= wanted[:, None], doc_start[None, :], 0), axis=1)
    joined_units = jnp.where(wanted >= 0, joined_units, -1)
    own_units = joined_units[units:]
    unit_ids = jnp.arange(units, dtype=jnp.int32)
    window = unit_ids[:, None] + 1 + unit_ids[None, :]
    same = (joined_units[window] == own_units[:, None]).astype(jnp.int32)
    lo = (unit_ids + units + 1 - jnp.sum(same, axis=1)).astype(jnp.int32)
    heads = q_cols // HEAD_SIZE
    kv_block = q_cols // (2 * k_cols)
    attended_all, query_total, own_last = attention_call(
        lo, packed, packed, None, output_gradient, [units - 1],
        heads=heads, kv_block=kv_block, interpret=INTERPRET)
    attended_all, query_total, prior_grads, own_first = attention_call(
        lo, packed, packed, earlier_kv, output_gradient, range(units - 1), (attended_all, query_total),
        heads=heads, kv_block=kv_block, interpret=INTERPRET)
    own_grads = own_first + own_last
    score_scale = HEAD_SIZE ** (-0.5)
    later = from_behind(prior_grads, "ctx", -1).astype(jnp.float32)
    later = jnp.concatenate([jnp.zeros((BLOCK, 2 * k_cols), jnp.float32), later], axis=0)
    summed_keys = (own_grads[:, :k_cols] * score_scale + later[:, :k_cols]).astype(jnp.bfloat16)
    summed_values = (own_grads[:, k_cols:] + later[:, k_cols:]).astype(jnp.bfloat16)
    return (attended_all, query_total, summed_keys, summed_values)


def solution(mesh):
    placed = (
        P(("ctx", "head"), None),
        P(("ctx", "head"), None),
        P(("ctx", "head"), None),
        P("ctx", "head"),
        P(),
    )
    return jax.shard_map(
        local,
        mesh=mesh,
        in_specs=placed,
        out_specs=(P("ctx", "head"), P("ctx", "head"), P("ctx", "head"), P("ctx", "head")),
        check_vma=False,
    )
```

```python
import jax
import jax.numpy as jnp
from jax import lax
from jax.sharding import PartitionSpec as P
import functools
from jax.experimental import pallas as pl
from jax.experimental.pallas import tpu as pltpu

QUERY_HEADS = 32
KEY_VALUE_HEADS = 8
HEAD_SIZE = 128
BLOCK = 256
INTERPRET = False


def from_behind(block, axis, distance):
    devices = range(lax.axis_size(axis))
    route = [(i - distance, i) for i in devices if i - distance in devices]
    return lax.ppermute(block, axis, route)


def _nt(a, b):
    return lax.dot_general(a, b, (((1,), (1,)), ((), ())), preferred_element_type=jnp.float32)


def _tn(a, b):
    return lax.dot_general(a, b, (((0,), (0,)), ((), ())), preferred_element_type=jnp.float32)


def _nn(a, b):
    return lax.dot_general(a, b, (((1,), (0,)), ((), ())), preferred_element_type=jnp.float32)


def attention_kernel(*refs, first_unit, units, heads, with_prior, aliased, steps, own_in):
    refs = list(refs)
    lo_ref, q_ref, kv_ref = refs[:3]
    refs = refs[3:]
    earlier_ref = refs.pop(0) if with_prior else None
    grad_ref = refs.pop(0)
    refs = refs[aliased:]
    own_init = refs.pop(0) if own_in else None
    att_ref, dq_ref = refs[:2]
    refs = refs[2:]
    prior_out = refs.pop(0) if with_prior else None
    own_ref, s_scr, att_scr, dq_scr = refs[:4]
    prior_ref = refs[4] if with_prior else None
    scale = HEAD_SIZE ** (-0.5)
    step = pl.program_id(0)

    @pl.when(step == 0)
    def _():
        if with_prior:
            prior_ref[...] = jnp.zeros(prior_ref.shape, prior_ref.dtype)
        if own_in:
            own_ref[...] = own_init[...]
        else:
            own_ref[...] = jnp.zeros(own_ref.shape, own_ref.dtype)

    rows = heads * BLOCK
    causal = (lax.broadcasted_iota(jnp.int32, (rows, BLOCK), 0) % BLOCK
              >= lax.broadcasted_iota(jnp.int32, (rows, BLOCK), 1))

    def load_kv(ref, col0, blk):
        start = pl.multiple_of(blk * BLOCK, BLOCK)
        return (ref[pl.ds(start, BLOCK), col0:col0 + HEAD_SIZE],
                ref[pl.ds(start, BLOCK), col0 + HEAD_SIZE:col0 + 2 * HEAD_SIZE])

    if True:
        u = first_unit + step
        qs = jnp.concatenate(
            [q_ref[:, h * HEAD_SIZE:(h + 1) * HEAD_SIZE] for h in range(heads)], axis=0)
        dos = jnp.concatenate(
            [grad_ref[:, h * HEAD_SIZE:(h + 1) * HEAD_SIZE] for h in range(heads)], axis=0)
        lo = lo_ref[u]
        diag = units + u
        first_own = jnp.maximum(lo, units)
        segments = ((kv_ref, 0, own_ref, first_own, diag, units),)
        if with_prior:
            segments = ((earlier_ref, 0, prior_ref, lo, units, 1),) + segments

        half = BLOCK // 2

        def pass1(b, m, ref, col0, off):
            k, _ = load_kv(ref, col0, b - off)
            s = _nt(qs, k) * scale
            s_scr[b - (u + 1)] = s
            return jnp.maximum(m, jnp.maximum(s[:, :half], s[:, half:]))

        k_d, v_d = load_kv(kv_ref, 0, u)
        s = jnp.where(causal, _nt(qs, k_d) * scale, -jnp.inf)
        m = jnp.maximum(s[:, :half], s[:, half:])
        for ref, col0, _, start, stop, off in segments:
            m = lax.fori_loop(start, stop, functools.partial(pass1, ref=ref, col0=col0, off=off), m)
        m = jnp.max(m, axis=1, keepdims=True)

        def pass1b(b, l):
            e = jnp.exp(s_scr[b - (u + 1)] - m)
            s_scr[b - (u + 1)] = e
            return l + e[:, :half] + e[:, half:]

        e = jnp.exp(s - m)
        l = lax.fori_loop(lo, diag, pass1b, e[:, :half] + e[:, half:])
        inv_total = 1.0 / jnp.sum(l, axis=1, keepdims=True)

        def pass2(b, _, ref, col0, off):
            _, v = load_kv(ref, col0, b - off)
            p = s_scr[b - (u + 1)] * inv_total
            s_scr[b - (u + 1)] = p
            att_scr[...] += _nn(p.astype(jnp.bfloat16), v)
            return 0

        p = e * inv_total
        att_scr[...] = _nn(p.astype(jnp.bfloat16), v_d)
        for ref, col0, _, start, stop, off in segments:
            lax.fori_loop(start, stop, functools.partial(pass2, ref=ref, col0=col0, off=off), 0)
        att = att_scr[...].astype(jnp.bfloat16)
        delta = jnp.sum(dos.astype(jnp.float32) * att.astype(jnp.float32), axis=1, keepdims=True)

        def pass3(b, _, ref, col0, gref, off):
            k, v = load_kv(ref, col0, b - off)
            p = s_scr[b - (u + 1)]
            ds = (p * (_nt(dos, v) - delta)).astype(jnp.bfloat16)
            dq_scr[...] += _nn(ds, k)
            start = pl.multiple_of((b - off) * BLOCK, BLOCK)
            gref[pl.ds(start, BLOCK), 0:HEAD_SIZE] += _tn(ds, qs)
            gref[pl.ds(start, BLOCK), HEAD_SIZE:2 * HEAD_SIZE] += _tn(p.astype(jnp.bfloat16), dos)
            return 0

        ds = (p * (_nt(dos, v_d) - delta)).astype(jnp.bfloat16)
        dq_scr[...] = _nn(ds, k_d)
        r0 = pl.multiple_of(u * BLOCK, BLOCK)
        own_ref[pl.ds(r0, BLOCK), 0:HEAD_SIZE] += _tn(ds, qs)
        own_ref[pl.ds(r0, BLOCK), HEAD_SIZE:2 * HEAD_SIZE] += _tn(p.astype(jnp.bfloat16), dos)
        for ref, col0, gref, start, stop, off in segments:
            lax.fori_loop(start, stop, functools.partial(pass3, ref=ref, col0=col0, gref=gref, off=off), 0)
        dq = (dq_scr[...] * scale).astype(jnp.bfloat16)
        for h in range(heads):
            att_ref[:, h * HEAD_SIZE:(h + 1) * HEAD_SIZE] = att[h * BLOCK:(h + 1) * BLOCK]
            dq_ref[:, h * HEAD_SIZE:(h + 1) * HEAD_SIZE] = dq[h * BLOCK:(h + 1) * BLOCK]

    if with_prior:
        @pl.when(step == steps - 1)
        def _():
            prior_out[:, 0:HEAD_SIZE] = (prior_ref[:, 0:HEAD_SIZE] * scale).astype(prior_out.dtype)
            prior_out[:, HEAD_SIZE:] = prior_ref[:, HEAD_SIZE:].astype(prior_out.dtype)


def attention_call(lo, packed, kv, earlier, grad, unit_list, out_alias=None, own=None, *, heads,
                   interpret=False):
    ctx_rows = packed.shape[0]
    units = ctx_rows // BLOCK
    q_cols = heads * HEAD_SIZE
    kv_cols = 2 * HEAD_SIZE
    with_prior = earlier is not None
    aliased = 0 if out_alias is None else 2
    first_unit = unit_list[0]
    steps = len(unit_list)
    kernel = functools.partial(attention_kernel, first_unit=first_unit, units=units, heads=heads,
                               with_prior=with_prior, aliased=aliased, steps=steps,
                               own_in=own is not None)
    rows = heads * BLOCK

    def whole(x):
        return pl.BlockSpec(x.shape, lambda i: (0,) * len(x.shape))

    operands = [lo, packed, kv] + ([earlier] if with_prior else []) + [grad]
    unit_block = pl.BlockSpec((BLOCK, q_cols), lambda i: (first_unit + i, 0))
    in_specs = [pl.BlockSpec(memory_space=pltpu.SMEM), unit_block]
    in_specs += [whole(x) for x in operands[2:-1]] + [unit_block]
    if out_alias is not None:
        operands += list(out_alias)
        in_specs += [pl.BlockSpec(memory_space=pl.ANY)] * 2
    out_shape = [jax.ShapeDtypeStruct((ctx_rows, q_cols), jnp.bfloat16)] * 2
    out_specs = [unit_block] * 2
    if with_prior:
        out_shape.append(jax.ShapeDtypeStruct(earlier.shape, jnp.bfloat16))
        out_specs.append(pl.BlockSpec(earlier.shape, lambda i: (0, 0)))
    out_shape.append(jax.ShapeDtypeStruct((ctx_rows, kv_cols), jnp.float32))
    out_specs.append(pl.BlockSpec((ctx_rows, kv_cols), lambda i: (0, 0)))
    visible_blocks = 4 * len(unit_list)
    flops = 12 * rows * BLOCK * HEAD_SIZE * visible_blocks
    aliases = {} if out_alias is None else {len(operands) - 2: 0, len(operands) - 1: 1}
    if own is not None:
        aliases[len(operands)] = len(out_shape) - 1
        operands.append(own)
        in_specs.append(whole(own))
    return pl.pallas_call(
        kernel,
        grid=(steps,),
        out_shape=tuple(out_shape),
        in_specs=in_specs,
        out_specs=tuple(out_specs),
        scratch_shapes=[
            pltpu.VMEM((units, rows, BLOCK), jnp.float32),
            pltpu.VMEM((rows, HEAD_SIZE), jnp.float32),
            pltpu.VMEM((rows, HEAD_SIZE), jnp.float32),
        ] + ([pltpu.VMEM(earlier.shape, jnp.float32)] if with_prior else []),
        input_output_aliases=aliases,
        compiler_params=pltpu.CompilerParams(
            dimension_semantics=("arbitrary",), vmem_limit_bytes=48 * 1024 * 1024),
        cost_estimate=pl.CostEstimate(flops=flops, transcendentals=2 * rows * BLOCK * visible_blocks,
                                      bytes_accessed=6 * 1024 * 1024),
        interpret=interpret,
    )(*operands)


def local(query_matrix, key_matrix, value_matrix, output_gradient, doc_start):
    token_per_shard = query_matrix.shape[0]
    head_groups = lax.axis_size("head")
    q_cols = query_matrix.shape[1] // head_groups
    k_cols = key_matrix.shape[1] // head_groups
    assert k_cols == HEAD_SIZE and 2 * token_per_shard == BLOCK
    kv_packed = jnp.concatenate(
        [
            key_matrix.reshape(token_per_shard, head_groups, k_cols),
            value_matrix.reshape(token_per_shard, head_groups, k_cols),
        ],
        axis=2,
    )
    kv = lax.all_to_all(kv_packed, "head", split_axis=1, concat_axis=0, tiled=True)
    ctx_rows = kv.shape[0]
    kv = kv.reshape(ctx_rows, 2 * k_cols)
    earlier_kv = from_behind(kv[BLOCK:], "ctx", 1)
    packed = lax.all_to_all(
        query_matrix.reshape(token_per_shard, head_groups, q_cols),
        "head", split_axis=1, concat_axis=0, tiled=True,
    ).reshape(ctx_rows, q_cols)
    units = ctx_rows // BLOCK
    ctx_index = lax.axis_index("ctx")
    wanted = (ctx_index - 1) * units + jnp.arange(2 * units, dtype=jnp.int32)
    unit_at = jnp.arange(doc_start.shape[0], dtype=jnp.int32)
    joined_units = jnp.sum(jnp.where(unit_at[None, :] <= wanted[:, None], doc_start[None, :], 0), axis=1)
    joined_units = jnp.where(wanted >= 0, joined_units, -1)
    own_units = joined_units[units:]
    unit_ids = jnp.arange(units, dtype=jnp.int32)
    window = unit_ids[:, None] + 1 + unit_ids[None, :]
    same = (joined_units[window] == own_units[:, None]).astype(jnp.int32)
    lo = (unit_ids + units + 1 - jnp.sum(same, axis=1)).astype(jnp.int32)
    heads = q_cols // HEAD_SIZE
    first = attention_call(lo, packed, kv, earlier_kv, output_gradient, range(units - 1),
                           heads=heads, interpret=INTERPRET)
    attended_all, query_total, prior_grads, own_first = first
    last = attention_call(lo, packed, kv, None, output_gradient, [units - 1],
                          (attended_all, query_total), own_first, heads=heads, interpret=INTERPRET)
    attended_all, query_total, own_grads = last
    score_scale = HEAD_SIZE ** (-0.5)
    later = from_behind(prior_grads, "ctx", -1).astype(jnp.float32)
    later = jnp.concatenate([jnp.zeros((BLOCK, 2 * k_cols), jnp.float32), later], axis=0)
    summed_keys = (own_grads[:, :k_cols] * score_scale + later[:, :k_cols]).astype(jnp.bfloat16)
    summed_values = (own_grads[:, k_cols:] + later[:, k_cols:]).astype(jnp.bfloat16)
    return (attended_all, query_total, summed_keys, summed_values)


def solution(mesh):
    placed = (
        P(("ctx", "head"), None),
        P(("ctx", "head"), None),
        P(("ctx", "head"), None),
        P("ctx", "head"),
        P(),
    )
    return jax.shard_map(
        local,
        mesh=mesh,
        in_specs=placed,
        out_specs=(P("ctx", "head"), P("ctx", "head"), P("ctx", "head"), P("ctx", "head")),
        check_vma=False,
    )
```

```python
import jax
import jax.numpy as jnp
from jax import lax
from jax.sharding import PartitionSpec as P
import functools
from jax.experimental import pallas as pl
from jax.experimental.pallas import tpu as pltpu

QUERY_HEADS = 32
KEY_VALUE_HEADS = 8
HEAD_SIZE = 128
BLOCK = 256
INTERPRET = False


def from_behind(block, axis, distance):
    devices = range(lax.axis_size(axis))
    route = [(i - distance, i) for i in devices if i - distance in devices]
    return lax.ppermute(block, axis, route)


def _nt(a, b):
    return lax.dot_general(a, b, (((1,), (1,)), ((), ())), preferred_element_type=jnp.float32)


def _tn(a, b):
    return lax.dot_general(a, b, (((0,), (0,)), ((), ())), preferred_element_type=jnp.float32)


def _nn(a, b):
    return lax.dot_general(a, b, (((1,), (0,)), ((), ())), preferred_element_type=jnp.float32)


def attention_kernel(*refs, first_unit, units, heads, with_prior, aliased, steps, own_in):
    refs = list(refs)
    lo_ref, q_ref, kv_ref = refs[:3]
    refs = refs[3:]
    earlier_ref = refs.pop(0) if with_prior else None
    grad_ref = refs.pop(0)
    refs = refs[aliased:]
    own_init = refs.pop(0) if own_in else None
    att_ref, dq_ref = refs[:2]
    refs = refs[2:]
    prior_out = refs.pop(0) if with_prior else None
    own_ref, s_scr, att_scr, dq_scr = refs[:4]
    prior_ref = refs[4] if with_prior else None
    scale = HEAD_SIZE ** (-0.5)
    step = pl.program_id(0)

    @pl.when(step == 0)
    def _():
        if with_prior:
            prior_ref[...] = jnp.zeros(prior_ref.shape, prior_ref.dtype)
        if own_in:
            own_ref[...] = own_init[...]
        else:
            own_ref[...] = jnp.zeros(own_ref.shape, own_ref.dtype)

    rows = heads * BLOCK
    causal = (lax.broadcasted_iota(jnp.int32, (rows, BLOCK), 0) % BLOCK
              >= lax.broadcasted_iota(jnp.int32, (rows, BLOCK), 1))

    def load_kv(ref, col0, blk):
        start = pl.multiple_of(blk * BLOCK, BLOCK)
        return (ref[pl.ds(start, BLOCK), col0:col0 + HEAD_SIZE],
                ref[pl.ds(start, BLOCK), col0 + HEAD_SIZE:col0 + 2 * HEAD_SIZE])

    if True:
        u = first_unit + step
        qs = jnp.concatenate(
            [q_ref[:, h * HEAD_SIZE:(h + 1) * HEAD_SIZE] for h in range(heads)], axis=0)
        dos = jnp.concatenate(
            [grad_ref[:, h * HEAD_SIZE:(h + 1) * HEAD_SIZE] for h in range(heads)], axis=0)
        lo = lo_ref[u]
        diag = units + u
        first_own = jnp.maximum(lo, units)
        segments = ((kv_ref, 0, own_ref, first_own, diag, units),)
        if with_prior:
            segments = ((earlier_ref, 0, prior_ref, lo, units, 1),) + segments

        half = BLOCK // 2

        def pass1(b, m, ref, col0, off):
            k, _ = load_kv(ref, col0, b - off)
            s = _nt(qs, k) * scale
            s_scr[b - (u + 1)] = s
            return jnp.maximum(m, jnp.maximum(s[:, :half], s[:, half:]))

        k_d, v_d = load_kv(kv_ref, 0, u)
        s = jnp.where(causal, _nt(qs, k_d) * scale, -jnp.inf)
        m = jnp.maximum(s[:, :half], s[:, half:])
        for ref, col0, _, start, stop, off in segments:
            m = lax.fori_loop(start, stop, functools.partial(pass1, ref=ref, col0=col0, off=off), m)
        m = jnp.max(m, axis=1, keepdims=True)

        def pass1b(b, l):
            e = jnp.exp(s_scr[b - (u + 1)] - m)
            s_scr[b - (u + 1)] = e
            return l + e[:, :half] + e[:, half:]

        e = jnp.exp(s - m)
        l = lax.fori_loop(lo, diag, pass1b, e[:, :half] + e[:, half:])
        inv_total = 1.0 / jnp.sum(l, axis=1, keepdims=True)

        def pass2(b, _, ref, col0, off):
            _, v = load_kv(ref, col0, b - off)
            p = s_scr[b - (u + 1)] * inv_total
            s_scr[b - (u + 1)] = p
            att_scr[...] += _nn(p.astype(jnp.bfloat16), v)
            return 0

        p = e * inv_total
        att_scr[...] = _nn(p.astype(jnp.bfloat16), v_d)
        for ref, col0, _, start, stop, off in segments:
            lax.fori_loop(start, stop, functools.partial(pass2, ref=ref, col0=col0, off=off), 0)
        att = att_scr[...].astype(jnp.bfloat16)
        delta = jnp.sum(dos.astype(jnp.float32) * att.astype(jnp.float32), axis=1, keepdims=True)

        def pass3(b, _, ref, col0, gref, off):
            k, v = load_kv(ref, col0, b - off)
            p = s_scr[b - (u + 1)]
            ds = (p * (_nt(dos, v) - delta)).astype(jnp.bfloat16)
            dq_scr[...] += _nn(ds, k)
            start = pl.multiple_of((b - off) * BLOCK, BLOCK)
            gref[pl.ds(start, BLOCK), 0:HEAD_SIZE] += _tn(ds, qs)
            gref[pl.ds(start, BLOCK), HEAD_SIZE:2 * HEAD_SIZE] += _tn(p.astype(jnp.bfloat16), dos)
            return 0

        ds = (p * (_nt(dos, v_d) - delta)).astype(jnp.bfloat16)
        dq_scr[...] = _nn(ds, k_d)
        r0 = pl.multiple_of(u * BLOCK, BLOCK)
        own_ref[pl.ds(r0, BLOCK), 0:HEAD_SIZE] += _tn(ds, qs)
        own_ref[pl.ds(r0, BLOCK), HEAD_SIZE:2 * HEAD_SIZE] += _tn(p.astype(jnp.bfloat16), dos)
        for ref, col0, gref, start, stop, off in segments:
            lax.fori_loop(start, stop, functools.partial(pass3, ref=ref, col0=col0, gref=gref, off=off), 0)
        dq = (dq_scr[...] * scale).astype(jnp.bfloat16)
        for h in range(heads):
            att_ref[:, h * HEAD_SIZE:(h + 1) * HEAD_SIZE] = att[h * BLOCK:(h + 1) * BLOCK]
            dq_ref[:, h * HEAD_SIZE:(h + 1) * HEAD_SIZE] = dq[h * BLOCK:(h + 1) * BLOCK]

    if with_prior:
        @pl.when(step == steps - 1)
        def _():
            prior_out[:, 0:HEAD_SIZE] = (prior_ref[:, 0:HEAD_SIZE] * scale).astype(prior_out.dtype)
            prior_out[:, HEAD_SIZE:] = prior_ref[:, HEAD_SIZE:].astype(prior_out.dtype)


def kv_pack_kernel(k_ref, v_ref, o_ref, *, groups, rows):
    for g in range(groups):
        o_ref[g * rows:(g + 1) * rows, 0:HEAD_SIZE] = k_ref[:, g * HEAD_SIZE:(g + 1) * HEAD_SIZE]
        o_ref[g * rows:(g + 1) * rows, HEAD_SIZE:] = v_ref[:, g * HEAD_SIZE:(g + 1) * HEAD_SIZE]


def kv_pack(key_matrix, value_matrix, groups, interpret=False):
    rows = key_matrix.shape[0]
    vmem = pltpu.MemorySpace.VMEM
    return pl.pallas_call(
        functools.partial(kv_pack_kernel, groups=groups, rows=rows),
        out_shape=jax.ShapeDtypeStruct((groups * rows, 2 * HEAD_SIZE), key_matrix.dtype),
        in_specs=[pl.BlockSpec(memory_space=vmem)] * 2,
        out_specs=pl.BlockSpec(memory_space=vmem),
        interpret=interpret,
    )(key_matrix, value_matrix)


def attention_call(lo, packed, kv, earlier, grad, unit_list, out_alias=None, own=None, *, heads,
                   interpret=False):
    ctx_rows = packed.shape[0]
    units = ctx_rows // BLOCK
    q_cols = heads * HEAD_SIZE
    kv_cols = 2 * HEAD_SIZE
    with_prior = earlier is not None
    aliased = 0 if out_alias is None else 2
    first_unit = unit_list[0]
    steps = len(unit_list)
    kernel = functools.partial(attention_kernel, first_unit=first_unit, units=units, heads=heads,
                               with_prior=with_prior, aliased=aliased, steps=steps,
                               own_in=own is not None)
    rows = heads * BLOCK

    def whole(x):
        return pl.BlockSpec(x.shape, lambda i: (0,) * len(x.shape))

    operands = [lo, packed, kv] + ([earlier] if with_prior else []) + [grad]
    unit_block = pl.BlockSpec((BLOCK, q_cols), lambda i: (first_unit + i, 0))
    in_specs = [pl.BlockSpec(memory_space=pltpu.SMEM), unit_block]
    in_specs += [whole(x) for x in operands[2:-1]] + [unit_block]
    if out_alias is not None:
        operands += list(out_alias)
        in_specs += [pl.BlockSpec(memory_space=pl.ANY)] * 2
    out_shape = [jax.ShapeDtypeStruct((ctx_rows, q_cols), jnp.bfloat16)] * 2
    out_specs = [unit_block] * 2
    if with_prior:
        out_shape.append(jax.ShapeDtypeStruct(earlier.shape, jnp.bfloat16))
        out_specs.append(pl.BlockSpec(earlier.shape, lambda i: (0, 0)))
    out_shape.append(jax.ShapeDtypeStruct((ctx_rows, kv_cols), jnp.float32))
    out_specs.append(pl.BlockSpec((ctx_rows, kv_cols), lambda i: (0, 0)))
    visible_blocks = 4 * len(unit_list)
    flops = 12 * rows * BLOCK * HEAD_SIZE * visible_blocks
    aliases = {} if out_alias is None else {len(operands) - 2: 0, len(operands) - 1: 1}
    if own is not None:
        aliases[len(operands)] = len(out_shape) - 1
        operands.append(own)
        in_specs.append(whole(own))
    return pl.pallas_call(
        kernel,
        grid=(steps,),
        out_shape=tuple(out_shape),
        in_specs=in_specs,
        out_specs=tuple(out_specs),
        scratch_shapes=[
            pltpu.VMEM((units, rows, BLOCK), jnp.float32),
            pltpu.VMEM((rows, HEAD_SIZE), jnp.float32),
            pltpu.VMEM((rows, HEAD_SIZE), jnp.float32),
        ] + ([pltpu.VMEM(earlier.shape, jnp.float32)] if with_prior else []),
        input_output_aliases=aliases,
        compiler_params=pltpu.CompilerParams(
            dimension_semantics=("arbitrary",), vmem_limit_bytes=48 * 1024 * 1024),
        cost_estimate=pl.CostEstimate(flops=flops, transcendentals=2 * rows * BLOCK * visible_blocks,
                                      bytes_accessed=6 * 1024 * 1024),
        interpret=interpret,
    )(*operands)


def local(query_matrix, key_matrix, value_matrix, output_gradient, doc_start):
    token_per_shard = query_matrix.shape[0]
    head_groups = lax.axis_size("head")
    q_cols = query_matrix.shape[1] // head_groups
    k_cols = key_matrix.shape[1] // head_groups
    assert k_cols == HEAD_SIZE and 2 * token_per_shard == BLOCK
    kv_packed = kv_pack(key_matrix, value_matrix, head_groups, interpret=INTERPRET)
    kv = lax.all_to_all(kv_packed, "head", split_axis=0, concat_axis=0, tiled=True)
    ctx_rows = kv.shape[0]
    earlier_kv = from_behind(kv[BLOCK:], "ctx", 1)
    packed = lax.all_to_all(
        query_matrix.reshape(token_per_shard, head_groups, q_cols),
        "head", split_axis=1, concat_axis=0, tiled=True,
    ).reshape(ctx_rows, q_cols)
    units = ctx_rows // BLOCK
    ctx_index = lax.axis_index("ctx")
    wanted = (ctx_index - 1) * units + jnp.arange(2 * units, dtype=jnp.int32)
    unit_at = jnp.arange(doc_start.shape[0], dtype=jnp.int32)
    joined_units = jnp.sum(jnp.where(unit_at[None, :] <= wanted[:, None], doc_start[None, :], 0), axis=1)
    joined_units = jnp.where(wanted >= 0, joined_units, -1)
    own_units = joined_units[units:]
    unit_ids = jnp.arange(units, dtype=jnp.int32)
    window = unit_ids[:, None] + 1 + unit_ids[None, :]
    same = (joined_units[window] == own_units[:, None]).astype(jnp.int32)
    lo = (unit_ids + units + 1 - jnp.sum(same, axis=1)).astype(jnp.int32)
    heads = q_cols // HEAD_SIZE
    first = attention_call(lo, packed, kv, earlier_kv, output_gradient, range(units - 1),
                           heads=heads, interpret=INTERPRET)
    attended_all, query_total, prior_grads, own_first = first
    last = attention_call(lo, packed, kv, None, output_gradient, [units - 1],
                          (attended_all, query_total), own_first, heads=heads, interpret=INTERPRET)
    attended_all, query_total, own_grads = last
    score_scale = HEAD_SIZE ** (-0.5)
    later = from_behind(prior_grads, "ctx", -1).astype(jnp.float32)
    later = jnp.concatenate([jnp.zeros((BLOCK, 2 * k_cols), jnp.float32), later], axis=0)
    summed_keys = (own_grads[:, :k_cols] * score_scale + later[:, :k_cols]).astype(jnp.bfloat16)
    summed_values = (own_grads[:, k_cols:] + later[:, k_cols:]).astype(jnp.bfloat16)
    return (attended_all, query_total, summed_keys, summed_values)


def solution(mesh):
    placed = (
        P(("ctx", "head"), None),
        P(("ctx", "head"), None),
        P(("ctx", "head"), None),
        P("ctx", "head"),
        P(),
    )
    return jax.shard_map(
        local,
        mesh=mesh,
        in_specs=placed,
        out_specs=(P("ctx", "head"), P("ctx", "head"), P("ctx", "head"), P("ctx", "head")),
        check_vma=False,
    )
```

```python
import jax
import jax.numpy as jnp
from jax import lax
from jax.sharding import PartitionSpec as P
import functools
from jax.experimental import pallas as pl
from jax.experimental.pallas import tpu as pltpu

QUERY_HEADS = 32
KEY_VALUE_HEADS = 8
HEAD_SIZE = 128
BLOCK = 256
INTERPRET = False


def from_behind(block, axis, distance):
    devices = range(lax.axis_size(axis))
    route = [(i - distance, i) for i in devices if i - distance in devices]
    return lax.ppermute(block, axis, route)


def _nt(a, b):
    return lax.dot_general(a, b, (((1,), (1,)), ((), ())), preferred_element_type=jnp.float32)


def _tn(a, b):
    return lax.dot_general(a, b, (((0,), (0,)), ((), ())), preferred_element_type=jnp.float32)


def _nn(a, b):
    return lax.dot_general(a, b, (((1,), (0,)), ((), ())), preferred_element_type=jnp.float32)


def attention_kernel(*refs, first_unit, units, heads, with_prior, aliased, steps, own_in):
    refs = list(refs)
    lo_ref, q_ref, kv_ref = refs[:3]
    refs = refs[3:]
    earlier_ref = refs.pop(0) if with_prior else None
    grad_ref = refs.pop(0)
    refs = refs[aliased:]
    own_init = refs.pop(0) if own_in else None
    att_ref, dq_ref = refs[:2]
    refs = refs[2:]
    prior_out = refs.pop(0) if with_prior else None
    own_ref, s_scr, att_scr, dq_scr = refs[:4]
    prior_ref = refs[4] if with_prior else None
    scale = HEAD_SIZE ** (-0.5)
    step = pl.program_id(0)

    @pl.when(step == 0)
    def _():
        if with_prior:
            prior_ref[...] = jnp.zeros(prior_ref.shape, prior_ref.dtype)
        if own_in:
            own_ref[...] = own_init[...]
        else:
            own_ref[...] = jnp.zeros(own_ref.shape, own_ref.dtype)

    rows = heads * BLOCK
    causal = (lax.broadcasted_iota(jnp.int32, (rows, BLOCK), 0) % BLOCK
              >= lax.broadcasted_iota(jnp.int32, (rows, BLOCK), 1))

    def load_kv(ref, col0, blk):
        start = pl.multiple_of(blk * BLOCK, BLOCK)
        return (ref[pl.ds(start, BLOCK), col0:col0 + HEAD_SIZE],
                ref[pl.ds(start, BLOCK), col0 + HEAD_SIZE:col0 + 2 * HEAD_SIZE])

    if True:
        u = first_unit + step
        qs = jnp.concatenate(
            [q_ref[:, h * HEAD_SIZE:(h + 1) * HEAD_SIZE] for h in range(heads)], axis=0)
        dos = jnp.concatenate(
            [grad_ref[:, h * HEAD_SIZE:(h + 1) * HEAD_SIZE] for h in range(heads)], axis=0)
        lo = lo_ref[u]
        diag = units + u
        first_own = jnp.maximum(lo, units)
        segments = ((kv_ref, 0, own_ref, first_own, diag, units),)
        if with_prior:
            segments = ((earlier_ref, 0, prior_ref, lo, units, 1),) + segments

        half = BLOCK // 2

        def pass1(b, m, ref, col0, off):
            k, _ = load_kv(ref, col0, b - off)
            s = _nt(qs, k) * scale
            s_scr[b - (u + 1)] = s
            return jnp.maximum(m, jnp.maximum(s[:, :half], s[:, half:]))

        k_d, v_d = load_kv(kv_ref, 0, u)
        s = jnp.where(causal, _nt(qs, k_d) * scale, -jnp.inf)
        m = jnp.maximum(s[:, :half], s[:, half:])
        for ref, col0, _, start, stop, off in segments:
            m = lax.fori_loop(start, stop, functools.partial(pass1, ref=ref, col0=col0, off=off), m)
        m = jnp.max(m, axis=1, keepdims=True)

        def pass1b(b, l):
            e = jnp.exp(s_scr[b - (u + 1)] - m)
            s_scr[b - (u + 1)] = e
            return l + e[:, :half] + e[:, half:]

        e = jnp.exp(s - m)
        l = lax.fori_loop(lo, diag, pass1b, e[:, :half] + e[:, half:])
        inv_total = 1.0 / jnp.sum(l, axis=1, keepdims=True)

        def pass2(b, _, ref, col0, off):
            _, v = load_kv(ref, col0, b - off)
            p = s_scr[b - (u + 1)] * inv_total
            s_scr[b - (u + 1)] = p
            att_scr[...] += _nn(p.astype(jnp.bfloat16), v)
            return 0

        p = e * inv_total
        att_scr[...] = _nn(p.astype(jnp.bfloat16), v_d)
        for ref, col0, _, start, stop, off in segments:
            lax.fori_loop(start, stop, functools.partial(pass2, ref=ref, col0=col0, off=off), 0)
        att = att_scr[...].astype(jnp.bfloat16)
        delta = jnp.sum(dos.astype(jnp.float32) * att.astype(jnp.float32), axis=1, keepdims=True)

        def pass3(b, _, ref, col0, gref, off):
            k, v = load_kv(ref, col0, b - off)
            p = s_scr[b - (u + 1)]
            ds = (p * (_nt(dos, v) - delta)).astype(jnp.bfloat16)
            dq_scr[...] += _nn(ds, k)
            start = pl.multiple_of((b - off) * BLOCK, BLOCK)
            gref[pl.ds(start, BLOCK), 0:HEAD_SIZE] += _tn(ds, qs)
            gref[pl.ds(start, BLOCK), HEAD_SIZE:2 * HEAD_SIZE] += _tn(p.astype(jnp.bfloat16), dos)
            return 0

        ds = (p * (_nt(dos, v_d) - delta)).astype(jnp.bfloat16)
        dq_scr[...] = _nn(ds, k_d)
        r0 = pl.multiple_of(u * BLOCK, BLOCK)
        own_ref[pl.ds(r0, BLOCK), 0:HEAD_SIZE] += _tn(ds, qs)
        own_ref[pl.ds(r0, BLOCK), HEAD_SIZE:2 * HEAD_SIZE] += _tn(p.astype(jnp.bfloat16), dos)
        for ref, col0, gref, start, stop, off in segments:
            lax.fori_loop(start, stop, functools.partial(pass3, ref=ref, col0=col0, gref=gref, off=off), 0)
        dq = (dq_scr[...] * scale).astype(jnp.bfloat16)
        for h in range(heads):
            att_ref[:, h * HEAD_SIZE:(h + 1) * HEAD_SIZE] = att[h * BLOCK:(h + 1) * BLOCK]
            dq_ref[:, h * HEAD_SIZE:(h + 1) * HEAD_SIZE] = dq[h * BLOCK:(h + 1) * BLOCK]

    if with_prior:
        @pl.when(step == steps - 1)
        def _():
            prior_out[:, 0:HEAD_SIZE] = (prior_ref[:, 0:HEAD_SIZE] * scale).astype(prior_out.dtype)
            prior_out[:, HEAD_SIZE:] = prior_ref[:, HEAD_SIZE:].astype(prior_out.dtype)


def kv_pack_kernel(k_hbm, v_hbm, o_hbm, sems, *, groups, rows):
    copies = []
    for g in range(groups):
        for i, source in enumerate((k_hbm, v_hbm)):
            copy = pltpu.make_async_copy(
                source.at[:, pl.ds(g * HEAD_SIZE, HEAD_SIZE)],
                o_hbm.at[pl.ds(g * rows, rows), pl.ds(i * HEAD_SIZE, HEAD_SIZE)],
                sems.at[2 * g + i],
            )
            copy.start()
            copies.append(copy)
    for copy in copies:
        copy.wait()


def kv_pack(key_matrix, value_matrix, groups, interpret=False):
    rows = key_matrix.shape[0]
    return pl.pallas_call(
        functools.partial(kv_pack_kernel, groups=groups, rows=rows),
        out_shape=jax.ShapeDtypeStruct((groups * rows, 2 * HEAD_SIZE), key_matrix.dtype),
        in_specs=[pl.BlockSpec(memory_space=pl.ANY)] * 2,
        out_specs=pl.BlockSpec(memory_space=pl.ANY),
        scratch_shapes=[pltpu.SemaphoreType.DMA((2 * groups,))],
        interpret=interpret,
    )(key_matrix, value_matrix)


def attention_call(lo, packed, kv, earlier, grad, unit_list, out_alias=None, own=None, *, heads,
                   interpret=False):
    ctx_rows = packed.shape[0]
    units = ctx_rows // BLOCK
    q_cols = heads * HEAD_SIZE
    kv_cols = 2 * HEAD_SIZE
    with_prior = earlier is not None
    aliased = 0 if out_alias is None else 2
    first_unit = unit_list[0]
    steps = len(unit_list)
    kernel = functools.partial(attention_kernel, first_unit=first_unit, units=units, heads=heads,
                               with_prior=with_prior, aliased=aliased, steps=steps,
                               own_in=own is not None)
    rows = heads * BLOCK

    def whole(x):
        return pl.BlockSpec(x.shape, lambda i: (0,) * len(x.shape))

    operands = [lo, packed, kv] + ([earlier] if with_prior else []) + [grad]
    unit_block = pl.BlockSpec((BLOCK, q_cols), lambda i: (first_unit + i, 0))
    in_specs = [pl.BlockSpec(memory_space=pltpu.SMEM), unit_block]
    in_specs += [whole(x) for x in operands[2:-1]] + [unit_block]
    if out_alias is not None:
        operands += list(out_alias)
        in_specs += [pl.BlockSpec(memory_space=pl.ANY)] * 2
    out_shape = [jax.ShapeDtypeStruct((ctx_rows, q_cols), jnp.bfloat16)] * 2
    out_specs = [unit_block] * 2
    if with_prior:
        out_shape.append(jax.ShapeDtypeStruct(earlier.shape, jnp.bfloat16))
        out_specs.append(pl.BlockSpec(earlier.shape, lambda i: (0, 0)))
    out_shape.append(jax.ShapeDtypeStruct((ctx_rows, kv_cols), jnp.float32))
    out_specs.append(pl.BlockSpec((ctx_rows, kv_cols), lambda i: (0, 0)))
    visible_blocks = 4 * len(unit_list)
    flops = 12 * rows * BLOCK * HEAD_SIZE * visible_blocks
    aliases = {} if out_alias is None else {len(operands) - 2: 0, len(operands) - 1: 1}
    if own is not None:
        aliases[len(operands)] = len(out_shape) - 1
        operands.append(own)
        in_specs.append(whole(own))
    return pl.pallas_call(
        kernel,
        grid=(steps,),
        out_shape=tuple(out_shape),
        in_specs=in_specs,
        out_specs=tuple(out_specs),
        scratch_shapes=[
            pltpu.VMEM((units, rows, BLOCK), jnp.float32),
            pltpu.VMEM((rows, HEAD_SIZE), jnp.float32),
            pltpu.VMEM((rows, HEAD_SIZE), jnp.float32),
        ] + ([pltpu.VMEM(earlier.shape, jnp.float32)] if with_prior else []),
        input_output_aliases=aliases,
        compiler_params=pltpu.CompilerParams(
            dimension_semantics=("arbitrary",), vmem_limit_bytes=48 * 1024 * 1024),
        cost_estimate=pl.CostEstimate(flops=flops, transcendentals=2 * rows * BLOCK * visible_blocks,
                                      bytes_accessed=6 * 1024 * 1024),
        interpret=interpret,
    )(*operands)


def local(query_matrix, key_matrix, value_matrix, output_gradient, doc_start):
    token_per_shard = query_matrix.shape[0]
    head_groups = lax.axis_size("head")
    q_cols = query_matrix.shape[1] // head_groups
    k_cols = key_matrix.shape[1] // head_groups
    assert k_cols == HEAD_SIZE and 2 * token_per_shard == BLOCK
    kv_packed = kv_pack(key_matrix, value_matrix, head_groups, interpret=INTERPRET)
    kv = lax.all_to_all(kv_packed, "head", split_axis=0, concat_axis=0, tiled=True)
    ctx_rows = kv.shape[0]
    earlier_kv = from_behind(kv[BLOCK:], "ctx", 1)
    packed = lax.all_to_all(
        query_matrix.reshape(token_per_shard, head_groups, q_cols),
        "head", split_axis=1, concat_axis=0, tiled=True,
    ).reshape(ctx_rows, q_cols)
    units = ctx_rows // BLOCK
    ctx_index = lax.axis_index("ctx")
    wanted = (ctx_index - 1) * units + jnp.arange(2 * units, dtype=jnp.int32)
    unit_at = jnp.arange(doc_start.shape[0], dtype=jnp.int32)
    joined_units = jnp.sum(jnp.where(unit_at[None, :] <= wanted[:, None], doc_start[None, :], 0), axis=1)
    joined_units = jnp.where(wanted >= 0, joined_units, -1)
    own_units = joined_units[units:]
    unit_ids = jnp.arange(units, dtype=jnp.int32)
    window = unit_ids[:, None] + 1 + unit_ids[None, :]
    same = (joined_units[window] == own_units[:, None]).astype(jnp.int32)
    lo = (unit_ids + units + 1 - jnp.sum(same, axis=1)).astype(jnp.int32)
    heads = q_cols // HEAD_SIZE
    first = attention_call(lo, packed, kv, earlier_kv, output_gradient, range(units - 1),
                           heads=heads, interpret=INTERPRET)
    attended_all, query_total, prior_grads, own_first = first
    last = attention_call(lo, packed, kv, None, output_gradient, [units - 1],
                          (attended_all, query_total), own_first, heads=heads, interpret=INTERPRET)
    attended_all, query_total, own_grads = last
    score_scale = HEAD_SIZE ** (-0.5)
    later = from_behind(prior_grads, "ctx", -1).astype(jnp.float32)
    later = jnp.concatenate([jnp.zeros((BLOCK, 2 * k_cols), jnp.float32), later], axis=0)
    summed_keys = (own_grads[:, :k_cols] * score_scale + later[:, :k_cols]).astype(jnp.bfloat16)
    summed_values = (own_grads[:, k_cols:] + later[:, k_cols:]).astype(jnp.bfloat16)
    return (attended_all, query_total, summed_keys, summed_values)


def solution(mesh):
    placed = (
        P(("ctx", "head"), None),
        P(("ctx", "head"), None),
        P(("ctx", "head"), None),
        P("ctx", "head"),
        P(),
    )
    return jax.shard_map(
        local,
        mesh=mesh,
        in_specs=placed,
        out_specs=(P("ctx", "head"), P("ctx", "head"), P("ctx", "head"), P("ctx", "head")),
        check_vma=False,
    )
```

```python
import jax
import jax.numpy as jnp
from jax import lax
from jax.sharding import PartitionSpec as P
import functools
from jax.experimental import pallas as pl
from jax.experimental.pallas import tpu as pltpu

QUERY_HEADS = 32
KEY_VALUE_HEADS = 8
HEAD_SIZE = 128
BLOCK = 256
INTERPRET = False


def from_behind(block, axis, distance):
    devices = range(lax.axis_size(axis))
    route = [(i - distance, i) for i in devices if i - distance in devices]
    return lax.ppermute(block, axis, route)


def _nt(a, b):
    return lax.dot_general(a, b, (((1,), (1,)), ((), ())), preferred_element_type=jnp.float32)


def _tn(a, b):
    return lax.dot_general(a, b, (((0,), (0,)), ((), ())), preferred_element_type=jnp.float32)


def _nn(a, b):
    return lax.dot_general(a, b, (((1,), (0,)), ((), ())), preferred_element_type=jnp.float32)


def attention_kernel(*refs, first_unit, units, heads, with_prior, aliased, steps, own_in):
    refs = list(refs)
    lo_ref, q_ref, kv_ref = refs[:3]
    refs = refs[3:]
    earlier_ref = refs.pop(0) if with_prior else None
    grad_ref = refs.pop(0)
    refs = refs[aliased:]
    own_init = refs.pop(0) if own_in else None
    att_ref, dq_ref = refs[:2]
    refs = refs[2:]
    prior_out = refs.pop(0) if with_prior else None
    own_ref, s_scr, att_scr, dq_scr = refs[:4]
    prior_ref = refs[4] if with_prior else None
    scale = HEAD_SIZE ** (-0.5)
    step = pl.program_id(0)

    @pl.when(step == 0)
    def _():
        if with_prior:
            prior_ref[...] = jnp.zeros(prior_ref.shape, prior_ref.dtype)
        if own_in:
            own_ref[...] = own_init[...]
        else:
            own_ref[...] = jnp.zeros(own_ref.shape, own_ref.dtype)

    rows = heads * BLOCK
    causal = (lax.broadcasted_iota(jnp.int32, (rows, BLOCK), 0) % BLOCK
              >= lax.broadcasted_iota(jnp.int32, (rows, BLOCK), 1))

    def load_kv(ref, col0, blk):
        start = pl.multiple_of(blk * BLOCK, BLOCK)
        return (ref[pl.ds(start, BLOCK), col0:col0 + HEAD_SIZE],
                ref[pl.ds(start, BLOCK), col0 + HEAD_SIZE:col0 + 2 * HEAD_SIZE])

    if True:
        u = first_unit + step
        qs = jnp.concatenate(
            [q_ref[:, h * HEAD_SIZE:(h + 1) * HEAD_SIZE] for h in range(heads)], axis=0)
        dos = jnp.concatenate(
            [grad_ref[:, h * HEAD_SIZE:(h + 1) * HEAD_SIZE] for h in range(heads)], axis=0)
        lo = lo_ref[u]
        diag = units + u
        first_own = jnp.maximum(lo, units)
        segments = ((kv_ref, 0, own_ref, first_own, diag, units),)
        if with_prior:
            segments = ((earlier_ref, 0, prior_ref, lo, units, 1),) + segments

        half = BLOCK // 2

        def pass1(b, m, ref, col0, off):
            k, _ = load_kv(ref, col0, b - off)
            s = _nt(qs, k) * scale
            s_scr[b - (u + 1)] = s
            return jnp.maximum(m, jnp.maximum(s[:, :half], s[:, half:]))

        k_d, v_d = load_kv(kv_ref, 0, u)
        s = jnp.where(causal, _nt(qs, k_d) * scale, -jnp.inf)
        m = jnp.maximum(s[:, :half], s[:, half:])
        for ref, col0, _, start, stop, off in segments:
            m = lax.fori_loop(start, stop, functools.partial(pass1, ref=ref, col0=col0, off=off), m)
        m = jnp.max(m, axis=1, keepdims=True)

        def pass1b(b, l):
            e = jnp.exp(s_scr[b - (u + 1)] - m)
            s_scr[b - (u + 1)] = e
            return l + e[:, :half] + e[:, half:]

        e = jnp.exp(s - m)
        l = lax.fori_loop(lo, diag, pass1b, e[:, :half] + e[:, half:])
        inv_total = 1.0 / jnp.sum(l, axis=1, keepdims=True)

        def pass2(b, _, ref, col0, off):
            _, v = load_kv(ref, col0, b - off)
            p = s_scr[b - (u + 1)] * inv_total
            s_scr[b - (u + 1)] = p
            att_scr[...] += _nn(p.astype(jnp.bfloat16), v)
            return 0

        p = e * inv_total
        att_scr[...] = _nn(p.astype(jnp.bfloat16), v_d)
        for ref, col0, _, start, stop, off in segments:
            lax.fori_loop(start, stop, functools.partial(pass2, ref=ref, col0=col0, off=off), 0)
        att = att_scr[...].astype(jnp.bfloat16)
        delta = jnp.sum(dos.astype(jnp.float32) * att.astype(jnp.float32), axis=1, keepdims=True)

        def pass3(b, _, ref, col0, gref, off):
            k, v = load_kv(ref, col0, b - off)
            p = s_scr[b - (u + 1)]
            ds = (p * (_nt(dos, v) - delta)).astype(jnp.bfloat16)
            dq_scr[...] += _nn(ds, k)
            start = pl.multiple_of((b - off) * BLOCK, BLOCK)
            gref[pl.ds(start, BLOCK), 0:HEAD_SIZE] += _tn(ds, qs)
            gref[pl.ds(start, BLOCK), HEAD_SIZE:2 * HEAD_SIZE] += _tn(p.astype(jnp.bfloat16), dos)
            return 0

        ds = (p * (_nt(dos, v_d) - delta)).astype(jnp.bfloat16)
        dq_scr[...] = _nn(ds, k_d)
        r0 = pl.multiple_of(u * BLOCK, BLOCK)
        own_ref[pl.ds(r0, BLOCK), 0:HEAD_SIZE] += _tn(ds, qs)
        own_ref[pl.ds(r0, BLOCK), HEAD_SIZE:2 * HEAD_SIZE] += _tn(p.astype(jnp.bfloat16), dos)
        for ref, col0, gref, start, stop, off in segments:
            lax.fori_loop(start, stop, functools.partial(pass3, ref=ref, col0=col0, gref=gref, off=off), 0)
        dq = (dq_scr[...] * scale).astype(jnp.bfloat16)
        for h in range(heads):
            att_ref[:, h * HEAD_SIZE:(h + 1) * HEAD_SIZE] = att[h * BLOCK:(h + 1) * BLOCK]
            dq_ref[:, h * HEAD_SIZE:(h + 1) * HEAD_SIZE] = dq[h * BLOCK:(h + 1) * BLOCK]

    if with_prior:
        @pl.when(step == steps - 1)
        def _():
            prior_out[:, 0:HEAD_SIZE] = (prior_ref[:, 0:HEAD_SIZE] * scale).astype(prior_out.dtype)
            prior_out[:, HEAD_SIZE:] = prior_ref[:, HEAD_SIZE:].astype(prior_out.dtype)


def kv_pack_kernel(k_ref, v_ref, o_ref):
    o_ref[:, 0:HEAD_SIZE] = k_ref[...]
    o_ref[:, HEAD_SIZE:] = v_ref[...]


def kv_pack(key_matrix, value_matrix, groups, interpret=False):
    rows = key_matrix.shape[0]
    column_block = pl.BlockSpec((rows, HEAD_SIZE), lambda g: (0, g))
    return pl.pallas_call(
        kv_pack_kernel,
        grid=(groups,),
        out_shape=jax.ShapeDtypeStruct((groups * rows, 2 * HEAD_SIZE), key_matrix.dtype),
        in_specs=[column_block, column_block],
        out_specs=pl.BlockSpec((rows, 2 * HEAD_SIZE), lambda g: (g, 0)),
        interpret=interpret,
    )(key_matrix, value_matrix)


def attention_call(lo, packed, kv, earlier, grad, unit_list, out_alias=None, own=None, *, heads,
                   interpret=False):
    ctx_rows = packed.shape[0]
    units = ctx_rows // BLOCK
    q_cols = heads * HEAD_SIZE
    kv_cols = 2 * HEAD_SIZE
    with_prior = earlier is not None
    aliased = 0 if out_alias is None else 2
    first_unit = unit_list[0]
    steps = len(unit_list)
    kernel = functools.partial(attention_kernel, first_unit=first_unit, units=units, heads=heads,
                               with_prior=with_prior, aliased=aliased, steps=steps,
                               own_in=own is not None)
    rows = heads * BLOCK

    def whole(x):
        return pl.BlockSpec(x.shape, lambda i: (0,) * len(x.shape))

    operands = [lo, packed, kv] + ([earlier] if with_prior else []) + [grad]
    unit_block = pl.BlockSpec((BLOCK, q_cols), lambda i: (first_unit + i, 0))
    in_specs = [pl.BlockSpec(memory_space=pltpu.SMEM), unit_block]
    in_specs += [whole(x) for x in operands[2:-1]] + [unit_block]
    if out_alias is not None:
        operands += list(out_alias)
        in_specs += [pl.BlockSpec(memory_space=pl.ANY)] * 2
    out_shape = [jax.ShapeDtypeStruct((ctx_rows, q_cols), jnp.bfloat16)] * 2
    out_specs = [unit_block] * 2
    if with_prior:
        out_shape.append(jax.ShapeDtypeStruct(earlier.shape, jnp.bfloat16))
        out_specs.append(pl.BlockSpec(earlier.shape, lambda i: (0, 0)))
    out_shape.append(jax.ShapeDtypeStruct((ctx_rows, kv_cols), jnp.float32))
    out_specs.append(pl.BlockSpec((ctx_rows, kv_cols), lambda i: (0, 0)))
    visible_blocks = 4 * len(unit_list)
    flops = 12 * rows * BLOCK * HEAD_SIZE * visible_blocks
    aliases = {} if out_alias is None else {len(operands) - 2: 0, len(operands) - 1: 1}
    if own is not None:
        aliases[len(operands)] = len(out_shape) - 1
        operands.append(own)
        in_specs.append(whole(own))
    return pl.pallas_call(
        kernel,
        grid=(steps,),
        out_shape=tuple(out_shape),
        in_specs=in_specs,
        out_specs=tuple(out_specs),
        scratch_shapes=[
            pltpu.VMEM((units, rows, BLOCK), jnp.float32),
            pltpu.VMEM((rows, HEAD_SIZE), jnp.float32),
            pltpu.VMEM((rows, HEAD_SIZE), jnp.float32),
        ] + ([pltpu.VMEM(earlier.shape, jnp.float32)] if with_prior else []),
        input_output_aliases=aliases,
        compiler_params=pltpu.CompilerParams(
            dimension_semantics=("arbitrary",), vmem_limit_bytes=48 * 1024 * 1024),
        cost_estimate=pl.CostEstimate(flops=flops, transcendentals=2 * rows * BLOCK * visible_blocks,
                                      bytes_accessed=6 * 1024 * 1024),
        interpret=interpret,
    )(*operands)


def local(query_matrix, key_matrix, value_matrix, output_gradient, doc_start):
    token_per_shard = query_matrix.shape[0]
    head_groups = lax.axis_size("head")
    q_cols = query_matrix.shape[1] // head_groups
    k_cols = key_matrix.shape[1] // head_groups
    assert k_cols == HEAD_SIZE and 2 * token_per_shard == BLOCK
    kv_packed = kv_pack(key_matrix, value_matrix, head_groups, interpret=INTERPRET)
    kv = lax.all_to_all(kv_packed, "head", split_axis=0, concat_axis=0, tiled=True)
    ctx_rows = kv.shape[0]
    earlier_kv = from_behind(kv[BLOCK:], "ctx", 1)
    packed = lax.all_to_all(
        query_matrix.reshape(token_per_shard, head_groups, q_cols),
        "head", split_axis=1, concat_axis=0, tiled=True,
    ).reshape(ctx_rows, q_cols)
    units = ctx_rows // BLOCK
    ctx_index = lax.axis_index("ctx")
    wanted = (ctx_index - 1) * units + jnp.arange(2 * units, dtype=jnp.int32)
    unit_at = jnp.arange(doc_start.shape[0], dtype=jnp.int32)
    joined_units = jnp.sum(jnp.where(unit_at[None, :] <= wanted[:, None], doc_start[None, :], 0), axis=1)
    joined_units = jnp.where(wanted >= 0, joined_units, -1)
    own_units = joined_units[units:]
    unit_ids = jnp.arange(units, dtype=jnp.int32)
    window = unit_ids[:, None] + 1 + unit_ids[None, :]
    same = (joined_units[window] == own_units[:, None]).astype(jnp.int32)
    lo = (unit_ids + units + 1 - jnp.sum(same, axis=1)).astype(jnp.int32)
    heads = q_cols // HEAD_SIZE
    first = attention_call(lo, packed, kv, earlier_kv, output_gradient, range(units - 1),
                           heads=heads, interpret=INTERPRET)
    attended_all, query_total, prior_grads, own_first = first
    last = attention_call(lo, packed, kv, None, output_gradient, [units - 1],
                          (attended_all, query_total), own_first, heads=heads, interpret=INTERPRET)
    attended_all, query_total, own_grads = last
    score_scale = HEAD_SIZE ** (-0.5)
    later = from_behind(prior_grads, "ctx", -1).astype(jnp.float32)
    later = jnp.concatenate([jnp.zeros((BLOCK, 2 * k_cols), jnp.float32), later], axis=0)
    summed_keys = (own_grads[:, :k_cols] * score_scale + later[:, :k_cols]).astype(jnp.bfloat16)
    summed_values = (own_grads[:, k_cols:] + later[:, k_cols:]).astype(jnp.bfloat16)
    return (attended_all, query_total, summed_keys, summed_values)


def solution(mesh):
    placed = (
        P(("ctx", "head"), None),
        P(("ctx", "head"), None),
        P(("ctx", "head"), None),
        P("ctx", "head"),
        P(),
    )
    return jax.shard_map(
        local,
        mesh=mesh,
        in_specs=placed,
        out_specs=(P("ctx", "head"), P("ctx", "head"), P("ctx", "head"), P("ctx", "head")),
        check_vma=False,
    )
```

```python
import jax
import jax.numpy as jnp
from jax import lax
from jax.sharding import PartitionSpec as P
import functools
from jax.experimental import pallas as pl
from jax.experimental.pallas import tpu as pltpu

QUERY_HEADS = 32
KEY_VALUE_HEADS = 8
HEAD_SIZE = 128
BLOCK = 256
INTERPRET = False


def from_behind(block, axis, distance):
    devices = range(lax.axis_size(axis))
    route = [(i - distance, i) for i in devices if i - distance in devices]
    return lax.ppermute(block, axis, route)


def _nt(a, b):
    return lax.dot_general(a, b, (((1,), (1,)), ((), ())), preferred_element_type=jnp.float32)


def _tn(a, b):
    return lax.dot_general(a, b, (((0,), (0,)), ((), ())), preferred_element_type=jnp.float32)


def _nn(a, b):
    return lax.dot_general(a, b, (((1,), (0,)), ((), ())), preferred_element_type=jnp.float32)


def attention_kernel(*refs, first_unit, units, heads, with_prior, aliased, steps, own_in):
    refs = list(refs)
    lo_ref, q_ref, kv_ref = refs[:3]
    refs = refs[3:]
    earlier_ref = refs.pop(0) if with_prior else None
    grad_ref = refs.pop(0)
    refs = refs[aliased:]
    own_init = refs.pop(0) if own_in else None
    att_ref, dq_ref = refs[:2]
    refs = refs[2:]
    prior_out = refs.pop(0) if with_prior else None
    own_ref, s_scr, att_scr, dq_scr = refs[:4]
    prior_ref = refs[4] if with_prior else None
    scale = HEAD_SIZE ** (-0.5)
    step = pl.program_id(0)

    @pl.when(step == 0)
    def _():
        if with_prior:
            prior_ref[...] = jnp.zeros(prior_ref.shape, prior_ref.dtype)
        if own_in:
            own_ref[...] = own_init[...]
        else:
            own_ref[...] = jnp.zeros(own_ref.shape, own_ref.dtype)

    rows = heads * BLOCK
    causal = (lax.broadcasted_iota(jnp.int32, (rows, BLOCK), 0) % BLOCK
              >= lax.broadcasted_iota(jnp.int32, (rows, BLOCK), 1))

    def load_kv(ref, col0, blk):
        start = pl.multiple_of(blk * BLOCK, BLOCK)
        return (ref[pl.ds(start, BLOCK), col0:col0 + HEAD_SIZE],
                ref[pl.ds(start, BLOCK), col0 + HEAD_SIZE:col0 + 2 * HEAD_SIZE])

    if True:
        u = first_unit + step
        qs = jnp.concatenate(
            [q_ref[:, h * HEAD_SIZE:(h + 1) * HEAD_SIZE] for h in range(heads)], axis=0)
        dos = jnp.concatenate(
            [grad_ref[:, h * HEAD_SIZE:(h + 1) * HEAD_SIZE] for h in range(heads)], axis=0)
        lo = lo_ref[u]
        diag = units + u
        first_own = jnp.maximum(lo, units)
        segments = ((kv_ref, 0, own_ref, first_own, diag, units),)
        if with_prior:
            segments = ((earlier_ref, 0, prior_ref, lo, units, 1),) + segments

        half = BLOCK // 2

        def pass1(b, m, ref, col0, off):
            k, _ = load_kv(ref, col0, b - off)
            s = _nt(qs, k) * scale
            s_scr[b - (u + 1)] = s
            return jnp.maximum(m, jnp.maximum(s[:, :half], s[:, half:]))

        k_d, v_d = load_kv(kv_ref, 0, u)
        s = jnp.where(causal, _nt(qs, k_d) * scale, -jnp.inf)
        m = jnp.maximum(s[:, :half], s[:, half:])
        for ref, col0, _, start, stop, off in segments:
            m = lax.fori_loop(start, stop, functools.partial(pass1, ref=ref, col0=col0, off=off), m)
        m = jnp.max(m, axis=1, keepdims=True)

        def pass1b(b, l):
            e = jnp.exp(s_scr[b - (u + 1)] - m)
            s_scr[b - (u + 1)] = e
            return l + e[:, :half] + e[:, half:]

        e = jnp.exp(s - m)
        l = lax.fori_loop(lo, diag, pass1b, e[:, :half] + e[:, half:])
        inv_total = 1.0 / jnp.sum(l, axis=1, keepdims=True)

        def pass2(b, _, ref, col0, off):
            _, v = load_kv(ref, col0, b - off)
            p = s_scr[b - (u + 1)] * inv_total
            s_scr[b - (u + 1)] = p
            att_scr[...] += _nn(p.astype(jnp.bfloat16), v)
            return 0

        p = e * inv_total
        att_scr[...] = _nn(p.astype(jnp.bfloat16), v_d)
        for ref, col0, _, start, stop, off in segments:
            lax.fori_loop(start, stop, functools.partial(pass2, ref=ref, col0=col0, off=off), 0)
        att = att_scr[...].astype(jnp.bfloat16)
        delta = jnp.sum(dos.astype(jnp.float32) * att.astype(jnp.float32), axis=1, keepdims=True)

        def pass3(b, _, ref, col0, gref, off):
            k, v = load_kv(ref, col0, b - off)
            p = s_scr[b - (u + 1)]
            ds = (p * (_nt(dos, v) - delta)).astype(jnp.bfloat16)
            dq_scr[...] += _nn(ds, k)
            start = pl.multiple_of((b - off) * BLOCK, BLOCK)
            gref[pl.ds(start, BLOCK), 0:HEAD_SIZE] += _tn(ds, qs)
            gref[pl.ds(start, BLOCK), HEAD_SIZE:2 * HEAD_SIZE] += _tn(p.astype(jnp.bfloat16), dos)
            return 0

        ds = (p * (_nt(dos, v_d) - delta)).astype(jnp.bfloat16)
        dq_scr[...] = _nn(ds, k_d)
        r0 = pl.multiple_of(u * BLOCK, BLOCK)
        own_ref[pl.ds(r0, BLOCK), 0:HEAD_SIZE] += _tn(ds, qs)
        own_ref[pl.ds(r0, BLOCK), HEAD_SIZE:2 * HEAD_SIZE] += _tn(p.astype(jnp.bfloat16), dos)
        for ref, col0, gref, start, stop, off in segments:
            lax.fori_loop(start, stop, functools.partial(pass3, ref=ref, col0=col0, gref=gref, off=off), 0)
        dq = (dq_scr[...] * scale).astype(jnp.bfloat16)
        for h in range(heads):
            att_ref[:, h * HEAD_SIZE:(h + 1) * HEAD_SIZE] = att[h * BLOCK:(h + 1) * BLOCK]
            dq_ref[:, h * HEAD_SIZE:(h + 1) * HEAD_SIZE] = dq[h * BLOCK:(h + 1) * BLOCK]

    if with_prior:
        @pl.when(step == steps - 1)
        def _():
            prior_out[:, 0:HEAD_SIZE] = (prior_ref[:, 0:HEAD_SIZE] * scale).astype(prior_out.dtype)
            prior_out[:, HEAD_SIZE:] = prior_ref[:, HEAD_SIZE:].astype(prior_out.dtype)


def kv_pack_kernel(k_ref, v_ref, o_ref, *, groups, rows):
    for g in range(groups):
        o_ref[g * rows:(g + 1) * rows, 0:HEAD_SIZE] = k_ref[:, g * HEAD_SIZE:(g + 1) * HEAD_SIZE]
        o_ref[g * rows:(g + 1) * rows, HEAD_SIZE:] = v_ref[:, g * HEAD_SIZE:(g + 1) * HEAD_SIZE]


def kv_pack(key_matrix, value_matrix, groups, interpret=False):
    rows = key_matrix.shape[0]
    per_step = groups // 2
    column_block = pl.BlockSpec((rows, per_step * HEAD_SIZE), lambda s: (0, s))
    return pl.pallas_call(
        functools.partial(kv_pack_kernel, groups=per_step, rows=rows),
        grid=(groups // per_step,),
        out_shape=jax.ShapeDtypeStruct((groups * rows, 2 * HEAD_SIZE), key_matrix.dtype),
        in_specs=[column_block, column_block],
        out_specs=pl.BlockSpec((per_step * rows, 2 * HEAD_SIZE), lambda s: (s, 0)),
        interpret=interpret,
    )(key_matrix, value_matrix)


def attention_call(lo, packed, kv, earlier, grad, unit_list, out_alias=None, own=None, *, heads,
                   interpret=False):
    ctx_rows = packed.shape[0]
    units = ctx_rows // BLOCK
    q_cols = heads * HEAD_SIZE
    kv_cols = 2 * HEAD_SIZE
    with_prior = earlier is not None
    aliased = 0 if out_alias is None else 2
    first_unit = unit_list[0]
    steps = len(unit_list)
    kernel = functools.partial(attention_kernel, first_unit=first_unit, units=units, heads=heads,
                               with_prior=with_prior, aliased=aliased, steps=steps,
                               own_in=own is not None)
    rows = heads * BLOCK

    def whole(x):
        return pl.BlockSpec(x.shape, lambda i: (0,) * len(x.shape))

    operands = [lo, packed, kv] + ([earlier] if with_prior else []) + [grad]
    unit_block = pl.BlockSpec((BLOCK, q_cols), lambda i: (first_unit + i, 0))
    in_specs = [pl.BlockSpec(memory_space=pltpu.SMEM), unit_block]
    in_specs += [whole(x) for x in operands[2:-1]] + [unit_block]
    if out_alias is not None:
        operands += list(out_alias)
        in_specs += [pl.BlockSpec(memory_space=pl.ANY)] * 2
    out_shape = [jax.ShapeDtypeStruct((ctx_rows, q_cols), jnp.bfloat16)] * 2
    out_specs = [unit_block] * 2
    if with_prior:
        out_shape.append(jax.ShapeDtypeStruct(earlier.shape, jnp.bfloat16))
        out_specs.append(pl.BlockSpec(earlier.shape, lambda i: (0, 0)))
    out_shape.append(jax.ShapeDtypeStruct((ctx_rows, kv_cols), jnp.float32))
    out_specs.append(pl.BlockSpec((ctx_rows, kv_cols), lambda i: (0, 0)))
    visible_blocks = 4 * len(unit_list)
    flops = 12 * rows * BLOCK * HEAD_SIZE * visible_blocks
    aliases = {} if out_alias is None else {len(operands) - 2: 0, len(operands) - 1: 1}
    if own is not None:
        aliases[len(operands)] = len(out_shape) - 1
        operands.append(own)
        in_specs.append(whole(own))
    return pl.pallas_call(
        kernel,
        grid=(steps,),
        out_shape=tuple(out_shape),
        in_specs=in_specs,
        out_specs=tuple(out_specs),
        scratch_shapes=[
            pltpu.VMEM((units, rows, BLOCK), jnp.float32),
            pltpu.VMEM((rows, HEAD_SIZE), jnp.float32),
            pltpu.VMEM((rows, HEAD_SIZE), jnp.float32),
        ] + ([pltpu.VMEM(earlier.shape, jnp.float32)] if with_prior else []),
        input_output_aliases=aliases,
        compiler_params=pltpu.CompilerParams(
            dimension_semantics=("arbitrary",), vmem_limit_bytes=48 * 1024 * 1024),
        cost_estimate=pl.CostEstimate(flops=flops, transcendentals=2 * rows * BLOCK * visible_blocks,
                                      bytes_accessed=6 * 1024 * 1024),
        interpret=interpret,
    )(*operands)


def local(query_matrix, key_matrix, value_matrix, output_gradient, doc_start):
    token_per_shard = query_matrix.shape[0]
    head_groups = lax.axis_size("head")
    q_cols = query_matrix.shape[1] // head_groups
    k_cols = key_matrix.shape[1] // head_groups
    assert k_cols == HEAD_SIZE and 2 * token_per_shard == BLOCK
    kv_packed = kv_pack(key_matrix, value_matrix, head_groups, interpret=INTERPRET)
    kv = lax.all_to_all(kv_packed, "head", split_axis=0, concat_axis=0, tiled=True)
    ctx_rows = kv.shape[0]
    earlier_kv = from_behind(kv[BLOCK:], "ctx", 1)
    packed = lax.all_to_all(
        query_matrix.reshape(token_per_shard, head_groups, q_cols),
        "head", split_axis=1, concat_axis=0, tiled=True,
    ).reshape(ctx_rows, q_cols)
    units = ctx_rows // BLOCK
    ctx_index = lax.axis_index("ctx")
    wanted = (ctx_index - 1) * units + jnp.arange(2 * units, dtype=jnp.int32)
    unit_at = jnp.arange(doc_start.shape[0], dtype=jnp.int32)
    joined_units = jnp.sum(jnp.where(unit_at[None, :] <= wanted[:, None], doc_start[None, :], 0), axis=1)
    joined_units = jnp.where(wanted >= 0, joined_units, -1)
    own_units = joined_units[units:]
    unit_ids = jnp.arange(units, dtype=jnp.int32)
    window = unit_ids[:, None] + 1 + unit_ids[None, :]
    same = (joined_units[window] == own_units[:, None]).astype(jnp.int32)
    lo = (unit_ids + units + 1 - jnp.sum(same, axis=1)).astype(jnp.int32)
    heads = q_cols // HEAD_SIZE
    first = attention_call(lo, packed, kv, earlier_kv, output_gradient, range(units - 1),
                           heads=heads, interpret=INTERPRET)
    attended_all, query_total, prior_grads, own_first = first
    last = attention_call(lo, packed, kv, None, output_gradient, [units - 1],
                          (attended_all, query_total), own_first, heads=heads, interpret=INTERPRET)
    attended_all, query_total, own_grads = last
    score_scale = HEAD_SIZE ** (-0.5)
    later = from_behind(prior_grads, "ctx", -1).astype(jnp.float32)
    later = jnp.concatenate([jnp.zeros((BLOCK, 2 * k_cols), jnp.float32), later], axis=0)
    summed_keys = (own_grads[:, :k_cols] * score_scale + later[:, :k_cols]).astype(jnp.bfloat16)
    summed_values = (own_grads[:, k_cols:] + later[:, k_cols:]).astype(jnp.bfloat16)
    return (attended_all, query_total, summed_keys, summed_values)


def solution(mesh):
    placed = (
        P(("ctx", "head"), None),
        P(("ctx", "head"), None),
        P(("ctx", "head"), None),
        P("ctx", "head"),
        P(),
    )
    return jax.shard_map(
        local,
        mesh=mesh,
        in_specs=placed,
        out_specs=(P("ctx", "head"), P("ctx", "head"), P("ctx", "head"), P("ctx", "head")),
        check_vma=False,
    )
```
